32 devices in a mesh: groups: 2 (over y), ctx: 4 (over z), head: 2 (over x), sub: 2 (over core).
Axes of the slice: x: 2, y: 2, z: 4, core: 2. Of those that a mesh axis runs over, the one named last changes fastest.
Arguments:
- x_raw: bfloat16 [8192, 8192], P(('groups', 'ctx'), 'head'), parts along dimension 0, may hold values from -6 to 6
- bc_raw: bfloat16 [2, 8, 128, 8192], P(None, 'head', 'sub', ('groups', 'ctx')), parts along dimension 3, may hold values from -6 to 6
- z_gate: bfloat16 [8192, 8192], P(('groups', 'ctx', 'sub'), 'head'), parts along dimension 0, may hold values from -31 to 31
- dt_raw: float32 [128, 8192], P('head', ('groups', 'ctx')), parts along dimension 1, may hold values from -2.3 to 11
- conv_x_w: float32 [4, 8192], P(None, 'head'), may hold values from -3 to 3
- conv_x_b: float32 [8192], P('head'), may hold values from -3 to 3
- conv_bc_w: float32 [4, 2, 8, 128], P(None, None, 'head'), may hold values from -3 to 3
- conv_bc_b: float32 [2, 8, 128], P(None, 'head'), may hold values from -3 to 3
- dt_bias: float32 [128], P('head'), may hold values from -10 to 0
- a_log: float32 [128], P('head'), may hold values from -3 to 0.7
- d_skip: float32 [128], P('head'), may hold values from 0.1 to 1
- norm_w: float32 [8192], P('head'), may hold values from 0.5 to 1.5
Outputs:
- out: bfloat16 [8192, 8192], P(('groups', 'ctx', 'sub'), 'head'), parts along dimension 0
The draws below stay inside these ranges and needn't reach their ends.
There are 2 independent parts, one for each index of `groups`. The reference program is written for one: setup_inputs(seed, part) draws one part's arguments, and reference() takes and returns one part's arrays. A program takes and returns all parts, laid end to end along the dimension named above; an argument that names none is the same for every part. Nothing has to cross between parts.
All inputs are finite; a program needn't handle non-finite values.
Results may differ from the reference program's by a relative error of at most 0.001.
Values may be sent and summed in bfloat16 or wider, within the bound.
No kernel may reach another device: no remote copies, remote signals or barrier semaphores. Data moves between devices by JAX's collectives and lax.ppermute only.
A program may use at most 192 MiB of HBM per device.

```python
import math
import jax
import jax.numpy as jnp
from jax import lax

HEADS = 128
HEAD_DIM = 64
STATE = 128
GROUPS = 8
CONV_K = 4
TOK_DEV = 1024
INNER = 8192
PIECE_WORDS = 4096


def head_params(key):
    fast_share = 0.5
    fast_heads = jax.random.bernoulli(jax.random.fold_in(key, 101), fast_share, (HEADS,))
    slow_total = jnp.exp(jax.random.uniform(jax.random.fold_in(key, 102), (HEADS,), jnp.float32, jnp.log(0.2), jnp.log(1.6)))
    slower_decay_rate = jnp.exp(jax.random.uniform(jax.random.fold_in(key, 103), (HEADS,), jnp.float32, jnp.log(0.05), jnp.log(0.2)))
    fast_step = jax.random.uniform(jax.random.fold_in(key, 104), (HEADS,), jnp.float32, 1.0 / 50.0, 1.0 / 30.0)
    fast_rate = jnp.exp(jax.random.uniform(jax.random.fold_in(key, 105), (HEADS,), jnp.float32, jnp.log(0.5), jnp.log(2.0)))
    decay_rate = jnp.where(fast_heads, fast_rate, slower_decay_rate)
    per_token = jnp.where(fast_heads, fast_step, slow_total / PIECE_WORDS)
    typical = per_token / decay_rate
    return (decay_rate, jnp.log(jnp.expm1(typical)))


def draw_a_log(key, part):
    decay_rate, bias_values = head_params(key)
    return jnp.log(decay_rate)


def draw_dt_bias(key, part):
    decay_rate, bias_values = head_params(key)
    return bias_values


def draw_dt_raw(key, part):
    jitter = 0.5 * jax.random.truncated_normal(jax.random.fold_in(key, 201), -3.0, 3.0, (HEADS, PIECE_WORDS), jnp.float32)
    shifts = jax.random.uniform(jax.random.fold_in(key, 202), (HEADS, PIECE_WORDS // TOK_DEV, 1), jnp.float32, -0.7, 0.7)
    shifts = jnp.broadcast_to(shifts, (HEADS, PIECE_WORDS // TOK_DEV, TOK_DEV)).reshape(HEADS, PIECE_WORDS)
    spike_indices = jax.random.randint(jax.random.fold_in(key, 203), (4,), 0, PIECE_WORDS)
    index_array = jnp.arange(PIECE_WORDS)
    spike_happening = jnp.any(index_array[None, :] == spike_indices[:, None], axis=0)
    boost_multiplier = jnp.where(spike_happening, jnp.log(0.35 * PIECE_WORDS), 0.0)
    return jitter + shifts + boost_multiplier[None, :]


def draw_z_gate(key, part):
    row_scale = jnp.exp(jax.random.uniform(jax.random.fold_in(key, 301), (PIECE_WORDS, 1), jnp.float32, jnp.log(0.3), jnp.log(3.0)))
    col_scale = jnp.exp(jax.random.uniform(jax.random.fold_in(key, 302), (1, INNER), jnp.float32, jnp.log(0.3), jnp.log(3.0)))
    base_values = jax.random.truncated_normal(jax.random.fold_in(key, 303), -3.0, 3.0, (PIECE_WORDS, INNER), jnp.float32)
    return (base_values * row_scale * col_scale).astype(jnp.bfloat16)


def block_levels(stream_key, shape, split, smallest, largest):
    def one(axis_at, parts):
        heights = jax.random.uniform(jax.random.fold_in(jax.random.fold_in(stream_key, 6), axis_at), (parts,), jnp.float32, smallest / len(split), largest / len(split))
        return jnp.repeat(jnp.exp(heights), shape[axis_at] // parts).reshape((-1,) + (1,) * (len(shape) - axis_at - 1))

    gain = one(*split[0])
    for cut in split[1:]:
        gain = gain * one(*cut)
    return gain


def normal_values(rng, extent, deviation, reach, cuts=(), kind=jnp.bfloat16):
    array = jax.random.normal(rng, extent, jnp.float32) * deviation
    if len(cuts) > 0:
        array = block_levels(rng, extent, cuts, -0.22, 0.18) * array
    return jnp.clip(array, min=-reach, max=reach).astype(kind)


def setup_inputs(seed: int = 0, part: int = 0) -> dict:
    key_of = jax.random.split(jax.random.key(seed), 13)
    part_keys = jax.random.split(jax.random.fold_in(key_of[12], part), 13)
    return {
        "x_raw": normal_values(part_keys[0], (PIECE_WORDS, INNER), 1.0, 6.0, ((0, 4), (1, 2))),
        "bc_raw": normal_values(part_keys[1], (2, GROUPS, STATE, PIECE_WORDS), 1.0, 6.0, ((1, 2), (2, 2), (3, 4))),
        "z_gate": draw_z_gate(jax.random.fold_in(jax.random.fold_in(key_of[12], part), 71), part),
        "dt_raw": draw_dt_raw(jax.random.fold_in(jax.random.fold_in(key_of[12], part), 71), part),
        "conv_x_w": normal_values(key_of[4], (CONV_K, INNER), CONV_K ** -0.5, 3.0, ((1, 2),), jnp.float32),
        "conv_x_b": normal_values(key_of[5], (INNER,), 0.5, 3.0, ((0, 2),), jnp.float32),
        "conv_bc_w": normal_values(key_of[6], (CONV_K, 2, GROUPS, STATE), CONV_K ** -0.5, 3.0, ((2, 2),), jnp.float32),
        "conv_bc_b": normal_values(key_of[7], (2, GROUPS, STATE), 0.5, 3.0, ((1, 2),), jnp.float32),
        "dt_bias": draw_dt_bias(jax.random.fold_in(key_of[12], 71), part),
        "a_log": draw_a_log(jax.random.fold_in(key_of[12], 71), part),
        "d_skip": jnp.clip(jnp.exp(math.log(1.0) - 2.3025851 * jax.random.uniform(key_of[10], (HEADS,), jnp.float32) ** block_levels(key_of[10], (HEADS,), ((0, 2),), -0.2, 0.2)), 0.1, 1.0),
        "norm_w": jnp.clip(1.0 + 0.1 * jax.random.normal(key_of[11], (INNER,), jnp.float32), 0.5, 1.5),
    }


HIGHEST = lax.Precision.HIGHEST

def conv_rows(padded, weights, bias_row):
    sequence_length = padded.shape[0] - (CONV_K - 1)
    total = jnp.zeros((sequence_length, padded.shape[1]), jnp.float32) + bias_row[None, :]
    for tap_index in range(CONV_K):
        total = total + weights[tap_index][None, :] * padded[tap_index:tap_index + sequence_length].astype(jnp.float32)
    return jax.nn.silu(total)

def conv_cols(padded, weights, bias_block):
    sequence_length = padded.shape[-1] - (CONV_K - 1)
    total = jnp.zeros(padded.shape[:-1] + (sequence_length,), jnp.float32) + bias_block[..., None]
    for tap_index in range(CONV_K):
        total = total + weights[tap_index][..., None] * padded[..., tap_index:tap_index + sequence_length].astype(jnp.float32)
    return jax.nn.silu(total)

def block_step(carried, pieces):
    x_block, step_block, decay_block, b_block, c_block = pieces
    cumulative = jnp.cumsum(decay_block, axis=-1)
    block_len = decay_block.shape[-1]
    row_ids = lax.broadcasted_iota(jnp.int32, (block_len, block_len), 0)
    col_ids = lax.broadcasted_iota(jnp.int32, (block_len, block_len), 1)
    gaps = cumulative[..., :, None] - cumulative[..., None, :]
    decays = jnp.exp(jnp.where(row_ids >= col_ids, gaps, -jnp.inf))
    scores = jnp.einsum('gnq,gnk->gqk', c_block, b_block, precision=HIGHEST)
    weights = scores[:, None] * decays * step_block[..., None, :]
    outputs = jnp.einsum('grqk,kgrp->qgrp', weights, x_block, precision=HIGHEST)
    inside = jnp.einsum('gnq,grnp->qgrp', c_block, carried, precision=HIGHEST)
    outputs = outputs + inside * jnp.exp(cumulative).transpose(2, 0, 1)[..., None]
    to_end = jnp.exp(cumulative[..., -1:] - cumulative) * step_block
    x_scaled = x_block * to_end.transpose(2, 0, 1)[..., None]
    new_state = carried * jnp.exp(cumulative[..., -1])[..., None, None]
    new_state = new_state + jnp.einsum('gnk,kgrp->grnp', b_block, x_scaled, precision=HIGHEST)
    return (new_state, outputs)

def split_blocks(values, num_blocks, block_len):
    shaped = values.reshape(values.shape[:-1] + (num_blocks, block_len))
    return jnp.moveaxis(shaped, -2, 0)

def local_pass(x_heads, step_sizes, log_decay, b_rows, c_rows, block_limit):
    sequence_length = x_heads.shape[0]
    block_len = min(block_limit, sequence_length)
    num_blocks = sequence_length // block_len
    x_blocks = x_heads.reshape((num_blocks, block_len) + x_heads.shape[1:])
    start = jnp.zeros((x_heads.shape[1], x_heads.shape[2], b_rows.shape[1], x_heads.shape[3]), jnp.float32)
    end_states, outputs = lax.scan(block_step, start, (x_blocks, split_blocks(step_sizes, num_blocks, block_len), split_blocks(log_decay, num_blocks, block_len), split_blocks(b_rows, num_blocks, block_len), split_blocks(c_rows, num_blocks, block_len)))
    return (outputs.reshape(x_heads.shape), end_states)

def reference(x_raw, bc_raw, z_gate, dt_raw, conv_x_w, conv_x_b, conv_bc_w, conv_bc_b, dt_bias, a_log, d_skip, norm_w):
    sequence_length = x_raw.shape[0]
    per_group = HEADS // GROUPS
    x_pad = jnp.concatenate([jnp.zeros((CONV_K - 1, x_raw.shape[1]), x_raw.dtype), x_raw], 0)
    x_conv = conv_rows(x_pad, conv_x_w, conv_x_b)
    bc_pad = jnp.concatenate([jnp.zeros(bc_raw.shape[:-1] + (CONV_K - 1,), bc_raw.dtype), bc_raw], 3)
    bc_conv = conv_cols(bc_pad, conv_bc_w, conv_bc_b)
    step_sizes = jax.nn.softplus(dt_raw + dt_bias[:, None])
    log_decay = -jnp.exp(a_log)[:, None] * step_sizes
    x_groups = x_conv.reshape(sequence_length, GROUPS, per_group, HEAD_DIM).transpose(1, 0, 2, 3)

    def one_group(pieces):
        x_group, step_group, decay_group, b_group, c_group = pieces
        outputs, end_states = local_pass(x_group[:, None], step_group[None], decay_group[None], b_group[None], c_group[None], 128)
        return outputs[:, 0]
    group_out = lax.map(one_group, (x_groups, step_sizes.reshape(GROUPS, per_group, sequence_length), log_decay.reshape(GROUPS, per_group, sequence_length), bc_conv[0], bc_conv[1]))
    y_all = group_out.transpose(1, 0, 2, 3).reshape(sequence_length, INNER)
    y_all = y_all + x_conv * jnp.repeat(d_skip, HEAD_DIM)[None, :]
    gated_output = y_all * jax.nn.silu(z_gate.astype(jnp.float32))
    group_width = per_group * HEAD_DIM
    grouped = gated_output.reshape(sequence_length, GROUPS, group_width)
    mean_square = lax.optimization_barrier(jnp.mean(grouped * grouped, axis=-1, keepdims=True))
    normed = grouped * lax.rsqrt(mean_square + 1e-05) * norm_w.reshape(1, GROUPS, group_width)
    return normed.reshape(sequence_length, INNER).astype(jnp.bfloat16)
```

```python
import jax
import jax.numpy as jnp
from jax import lax
from jax.experimental import pallas as pl
from jax.experimental.pallas import tpu as pltpu
from jax.sharding import PartitionSpec as P

HEADS = 128
HEAD_DIM = 64
GROUPS = 8
CONV_K = 4


HIGHEST = lax.Precision.HIGHEST
F32 = jnp.float32


def passed_along(x, axis, by):
    length = lax.axis_size(axis)
    pairs = [(i, i + by) for i in range(length) if 0 <= i + by < length]
    return lax.ppermute(x, axis, pairs)


def swapped(x, axis):
    return lax.ppermute(x, axis, [(0, 1), (1, 0)])


def conv_rows(padded, weights, bias_row):
    sequence_length = padded.shape[0] - (CONV_K - 1)
    total = jnp.zeros((sequence_length, padded.shape[1]), jnp.float32) + bias_row[None, :]
    for tap_index in range(CONV_K):
        total = total + weights[tap_index][None, :] * padded[
            tap_index : tap_index + sequence_length
        ].astype(jnp.float32)
    return jax.nn.silu(total)


def conv_cols(padded, weights, bias_block):
    sequence_length = padded.shape[-1] - (CONV_K - 1)
    total = jnp.zeros(padded.shape[:-1] + (sequence_length,), jnp.float32) + bias_block[..., None]
    for tap_index in range(CONV_K):
        total = total + weights[tap_index][..., None] * padded[
            ..., tap_index : tap_index + sequence_length
        ].astype(jnp.float32)
    return jax.nn.silu(total)


def dot(a, b):
    return jnp.dot(a, b, precision=HIGHEST, preferred_element_type=F32)


def pair_picker(heads, pair):
    rows = lax.broadcasted_iota(jnp.int32, (heads, 128), 0)
    lanes = lax.broadcasted_iota(jnp.int32, (heads, 128), 1)
    target = jnp.where(lanes < HEAD_DIM, 2 * pair, 2 * pair + 1)
    return (rows == target).astype(F32)


def scan_kernel(xc_ref, ct_ref, b_ref, cumr_ref, cumc_ref, stp_ref, dsk_ref, y_ref, e_ref):
    chunk = pl.program_id(1)
    block_len = xc_ref.shape[0]
    pairs = e_ref.shape[1]
    heads = 2 * pairs

    @pl.when(chunk == 0)
    def _():
        e_ref[...] = jnp.zeros_like(e_ref)

    ct = ct_ref[0]
    bm = b_ref[0]
    scores = dot(ct, bm)
    rows = lax.broadcasted_iota(jnp.int32, (block_len, block_len), 0)
    cols = lax.broadcasted_iota(jnp.int32, (block_len, block_len), 1)
    causal = rows >= cols
    cumr = cumr_ref[0]
    cumc = cumc_ref[0]
    stp = stp_ref[0]
    head_rows = lax.broadcasted_iota(jnp.int32, (heads, block_len), 0)
    left = lax.broadcasted_iota(jnp.int32, (1, 128), 1) < HEAD_DIM
    for pair in range(pairs):
        lanes = slice(pair * 128, (pair + 1) * 128)
        xp = xc_ref[:, lanes]
        s_old = e_ref[0, pair]
        ys = []
        us = []
        for side in range(2):
            head = 2 * pair + side
            dq = dot(cumc, (head_rows == head).astype(F32))
            ck = cumr[head : head + 1, :]
            sk = stp[head : head + 1, :]
            dec = jnp.exp(jnp.where(causal, dq - ck, -jnp.inf))
            ys.append(dot(scores * dec * sk, xp))
            wk = jnp.exp(dq[block_len - 1 : block_len, :] - ck) * sk
            us.append(dot(bm * wk, xp))
        cq = dot(cumc, pair_picker(heads, pair))
        inflow = dot(ct, s_old) * jnp.exp(cq)
        y = jnp.where(left, ys[0], ys[1]) + inflow
        y_ref[:, lanes] = y + xp * dsk_ref[:, lanes]
        e_ref[0, pair] = jnp.exp(cq[block_len - 1 : block_len, :]) * s_old + jnp.where(
            left, us[0], us[1]
        )


def out_kernel(y_ref, ct_ref, cumc_ref, v_ref, z_ref, nw_ref, o_ref, g_ref):
    pairs = v_ref.shape[1]
    heads = 2 * pairs
    ct = ct_ref[0]
    cumc = cumc_ref[0]
    total = jnp.zeros((y_ref.shape[0], 1), F32)
    for pair in range(pairs):
        lanes = slice(pair * 128, (pair + 1) * 128)
        cq = dot(cumc, pair_picker(heads, pair))
        y = y_ref[:, lanes] + dot(ct, v_ref[0, pair]) * jnp.exp(cq)
        z = z_ref[:, lanes].astype(F32)
        gated = y * (z / (1.0 + jnp.exp(-z)))
        g_ref[:, lanes] = gated
        total = total + jnp.sum(gated * gated, axis=-1, keepdims=True)
    mean_square = total / g_ref.shape[1]
    o_ref[...] = (g_ref[...] * lax.rsqrt(mean_square + 1e-05) * nw_ref[...]).astype(o_ref.dtype)


def per_device(
    x_raw,
    bc_raw,
    z_gate,
    dt_raw,
    conv_x_w,
    conv_x_b,
    conv_bc_w,
    conv_bc_b,
    dt_bias,
    a_log,
    d_skip,
    norm_w,
):
    tokens = x_raw.shape[0]
    heads_dev = dt_raw.shape[0]
    per_group = HEADS // GROUPS
    set_groups = heads_dev // per_group
    pairs = per_group // 2
    group_width = per_group * HEAD_DIM
    nsub = lax.axis_size("sub")
    sub_index = lax.axis_index("sub")
    own = tokens // nsub
    half = bc_raw.shape[2]
    state = half * nsub
    channels = heads_dev * HEAD_DIM
    rim_len = CONV_K - 1

    x_rim, bc_rim = passed_along(
        (x_raw[tokens - rim_len :], bc_raw[..., tokens - rim_len :]), "ctx", 1
    )
    x_pad = jnp.concatenate([x_rim, x_raw], 0)
    x_own = conv_rows(
        lax.dynamic_slice_in_dim(x_pad, sub_index * own, own + rim_len, 0), conv_x_w, conv_x_b
    )
    bc_weights = lax.dynamic_slice_in_dim(conv_bc_w, sub_index * half, half, 3)
    bc_bias = lax.dynamic_slice_in_dim(conv_bc_b, sub_index * half, half, 2)
    bc_conv = conv_cols(jnp.concatenate([bc_rim, bc_raw], 3), bc_weights, bc_bias)
    bc_own = lax.all_to_all(bc_conv, "sub", 3, 2, tiled=True)
    b_rows = bc_own[0]
    c_cols = bc_own[1].transpose(0, 2, 1)

    step_sizes = jax.nn.softplus(dt_raw + dt_bias[:, None])
    log_decay = -jnp.exp(a_log)[:, None] * step_sizes
    half_totals = jnp.exp(log_decay.reshape(heads_dev, nsub, own).sum(-1))
    step_own = lax.dynamic_slice_in_dim(step_sizes, sub_index * own, own, 1)
    decay_own = lax.dynamic_slice_in_dim(log_decay, sub_index * own, own, 1)
    block_len = min(256, own)
    blocks = own // block_len
    upper = (
        lax.broadcasted_iota(jnp.int32, (block_len, block_len), 0)
        <= lax.broadcasted_iota(jnp.int32, (block_len, block_len), 1)
    ).astype(F32)
    cum_local = jnp.einsum(
        "hct,tu->hcu", decay_own.reshape(heads_dev, blocks, block_len), upper, precision=HIGHEST
    )
    block_totals = cum_local[..., -1]
    offsets = jnp.cumsum(block_totals, axis=-1) - block_totals
    cum_device = (cum_local + offsets[..., None]).reshape(set_groups, per_group, own)
    cum_rows = cum_local.reshape(set_groups, per_group, own)
    cum_cols = cum_rows.transpose(0, 2, 1)
    step_rows = step_own.reshape(set_groups, per_group, own)
    skip_row = jnp.repeat(d_skip, HEAD_DIM)[None, :]

    y_local, end_state = pl.pallas_call(
        scan_kernel,
        grid=(set_groups, blocks),
        in_specs=[
            pl.BlockSpec((block_len, group_width), lambda g, c: (c, g)),
            pl.BlockSpec((1, block_len, state), lambda g, c: (g, c, 0)),
            pl.BlockSpec((1, state, block_len), lambda g, c: (g, 0, c)),
            pl.BlockSpec((1, per_group, block_len), lambda g, c: (g, 0, c)),
            pl.BlockSpec((1, block_len, per_group), lambda g, c: (g, c, 0)),
            pl.BlockSpec((1, per_group, block_len), lambda g, c: (g, 0, c)),
            pl.BlockSpec((1, group_width), lambda g, c: (0, g)),
        ],
        out_specs=[
            pl.BlockSpec((block_len, group_width), lambda g, c: (c, g)),
            pl.BlockSpec((1, pairs, state, 128), lambda g, c: (g, 0, 0, 0)),
        ],
        out_shape=[
            jax.ShapeDtypeStruct((own, channels), F32),
            jax.ShapeDtypeStruct((set_groups, pairs, state, 128), F32),
        ],
    )(x_own, c_cols, b_rows, cum_rows, cum_cols, step_rows, skip_row)

    def pair_layout(values):
        return jnp.repeat(values.reshape(set_groups, pairs, 2), HEAD_DIM, axis=-1)[:, :, None, :]

    decay_first = pair_layout(half_totals[:, 0])
    decay_second = pair_layout(half_totals[:, 1])
    halves = end_state.reshape(set_groups, pairs, nsub, half, 128)
    mine = lax.dynamic_index_in_dim(halves, sub_index, 2, keepdims=False)
    theirs = swapped(lax.dynamic_index_in_dim(halves, 1 - sub_index, 2, keepdims=False), "sub")
    first_end = jnp.where(sub_index == 0, mine, theirs)
    second_end = jnp.where(sub_index == 0, theirs, mine)
    chip_end = decay_second * first_end + second_end
    chip_decay = decay_first * decay_second
    carried = jnp.zeros_like(chip_end)
    for _ in range(lax.axis_size("ctx") - 1):
        carried = passed_along(chip_end + chip_decay * carried, "ctx", 1)
    into_second = decay_first * carried + first_end
    keep = jnp.where(sub_index == 0, carried, into_second)
    got = swapped(jnp.where(sub_index == 0, into_second, carried), "sub")
    low = jnp.where(sub_index == 0, keep, got)
    high = jnp.where(sub_index == 0, got, keep)
    incoming = jnp.stack([low, high], 2).reshape(set_groups, pairs, state, 128)

    out_len = min(256, own)
    return pl.pallas_call(
        out_kernel,
        grid=(set_groups, own // out_len),
        in_specs=[
            pl.BlockSpec((out_len, group_width), lambda g, c: (c, g)),
            pl.BlockSpec((1, out_len, state), lambda g, c: (g, c, 0)),
            pl.BlockSpec((1, out_len, per_group), lambda g, c: (g, c, 0)),
            pl.BlockSpec((1, pairs, state, 128), lambda g, c: (g, 0, 0, 0)),
            pl.BlockSpec((out_len, group_width), lambda g, c: (c, g)),
            pl.BlockSpec((1, group_width), lambda g, c: (0, g)),
        ],
        out_specs=pl.BlockSpec((out_len, group_width), lambda g, c: (c, g)),
        out_shape=jax.ShapeDtypeStruct((own, channels), jnp.bfloat16),
        scratch_shapes=[pltpu.VMEM((out_len, group_width), F32)],
    )(y_local, c_cols, cum_device.transpose(0, 2, 1), incoming, z_gate, norm_w[None, :])


def solution(mesh):
    in_specs = (
        P(("groups", "ctx"), "head"),
        P(None, "head", "sub", ("groups", "ctx")),
        P(("groups", "ctx", "sub"), "head"),
        P("head", ("groups", "ctx")),
        P(None, "head"),
        P("head"),
        P(None, None, "head", None),
        P(None, "head", None),
        P("head"),
        P("head"),
        P("head"),
        P("head"),
    )
    out_specs = P(("groups", "ctx", "sub"), "head")
    return jax.shard_map(
        per_device, mesh=mesh, in_specs=in_specs, out_specs=out_specs, check_vma=False
    )
```

```python
import jax
import jax.numpy as jnp
from jax import lax
from jax.experimental import pallas as pl
from jax.experimental.pallas import tpu as pltpu
from jax.sharding import PartitionSpec as P

HEADS = 128
HEAD_DIM = 64
GROUPS = 8
CONV_K = 4


HIGHEST = lax.Precision.HIGHEST
F32 = jnp.float32


def passed_along(x, axis, by):
    length = lax.axis_size(axis)
    pairs = [(i, i + by) for i in range(length) if 0 <= i + by < length]
    return lax.ppermute(x, axis, pairs)


def swapped(x, axis):
    return lax.ppermute(x, axis, [(0, 1), (1, 0)])


def conv_rows(padded, weights, bias_row):
    sequence_length = padded.shape[0] - (CONV_K - 1)
    total = jnp.zeros((sequence_length, padded.shape[1]), jnp.float32) + bias_row[None, :]
    for tap_index in range(CONV_K):
        total = total + weights[tap_index][None, :] * padded[
            tap_index : tap_index + sequence_length
        ].astype(jnp.float32)
    return jax.nn.silu(total)


def conv_cols(padded, weights, bias_block):
    sequence_length = padded.shape[-1] - (CONV_K - 1)
    total = jnp.zeros(padded.shape[:-1] + (sequence_length,), jnp.float32) + bias_block[..., None]
    for tap_index in range(CONV_K):
        total = total + weights[tap_index][..., None] * padded[
            ..., tap_index : tap_index + sequence_length
        ].astype(jnp.float32)
    return jax.nn.silu(total)


def dot(a, b):
    return jnp.dot(a, b, precision=HIGHEST, preferred_element_type=F32)


def split(a):
    high = a.astype(jnp.bfloat16)
    return high, (a - high.astype(F32)).astype(jnp.bfloat16)


def dot3(a_parts, b_parts):
    a_high, a_low = a_parts
    b_high, b_low = b_parts
    flat = lambda u, v: jnp.dot(u, v, preferred_element_type=F32)
    return flat(a_high, b_high) + (flat(a_high, b_low) + flat(a_low, b_high))


def pair_columns(cumc, pair, rows):
    left = lax.broadcasted_iota(jnp.int32, (1, 128), 1) < HEAD_DIM
    return jnp.where(
        left,
        jnp.broadcast_to(cumc[:, 2 * pair : 2 * pair + 1], (rows, 128)),
        jnp.broadcast_to(cumc[:, 2 * pair + 1 : 2 * pair + 2], (rows, 128)),
    )


def scan_kernel(xc_ref, ct_ref, b_ref, cumr_ref, cumc_ref, stp_ref, dsk_ref, y_ref, e_ref):
    chunk = pl.program_id(1)
    block_len = xc_ref.shape[0]
    pairs = e_ref.shape[1]
    heads = 2 * pairs

    @pl.when(chunk == 0)
    def _():
        e_ref[...] = jnp.zeros_like(e_ref)

    ct = split(ct_ref[0])
    bm = b_ref[0]
    scores = dot3(ct, split(bm))
    rows = lax.broadcasted_iota(jnp.int32, (block_len, block_len), 0)
    cols = lax.broadcasted_iota(jnp.int32, (block_len, block_len), 1)
    causal = rows >= cols
    cumr = cumr_ref[0]
    cumc = cumc_ref[0]
    stp = stp_ref[0]
    left = lax.broadcasted_iota(jnp.int32, (1, 128), 1) < HEAD_DIM
    for pair in range(pairs):
        lanes = slice(pair * 128, (pair + 1) * 128)
        xp = xc_ref[:, lanes]
        xs = split(xp)
        s_old = e_ref[0, pair]
        ys = []
        us = []
        for side in range(2):
            head = 2 * pair + side
            dq = jnp.broadcast_to(cumc[:, head : head + 1], (block_len, block_len))
            ck = cumr[head : head + 1, :]
            sk = stp[head : head + 1, :]
            dec = jnp.exp(jnp.where(causal, dq - ck, -jnp.inf))
            ys.append(dot3(split(scores * dec * sk), xs))
            wk = jnp.exp(dq[block_len - 1 : block_len, :] - ck) * sk
            us.append(dot3(split(bm * wk), xs))
        cq = pair_columns(cumc, pair, block_len)
        inflow = dot3(ct, split(s_old)) * jnp.exp(cq)
        y = jnp.where(left, ys[0], ys[1]) + inflow
        y_ref[:, lanes] = y + xp * dsk_ref[:, lanes]
        e_ref[0, pair] = jnp.exp(cq[block_len - 1 : block_len, :]) * s_old + jnp.where(
            left, us[0], us[1]
        )


def out_kernel(y_ref, ct_ref, cumc_ref, v_ref, z_ref, nw_ref, o_ref, g_ref):
    pairs = v_ref.shape[1]
    heads = 2 * pairs
    ct = split(ct_ref[0])
    cumc = cumc_ref[0]
    total = jnp.zeros((y_ref.shape[0], 1), F32)
    for pair in range(pairs):
        lanes = slice(pair * 128, (pair + 1) * 128)
        cq = pair_columns(cumc, pair, y_ref.shape[0])
        y = y_ref[:, lanes] + dot3(ct, split(v_ref[0, pair])) * jnp.exp(cq)
        z = z_ref[:, lanes].astype(F32)
        gated = y * (z / (1.0 + jnp.exp(-z)))
        g_ref[:, lanes] = gated
        total = total + jnp.sum(gated * gated, axis=-1, keepdims=True)
    mean_square = total / g_ref.shape[1]
    o_ref[...] = (g_ref[...] * lax.rsqrt(mean_square + 1e-05) * nw_ref[...]).astype(o_ref.dtype)


def per_device(
    x_raw,
    bc_raw,
    z_gate,
    dt_raw,
    conv_x_w,
    conv_x_b,
    conv_bc_w,
    conv_bc_b,
    dt_bias,
    a_log,
    d_skip,
    norm_w,
):
    tokens = x_raw.shape[0]
    heads_dev = dt_raw.shape[0]
    per_group = HEADS // GROUPS
    set_groups = heads_dev // per_group
    pairs = per_group // 2
    group_width = per_group * HEAD_DIM
    nsub = lax.axis_size("sub")
    sub_index = lax.axis_index("sub")
    own = tokens // nsub
    half = bc_raw.shape[2]
    state = half * nsub
    channels = heads_dev * HEAD_DIM
    rim_len = CONV_K - 1

    x_rim, bc_rim = passed_along(
        (x_raw[tokens - rim_len :], bc_raw[..., tokens - rim_len :]), "ctx", 1
    )
    x_pad = jnp.concatenate([x_rim, x_raw], 0)
    x_own = conv_rows(
        lax.dynamic_slice_in_dim(x_pad, sub_index * own, own + rim_len, 0), conv_x_w, conv_x_b
    )
    bc_weights = lax.dynamic_slice_in_dim(conv_bc_w, sub_index * half, half, 3)
    bc_bias = lax.dynamic_slice_in_dim(conv_bc_b, sub_index * half, half, 2)
    bc_conv = conv_cols(jnp.concatenate([bc_rim, bc_raw], 3), bc_weights, bc_bias)
    bc_own = lax.all_to_all(bc_conv, "sub", 3, 2, tiled=True)
    b_rows = bc_own[0]
    c_cols = bc_own[1].transpose(0, 2, 1)

    step_sizes = jax.nn.softplus(dt_raw + dt_bias[:, None])
    log_decay = -jnp.exp(a_log)[:, None] * step_sizes
    half_totals = jnp.exp(log_decay.reshape(heads_dev, nsub, own).sum(-1))
    step_own = lax.dynamic_slice_in_dim(step_sizes, sub_index * own, own, 1)
    decay_own = lax.dynamic_slice_in_dim(log_decay, sub_index * own, own, 1)
    block_len = min(256, own)
    blocks = own // block_len
    upper = (
        lax.broadcasted_iota(jnp.int32, (block_len, block_len), 0)
        <= lax.broadcasted_iota(jnp.int32, (block_len, block_len), 1)
    ).astype(F32)
    cum_local = jnp.einsum(
        "hct,tu->hcu", decay_own.reshape(heads_dev, blocks, block_len), upper, precision=HIGHEST
    )
    block_totals = cum_local[..., -1]
    offsets = jnp.cumsum(block_totals, axis=-1) - block_totals
    cum_device = (cum_local + offsets[..., None]).reshape(set_groups, per_group, own)
    cum_rows = cum_local.reshape(set_groups, per_group, own)
    cum_cols = cum_rows.transpose(0, 2, 1)
    step_rows = step_own.reshape(set_groups, per_group, own)
    skip_row = jnp.repeat(d_skip, HEAD_DIM)[None, :]

    y_local, end_state = pl.pallas_call(
        scan_kernel,
        grid=(set_groups, blocks),
        in_specs=[
            pl.BlockSpec((block_len, group_width), lambda g, c: (c, g)),
            pl.BlockSpec((1, block_len, state), lambda g, c: (g, c, 0)),
            pl.BlockSpec((1, state, block_len), lambda g, c: (g, 0, c)),
            pl.BlockSpec((1, per_group, block_len), lambda g, c: (g, 0, c)),
            pl.BlockSpec((1, block_len, per_group), lambda g, c: (g, c, 0)),
            pl.BlockSpec((1, per_group, block_len), lambda g, c: (g, 0, c)),
            pl.BlockSpec((1, group_width), lambda g, c: (0, g)),
        ],
        out_specs=[
            pl.BlockSpec((block_len, group_width), lambda g, c: (c, g)),
            pl.BlockSpec((1, pairs, state, 128), lambda g, c: (g, 0, 0, 0)),
        ],
        out_shape=[
            jax.ShapeDtypeStruct((own, channels), F32),
            jax.ShapeDtypeStruct((set_groups, pairs, state, 128), F32),
        ],
    )(x_own, c_cols, b_rows, cum_rows, cum_cols, step_rows, skip_row)

    def pair_layout(values):
        return jnp.repeat(values.reshape(set_groups, pairs, 2), HEAD_DIM, axis=-1)[:, :, None, :]

    decay_first = pair_layout(half_totals[:, 0])
    decay_second = pair_layout(half_totals[:, 1])
    halves = end_state.reshape(set_groups, pairs, nsub, half, 128)
    mine = lax.dynamic_index_in_dim(halves, sub_index, 2, keepdims=False)
    theirs = swapped(lax.dynamic_index_in_dim(halves, 1 - sub_index, 2, keepdims=False), "sub")
    first_end = jnp.where(sub_index == 0, mine, theirs)
    second_end = jnp.where(sub_index == 0, theirs, mine)
    chip_end = decay_second * first_end + second_end
    chip_decay = decay_first * decay_second
    carried = jnp.zeros_like(chip_end)
    for _ in range(lax.axis_size("ctx") - 1):
        carried = passed_along(chip_end + chip_decay * carried, "ctx", 1)
    into_second = decay_first * carried + first_end
    keep = jnp.where(sub_index == 0, carried, into_second)
    got = swapped(jnp.where(sub_index == 0, into_second, carried), "sub")
    low = jnp.where(sub_index == 0, keep, got)
    high = jnp.where(sub_index == 0, got, keep)
    incoming = jnp.stack([low, high], 2).reshape(set_groups, pairs, state, 128)

    out_len = min(256, own)
    return pl.pallas_call(
        out_kernel,
        grid=(set_groups, own // out_len),
        in_specs=[
            pl.BlockSpec((out_len, group_width), lambda g, c: (c, g)),
            pl.BlockSpec((1, out_len, state), lambda g, c: (g, c, 0)),
            pl.BlockSpec((1, out_len, per_group), lambda g, c: (g, c, 0)),
            pl.BlockSpec((1, pairs, state, 128), lambda g, c: (g, 0, 0, 0)),
            pl.BlockSpec((out_len, group_width), lambda g, c: (c, g)),
            pl.BlockSpec((1, group_width), lambda g, c: (0, g)),
        ],
        out_specs=pl.BlockSpec((out_len, group_width), lambda g, c: (c, g)),
        out_shape=jax.ShapeDtypeStruct((own, channels), jnp.bfloat16),
        scratch_shapes=[pltpu.VMEM((out_len, group_width), F32)],
    )(y_local, c_cols, cum_device.transpose(0, 2, 1), incoming, z_gate, norm_w[None, :])


def solution(mesh):
    in_specs = (
        P(("groups", "ctx"), "head"),
        P(None, "head", "sub", ("groups", "ctx")),
        P(("groups", "ctx", "sub"), "head"),
        P("head", ("groups", "ctx")),
        P(None, "head"),
        P("head"),
        P(None, None, "head", None),
        P(None, "head", None),
        P("head"),
        P("head"),
        P("head"),
        P("head"),
    )
    out_specs = P(("groups", "ctx", "sub"), "head")
    return jax.shard_map(
        per_device, mesh=mesh, in_specs=in_specs, out_specs=out_specs, check_vma=False
    )
```

```python
import jax
import jax.numpy as jnp
from jax import lax
from jax.experimental import pallas as pl
from jax.experimental.pallas import tpu as pltpu
from jax.sharding import PartitionSpec as P

HEADS = 128
HEAD_DIM = 64
GROUPS = 8
CONV_K = 4


HIGHEST = lax.Precision.HIGHEST
F32 = jnp.float32


def passed_along(x, axis, by):
    length = lax.axis_size(axis)
    pairs = [(i, i + by) for i in range(length) if 0 <= i + by < length]
    return lax.ppermute(x, axis, pairs)


def swapped(x, axis):
    return lax.ppermute(x, axis, [(0, 1), (1, 0)])


def conv_rows(padded, weights, bias_row):
    sequence_length = padded.shape[0] - (CONV_K - 1)
    total = jnp.zeros((sequence_length, padded.shape[1]), jnp.float32) + bias_row[None, :]
    for tap_index in range(CONV_K):
        total = total + weights[tap_index][None, :] * padded[
            tap_index : tap_index + sequence_length
        ].astype(jnp.float32)
    return jax.nn.silu(total)


def conv_cols(padded, weights, bias_block):
    sequence_length = padded.shape[-1] - (CONV_K - 1)
    total = jnp.zeros(padded.shape[:-1] + (sequence_length,), jnp.float32) + bias_block[..., None]
    for tap_index in range(CONV_K):
        total = total + weights[tap_index][..., None] * padded[
            ..., tap_index : tap_index + sequence_length
        ].astype(jnp.float32)
    return jax.nn.silu(total)


def dot(a, b):
    return jnp.dot(a, b, precision=HIGHEST, preferred_element_type=F32)


def split(a):
    high = a.astype(jnp.bfloat16)
    return high, (a - high.astype(F32)).astype(jnp.bfloat16)


def dot3(a_parts, b_parts):
    a_high, a_low = a_parts
    b_high, b_low = b_parts
    flat = lambda u, v: jnp.dot(u, v, preferred_element_type=F32)
    return flat(a_high, b_high) + (flat(a_high, b_low) + flat(a_low, b_high))


def pair_columns(cumc, pair, rows):
    left = lax.broadcasted_iota(jnp.int32, (1, 128), 1) < HEAD_DIM
    return jnp.where(
        left,
        jnp.broadcast_to(cumc[:, 2 * pair : 2 * pair + 1], (rows, 128)),
        jnp.broadcast_to(cumc[:, 2 * pair + 1 : 2 * pair + 2], (rows, 128)),
    )


def scan_kernel(xc_ref, ct_ref, b_ref, cumr_ref, cumc_ref, stp_ref, dsk_ref, y_ref, e_ref):
    chunk = pl.program_id(1)
    block_len = xc_ref.shape[0]
    pairs = e_ref.shape[0]
    heads = 2 * pairs

    @pl.when(chunk == 0)
    def _():
        e_ref[...] = jnp.zeros_like(e_ref)

    ct = split(ct_ref[0])
    bm = b_ref[0]
    scores = dot3(ct, split(bm))
    rows = lax.broadcasted_iota(jnp.int32, (block_len, block_len), 0)
    cols = lax.broadcasted_iota(jnp.int32, (block_len, block_len), 1)
    causal = rows >= cols
    cumr = cumr_ref[0]
    cumc = cumc_ref[0]
    stp = stp_ref[0]
    left = lax.broadcasted_iota(jnp.int32, (1, 128), 1) < HEAD_DIM
    for pair in range(pairs):
        lanes = slice(pair * 128, (pair + 1) * 128)
        xp = xc_ref[:, lanes]
        xs = split(xp)
        s_old = e_ref[pair]
        ys = []
        us = []
        for side in range(2):
            head = 2 * pair + side
            dq = jnp.broadcast_to(cumc[:, head : head + 1], (block_len, block_len))
            ck = cumr[head : head + 1, :]
            sk = stp[head : head + 1, :]
            dec = jnp.exp(jnp.where(causal, dq - ck, -jnp.inf))
            ys.append(dot3(split(scores * dec * sk), xs))
            wk = jnp.exp(dq[block_len - 1 : block_len, :] - ck) * sk
            us.append(dot3(split(bm * wk), xs))
        cq = pair_columns(cumc, pair, block_len)
        inflow = dot3(ct, split(s_old)) * jnp.exp(cq)
        y = jnp.where(left, ys[0], ys[1]) + inflow
        y_ref[:, lanes] = y + xp * dsk_ref[:, lanes]
        e_ref[pair] = jnp.exp(cq[block_len - 1 : block_len, :]) * s_old + jnp.where(
            left, us[0], us[1]
        )


def end_kernel(xc_ref, b_ref, wk_ref, e_ref):
    pairs = e_ref.shape[1]
    bm = b_ref[0]
    wk = wk_ref[0]
    left = lax.broadcasted_iota(jnp.int32, (1, 128), 1) < HEAD_DIM
    for pair in range(pairs):
        xs = split(xc_ref[:, pair * 128 : (pair + 1) * 128])
        us = [
            dot3(split(bm * wk[2 * pair + side : 2 * pair + side + 1, :]), xs) for side in range(2)
        ]
        e_ref[0, pair] = jnp.where(left, us[0], us[1])


def out_kernel(y_ref, ct_ref, cumc_ref, v_ref, z_ref, nw_ref, o_ref, g_ref):
    pairs = v_ref.shape[1]
    heads = 2 * pairs
    ct = split(ct_ref[0])
    cumc = cumc_ref[0]
    total = jnp.zeros((y_ref.shape[0], 1), F32)
    for pair in range(pairs):
        lanes = slice(pair * 128, (pair + 1) * 128)
        cq = pair_columns(cumc, pair, y_ref.shape[0])
        y = y_ref[:, lanes] + dot3(ct, split(v_ref[0, pair])) * jnp.exp(cq)
        z = z_ref[:, lanes].astype(F32)
        gated = y * (z / (1.0 + jnp.exp(-z)))
        g_ref[:, lanes] = gated
        total = total + jnp.sum(gated * gated, axis=-1, keepdims=True)
    mean_square = total / g_ref.shape[1]
    o_ref[...] = (g_ref[...] * lax.rsqrt(mean_square + 1e-05) * nw_ref[...]).astype(o_ref.dtype)


def per_device(
    x_raw,
    bc_raw,
    z_gate,
    dt_raw,
    conv_x_w,
    conv_x_b,
    conv_bc_w,
    conv_bc_b,
    dt_bias,
    a_log,
    d_skip,
    norm_w,
):
    tokens = x_raw.shape[0]
    heads_dev = dt_raw.shape[0]
    per_group = HEADS // GROUPS
    set_groups = heads_dev // per_group
    pairs = per_group // 2
    group_width = per_group * HEAD_DIM
    nsub = lax.axis_size("sub")
    sub_index = lax.axis_index("sub")
    own = tokens // nsub
    half = bc_raw.shape[2]
    state = half * nsub
    channels = heads_dev * HEAD_DIM
    rim_len = CONV_K - 1

    x_rim, bc_rim = passed_along(
        (x_raw[tokens - rim_len :], bc_raw[..., tokens - rim_len :]), "ctx", 1
    )
    x_pad = jnp.concatenate([x_rim, x_raw], 0)
    x_own = conv_rows(
        lax.dynamic_slice_in_dim(x_pad, sub_index * own, own + rim_len, 0), conv_x_w, conv_x_b
    )
    bc_weights = lax.dynamic_slice_in_dim(conv_bc_w, sub_index * half, half, 3)
    bc_bias = lax.dynamic_slice_in_dim(conv_bc_b, sub_index * half, half, 2)
    bc_conv = conv_cols(jnp.concatenate([bc_rim, bc_raw], 3), bc_weights, bc_bias)
    bc_halves = bc_conv.reshape(2, set_groups, half, nsub, own)
    bc_mine = lax.dynamic_index_in_dim(bc_halves, sub_index, 3, keepdims=False)
    bc_theirs = swapped(
        lax.dynamic_index_in_dim(bc_halves, 1 - sub_index, 3, keepdims=False), "sub"
    )
    bc_own = jnp.stack(
        [
            jnp.where(sub_index == 0, bc_mine, bc_theirs),
            jnp.where(sub_index == 0, bc_theirs, bc_mine),
        ],
        2,
    ).reshape(2, set_groups, state, own)
    b_rows = bc_own[0]
    c_cols = bc_own[1].transpose(0, 2, 1)

    step_sizes = jax.nn.softplus(dt_raw + dt_bias[:, None])
    log_decay = -jnp.exp(a_log)[:, None] * step_sizes
    half_totals = jnp.exp(log_decay.reshape(heads_dev, nsub, own).sum(-1))
    step_own = lax.dynamic_slice_in_dim(step_sizes, sub_index * own, own, 1)
    decay_own = lax.dynamic_slice_in_dim(log_decay, sub_index * own, own, 1)
    block_len = min(256, own)
    blocks = own // block_len
    upper = (
        lax.broadcasted_iota(jnp.int32, (block_len, block_len), 0)
        <= lax.broadcasted_iota(jnp.int32, (block_len, block_len), 1)
    ).astype(F32)
    cum_local = jnp.einsum(
        "hct,tu->hcu", decay_own.reshape(heads_dev, blocks, block_len), upper, precision=HIGHEST
    )
    block_totals = cum_local[..., -1]
    offsets = jnp.cumsum(block_totals, axis=-1) - block_totals
    cum_device = (cum_local + offsets[..., None]).reshape(set_groups, per_group, own)
    cum_rows = cum_local.reshape(set_groups, per_group, own)
    cum_cols = cum_rows.transpose(0, 2, 1)
    step_rows = step_own.reshape(set_groups, per_group, own)
    skip_row = jnp.repeat(d_skip, HEAD_DIM)[None, :]

    to_end = jnp.exp(cum_device[..., own - 1 :] - cum_device) * step_rows
    end_state = pl.pallas_call(
        end_kernel,
        grid=(set_groups,),
        in_specs=[
            pl.BlockSpec((own, group_width), lambda g: (0, g)),
            pl.BlockSpec((1, state, own), lambda g: (g, 0, 0)),
            pl.BlockSpec((1, per_group, own), lambda g: (g, 0, 0)),
        ],
        out_specs=pl.BlockSpec((1, pairs, state, 128), lambda g: (g, 0, 0, 0)),
        out_shape=jax.ShapeDtypeStruct((set_groups, pairs, state, 128), F32),
    )(x_own, b_rows, to_end)

    def pair_layout(values):
        return jnp.repeat(values.reshape(set_groups, pairs, 2), HEAD_DIM, axis=-1)[:, :, None, :]

    decay_first = pair_layout(half_totals[:, 0])
    decay_second = pair_layout(half_totals[:, 1])
    halves = end_state.reshape(set_groups, pairs, nsub, half, 128)
    mine = lax.dynamic_index_in_dim(halves, sub_index, 2, keepdims=False)
    theirs = swapped(lax.dynamic_index_in_dim(halves, 1 - sub_index, 2, keepdims=False), "sub")
    first_end = jnp.where(sub_index == 0, mine, theirs)
    second_end = jnp.where(sub_index == 0, theirs, mine)
    chip_end = decay_second * first_end + second_end
    chip_decay = decay_first * decay_second
    ctx_index = lax.axis_index("ctx")
    packed = jnp.concatenate([chip_end, chip_decay], 2)
    packed, x_held = lax.optimization_barrier((packed, x_own))
    y_local = pl.pallas_call(
        scan_kernel,
        grid=(set_groups, blocks),
        in_specs=[
            pl.BlockSpec((block_len, group_width), lambda g, c: (c, g)),
            pl.BlockSpec((1, block_len, state), lambda g, c: (g, c, 0)),
            pl.BlockSpec((1, state, block_len), lambda g, c: (g, 0, c)),
            pl.BlockSpec((1, per_group, block_len), lambda g, c: (g, 0, c)),
            pl.BlockSpec((1, block_len, per_group), lambda g, c: (g, c, 0)),
            pl.BlockSpec((1, per_group, block_len), lambda g, c: (g, 0, c)),
            pl.BlockSpec((1, group_width), lambda g, c: (0, g)),
        ],
        out_specs=pl.BlockSpec((block_len, group_width), lambda g, c: (c, g)),
        out_shape=jax.ShapeDtypeStruct((own, channels), F32),
        scratch_shapes=[pltpu.VMEM((pairs, state, 128), F32)],
    )(x_held, c_cols, b_rows, cum_rows, cum_cols, step_rows, skip_row)

    gathered = lax.all_gather(packed, "ctx")
    gathered, y_local = lax.optimization_barrier((gathered, y_local))
    all_ends = gathered[:, :, :, :half]
    all_decays = gathered[:, :, :, half:]
    carried = jnp.zeros_like(chip_end)
    for earlier in range(lax.axis_size("ctx") - 1):
        carried = jnp.where(
            earlier < ctx_index, all_ends[earlier] + all_decays[earlier] * carried, carried
        )
    into_second = decay_first * carried + first_end
    keep = jnp.where(sub_index == 0, carried, into_second)
    got = swapped(jnp.where(sub_index == 0, into_second, carried), "sub")
    low = jnp.where(sub_index == 0, keep, got)
    high = jnp.where(sub_index == 0, got, keep)
    incoming = jnp.stack([low, high], 2).reshape(set_groups, pairs, state, 128)

    out_len = min(256, own)
    return pl.pallas_call(
        out_kernel,
        grid=(set_groups, own // out_len),
        in_specs=[
            pl.BlockSpec((out_len, group_width), lambda g, c: (c, g)),
            pl.BlockSpec((1, out_len, state), lambda g, c: (g, c, 0)),
            pl.BlockSpec((1, out_len, per_group), lambda g, c: (g, c, 0)),
            pl.BlockSpec((1, pairs, state, 128), lambda g, c: (g, 0, 0, 0)),
            pl.BlockSpec((out_len, group_width), lambda g, c: (c, g)),
            pl.BlockSpec((1, group_width), lambda g, c: (0, g)),
        ],
        out_specs=pl.BlockSpec((out_len, group_width), lambda g, c: (c, g)),
        out_shape=jax.ShapeDtypeStruct((own, channels), jnp.bfloat16),
        scratch_shapes=[pltpu.VMEM((out_len, group_width), F32)],
    )(y_local, c_cols, cum_device.transpose(0, 2, 1), incoming, z_gate, norm_w[None, :])


def solution(mesh):
    in_specs = (
        P(("groups", "ctx"), "head"),
        P(None, "head", "sub", ("groups", "ctx")),
        P(("groups", "ctx", "sub"), "head"),
        P("head", ("groups", "ctx")),
        P(None, "head"),
        P("head"),
        P(None, None, "head", None),
        P(None, "head", None),
        P("head"),
        P("head"),
        P("head"),
        P("head"),
    )
    out_specs = P(("groups", "ctx", "sub"), "head")
    return jax.shard_map(
        per_device, mesh=mesh, in_specs=in_specs, out_specs=out_specs, check_vma=False
    )
```

```python
import jax
import jax.numpy as jnp
from jax import lax
from jax.experimental import pallas as pl
from jax.experimental.pallas import tpu as pltpu
from jax.sharding import PartitionSpec as P

HEADS = 128
HEAD_DIM = 64
GROUPS = 8
CONV_K = 4


HIGHEST = lax.Precision.HIGHEST
F32 = jnp.float32


def passed_along(x, axis, by):
    length = lax.axis_size(axis)
    pairs = [(i, i + by) for i in range(length) if 0 <= i + by < length]
    return lax.ppermute(x, axis, pairs)


def swapped(x, axis):
    return lax.ppermute(x, axis, [(0, 1), (1, 0)])


def conv_rows(padded, weights, bias_row):
    sequence_length = padded.shape[0] - (CONV_K - 1)
    total = jnp.zeros((sequence_length, padded.shape[1]), jnp.float32) + bias_row[None, :]
    for tap_index in range(CONV_K):
        total = total + weights[tap_index][None, :] * padded[
            tap_index : tap_index + sequence_length
        ].astype(jnp.float32)
    return jax.nn.silu(total)


def conv_cols(padded, weights, bias_block):
    sequence_length = padded.shape[-1] - (CONV_K - 1)
    total = jnp.zeros(padded.shape[:-1] + (sequence_length,), jnp.float32) + bias_block[..., None]
    for tap_index in range(CONV_K):
        total = total + weights[tap_index][..., None] * padded[
            ..., tap_index : tap_index + sequence_length
        ].astype(jnp.float32)
    return jax.nn.silu(total)


def dot(a, b):
    return jnp.dot(a, b, precision=HIGHEST, preferred_element_type=F32)


def split(a):
    high = a.astype(jnp.bfloat16)
    return high, (a - high.astype(F32)).astype(jnp.bfloat16)


def dot3(a_parts, b_parts):
    a_high, a_low = a_parts
    b_high, b_low = b_parts
    flat = lambda u, v: jnp.dot(u, v, preferred_element_type=F32)
    return flat(a_high, b_high) + (flat(a_high, b_low) + flat(a_low, b_high))


def pair_columns(cumc, pair, rows):
    left = lax.broadcasted_iota(jnp.int32, (1, 128), 1) < HEAD_DIM
    return jnp.where(
        left,
        jnp.broadcast_to(cumc[:, 2 * pair : 2 * pair + 1], (rows, 128)),
        jnp.broadcast_to(cumc[:, 2 * pair + 1 : 2 * pair + 2], (rows, 128)),
    )


def scan_kernel(xc_ref, ct_ref, b_ref, cumr_ref, cumc_ref, stp_ref, dsk_ref, y_ref, e_ref):
    chunk = pl.program_id(1)
    block_len = xc_ref.shape[0]
    pairs = e_ref.shape[0]
    heads = 2 * pairs

    @pl.when(chunk == 0)
    def _():
        e_ref[...] = jnp.zeros_like(e_ref)

    ct = split(ct_ref[0])
    bm = b_ref[0]
    scores = dot3(ct, split(bm))
    rows = lax.broadcasted_iota(jnp.int32, (block_len, block_len), 0)
    cols = lax.broadcasted_iota(jnp.int32, (block_len, block_len), 1)
    causal = rows >= cols
    cumr = cumr_ref[0]
    cumc = cumc_ref[0]
    stp = stp_ref[0]
    left = lax.broadcasted_iota(jnp.int32, (1, 128), 1) < HEAD_DIM
    for pair in range(pairs):
        lanes = slice(pair * 128, (pair + 1) * 128)
        xp = xc_ref[:, lanes]
        xs = split(xp)
        s_old = e_ref[pair]
        ys = []
        us = []
        for side in range(2):
            head = 2 * pair + side
            dq = jnp.broadcast_to(cumc[:, head : head + 1], (block_len, block_len))
            ck = cumr[head : head + 1, :]
            sk = stp[head : head + 1, :]
            dec = jnp.exp(jnp.where(causal, dq - ck, -jnp.inf))
            ys.append(dot3(split(scores * dec * sk), xs))
            wk = jnp.exp(dq[block_len - 1 : block_len, :] - ck) * sk
            us.append(dot3(split(bm * wk), xs))
        cq = pair_columns(cumc, pair, block_len)
        inflow = dot3(ct, split(s_old)) * jnp.exp(cq)
        y = jnp.where(left, ys[0], ys[1]) + inflow
        y_ref[:, lanes] = y + xp * dsk_ref[:, lanes]
        e_ref[pair] = jnp.exp(cq[block_len - 1 : block_len, :]) * s_old + jnp.where(
            left, us[0], us[1]
        )


def end_kernel(xc_ref, b_ref, wk_ref, e_ref):
    pairs = e_ref.shape[1]
    bm = b_ref[0]
    wk = wk_ref[0]
    left = lax.broadcasted_iota(jnp.int32, (1, 128), 1) < HEAD_DIM
    for pair in range(pairs):
        xs = split(xc_ref[:, pair * 128 : (pair + 1) * 128])
        us = [
            dot3(split(bm * wk[2 * pair + side : 2 * pair + side + 1, :]), xs) for side in range(2)
        ]
        e_ref[0, pair] = jnp.where(left, us[0], us[1])


def out_kernel(y_ref, ct_ref, cumc_ref, v_ref, z_ref, nw_ref, o_ref, g_ref):
    pairs = v_ref.shape[1]
    heads = 2 * pairs
    ct = split(ct_ref[0])
    cumc = cumc_ref[0]
    total = jnp.zeros((y_ref.shape[0], 1), F32)
    for pair in range(pairs):
        lanes = slice(pair * 128, (pair + 1) * 128)
        cq = pair_columns(cumc, pair, y_ref.shape[0])
        y = y_ref[:, lanes] + dot3(ct, split(v_ref[0, pair])) * jnp.exp(cq)
        z = z_ref[:, lanes].astype(F32)
        gated = y * (z / (1.0 + jnp.exp(-z)))
        g_ref[:, lanes] = gated
        total = total + jnp.sum(gated * gated, axis=-1, keepdims=True)
    mean_square = total / g_ref.shape[1]
    o_ref[...] = (g_ref[...] * lax.rsqrt(mean_square + 1e-05) * nw_ref[...]).astype(o_ref.dtype)


def per_device(
    x_raw,
    bc_raw,
    z_gate,
    dt_raw,
    conv_x_w,
    conv_x_b,
    conv_bc_w,
    conv_bc_b,
    dt_bias,
    a_log,
    d_skip,
    norm_w,
):
    tokens = x_raw.shape[0]
    heads_dev = dt_raw.shape[0]
    per_group = HEADS // GROUPS
    set_groups = heads_dev // per_group
    pairs = per_group // 2
    group_width = per_group * HEAD_DIM
    nsub = lax.axis_size("sub")
    sub_index = lax.axis_index("sub")
    own = tokens // nsub
    half = bc_raw.shape[2]
    state = half * nsub
    channels = heads_dev * HEAD_DIM
    rim_len = CONV_K - 1

    bc_tail = bc_raw[..., tokens - rim_len :]
    rims = passed_along(
        jnp.concatenate(
            [x_raw[tokens - rim_len :], bc_tail.reshape(-1, rim_len).transpose(1, 0)], 1
        ),
        "ctx",
        1,
    )
    x_rim = rims[:, :channels]
    bc_rim = rims[:, channels:].transpose(1, 0).reshape(bc_tail.shape)
    x_pad = jnp.concatenate([x_rim, x_raw], 0)
    x_all = conv_rows(x_pad, conv_x_w, conv_x_b)
    bc_weights = lax.dynamic_slice_in_dim(conv_bc_w, sub_index * half, half, 3)
    bc_bias = lax.dynamic_slice_in_dim(conv_bc_b, sub_index * half, half, 2)
    bc_conv = conv_cols(jnp.concatenate([bc_rim, bc_raw], 3), bc_weights, bc_bias)
    bc_halves = bc_conv.reshape(2, set_groups, half, nsub, own)
    bc_mine = lax.dynamic_index_in_dim(bc_halves, sub_index, 3, keepdims=False)
    bc_theirs = swapped(
        lax.dynamic_index_in_dim(bc_halves, 1 - sub_index, 3, keepdims=False), "sub"
    )
    bc_own = jnp.stack(
        [
            jnp.where(sub_index == 0, bc_mine, bc_theirs),
            jnp.where(sub_index == 0, bc_theirs, bc_mine),
        ],
        2,
    ).reshape(2, set_groups, state, own)
    b_rows = bc_own[0]
    c_cols = bc_own[1].transpose(0, 2, 1)

    step_sizes = jax.nn.softplus(dt_raw + dt_bias[:, None])
    log_decay = -jnp.exp(a_log)[:, None] * step_sizes
    half_totals = jnp.exp(log_decay.reshape(heads_dev, nsub, own).sum(-1))
    step_own = lax.dynamic_slice_in_dim(step_sizes, sub_index * own, own, 1)
    decay_own = lax.dynamic_slice_in_dim(log_decay, sub_index * own, own, 1)
    block_len = min(256, own)
    blocks = own // block_len
    upper = (
        lax.broadcasted_iota(jnp.int32, (block_len, block_len), 0)
        <= lax.broadcasted_iota(jnp.int32, (block_len, block_len), 1)
    ).astype(F32)
    cum_local = jnp.einsum(
        "hct,tu->hcu", decay_own.reshape(heads_dev, blocks, block_len), upper, precision=HIGHEST
    )
    block_totals = cum_local[..., -1]
    offsets = jnp.cumsum(block_totals, axis=-1) - block_totals
    cum_device = (cum_local + offsets[..., None]).reshape(set_groups, per_group, own)
    cum_rows = cum_local.reshape(set_groups, per_group, own)
    cum_cols = cum_rows.transpose(0, 2, 1)
    step_rows = step_own.reshape(set_groups, per_group, own)
    skip_row = jnp.repeat(d_skip, HEAD_DIM)[None, :]

    cum_all = jnp.einsum(
        "hjct,tu->hjcu",
        log_decay.reshape(heads_dev, nsub, blocks, block_len),
        upper,
        precision=HIGHEST,
    )
    all_totals = cum_all[..., -1]
    cum_all = (cum_all + (jnp.cumsum(all_totals, axis=-1) - all_totals)[..., None]).reshape(
        heads_dev, nsub, own
    )
    to_end = jnp.exp(cum_all[..., own - 1 :] - cum_all) * step_sizes.reshape(heads_dev, nsub, own)
    to_end = to_end.reshape(set_groups, per_group, tokens)
    ends = pl.pallas_call(
        end_kernel,
        grid=(nsub, set_groups),
        in_specs=[
            pl.BlockSpec((own, group_width), lambda j, g: (j, g)),
            pl.BlockSpec((1, half, own), lambda j, g: (g, 0, j)),
            pl.BlockSpec((1, per_group, own), lambda j, g: (g, 0, j)),
        ],
        out_specs=pl.BlockSpec((1, pairs, half, 128), lambda j, g: (j * set_groups + g, 0, 0, 0)),
        out_shape=jax.ShapeDtypeStruct((nsub * set_groups, pairs, half, 128), F32),
    )(x_all, bc_conv[0], to_end)
    ends = ends.reshape(nsub, set_groups, pairs, half, 128)

    def pair_layout(values):
        return jnp.repeat(values.reshape(set_groups, pairs, 2), HEAD_DIM, axis=-1)[:, :, None, :]

    decay_first = pair_layout(half_totals[:, 0])
    decay_second = pair_layout(half_totals[:, 1])
    first_end = ends[0]
    second_end = ends[1]
    chip_end = decay_second * first_end + second_end
    chip_decay = decay_first * decay_second
    ctx_index = lax.axis_index("ctx")
    packed = jnp.concatenate([chip_end, chip_decay], 2)
    packed, x_held = lax.optimization_barrier((packed, x_all))
    x_own = lax.dynamic_slice_in_dim(x_held, sub_index * own, own, 0)
    y_local = pl.pallas_call(
        scan_kernel,
        grid=(set_groups, blocks),
        in_specs=[
            pl.BlockSpec((block_len, group_width), lambda g, c: (c, g)),
            pl.BlockSpec((1, block_len, state), lambda g, c: (g, c, 0)),
            pl.BlockSpec((1, state, block_len), lambda g, c: (g, 0, c)),
            pl.BlockSpec((1, per_group, block_len), lambda g, c: (g, 0, c)),
            pl.BlockSpec((1, block_len, per_group), lambda g, c: (g, c, 0)),
            pl.BlockSpec((1, per_group, block_len), lambda g, c: (g, 0, c)),
            pl.BlockSpec((1, group_width), lambda g, c: (0, g)),
        ],
        out_specs=pl.BlockSpec((block_len, group_width), lambda g, c: (c, g)),
        out_shape=jax.ShapeDtypeStruct((own, channels), F32),
        scratch_shapes=[pltpu.VMEM((pairs, state, 128), F32)],
    )(x_own, c_cols, b_rows, cum_rows, cum_cols, step_rows, skip_row)

    gathered = lax.all_gather(packed, "ctx")
    gathered, y_local = lax.optimization_barrier((gathered, y_local))
    all_ends = gathered[:, :, :, :half]
    all_decays = gathered[:, :, :, half:]
    carried = jnp.zeros_like(chip_end)
    for earlier in range(lax.axis_size("ctx") - 1):
        carried = jnp.where(
            earlier < ctx_index, all_ends[earlier] + all_decays[earlier] * carried, carried
        )
    into_second = decay_first * carried + first_end
    keep = jnp.where(sub_index == 0, carried, into_second)
    got = swapped(jnp.where(sub_index == 0, into_second, carried), "sub")
    low = jnp.where(sub_index == 0, keep, got)
    high = jnp.where(sub_index == 0, got, keep)
    incoming = jnp.stack([low, high], 2).reshape(set_groups, pairs, state, 128)

    out_len = min(256, own)
    return pl.pallas_call(
        out_kernel,
        grid=(set_groups, own // out_len),
        in_specs=[
            pl.BlockSpec((out_len, group_width), lambda g, c: (c, g)),
            pl.BlockSpec((1, out_len, state), lambda g, c: (g, c, 0)),
            pl.BlockSpec((1, out_len, per_group), lambda g, c: (g, c, 0)),
            pl.BlockSpec((1, pairs, state, 128), lambda g, c: (g, 0, 0, 0)),
            pl.BlockSpec((out_len, group_width), lambda g, c: (c, g)),
            pl.BlockSpec((1, group_width), lambda g, c: (0, g)),
        ],
        out_specs=pl.BlockSpec((out_len, group_width), lambda g, c: (c, g)),
        out_shape=jax.ShapeDtypeStruct((own, channels), jnp.bfloat16),
        scratch_shapes=[pltpu.VMEM((out_len, group_width), F32)],
    )(y_local, c_cols, cum_device.transpose(0, 2, 1), incoming, z_gate, norm_w[None, :])


def solution(mesh):
    in_specs = (
        P(("groups", "ctx"), "head"),
        P(None, "head", "sub", ("groups", "ctx")),
        P(("groups", "ctx", "sub"), "head"),
        P("head", ("groups", "ctx")),
        P(None, "head"),
        P("head"),
        P(None, None, "head", None),
        P(None, "head", None),
        P("head"),
        P("head"),
        P("head"),
        P("head"),
    )
    out_specs = P(("groups", "ctx", "sub"), "head")
    return jax.shard_map(
        per_device, mesh=mesh, in_specs=in_specs, out_specs=out_specs, check_vma=False
    )
```

```python
import jax
import jax.numpy as jnp
from jax import lax
from jax.experimental import pallas as pl
from jax.experimental.pallas import tpu as pltpu
from jax.sharding import PartitionSpec as P

HEADS = 128
HEAD_DIM = 64
GROUPS = 8
CONV_K = 4


HIGHEST = lax.Precision.HIGHEST
F32 = jnp.float32


def passed_along(x, axis, by):
    length = lax.axis_size(axis)
    pairs = [(i, i + by) for i in range(length) if 0 <= i + by < length]
    return lax.ppermute(x, axis, pairs)


def swapped(x, axis):
    return lax.ppermute(x, axis, [(0, 1), (1, 0)])


def conv_rows(padded, weights, bias_row):
    sequence_length = padded.shape[0] - (CONV_K - 1)
    total = jnp.zeros((sequence_length, padded.shape[1]), jnp.float32) + bias_row[None, :]
    for tap_index in range(CONV_K):
        total = total + weights[tap_index][None, :] * padded[
            tap_index : tap_index + sequence_length
        ].astype(jnp.float32)
    return jax.nn.silu(total)


def conv_cols(padded, weights, bias_block):
    sequence_length = padded.shape[-1] - (CONV_K - 1)
    total = jnp.zeros(padded.shape[:-1] + (sequence_length,), jnp.float32) + bias_block[..., None]
    for tap_index in range(CONV_K):
        total = total + weights[tap_index][..., None] * padded[
            ..., tap_index : tap_index + sequence_length
        ].astype(jnp.float32)
    return jax.nn.silu(total)


def dot(a, b):
    return jnp.dot(a, b, precision=HIGHEST, preferred_element_type=F32)


def split(a):
    high = a.astype(jnp.bfloat16)
    return high, (a - high.astype(F32)).astype(jnp.bfloat16)


def dot3(a_parts, b_parts):
    a_high, a_low = a_parts
    b_high, b_low = b_parts
    flat = lambda u, v: jnp.dot(u, v, preferred_element_type=F32)
    return flat(a_high, b_high) + (flat(a_high, b_low) + flat(a_low, b_high))


def pair_columns(cumc, pair, rows):
    left = lax.broadcasted_iota(jnp.int32, (1, 128), 1) < HEAD_DIM
    return jnp.where(
        left,
        jnp.broadcast_to(cumc[:, 2 * pair : 2 * pair + 1], (rows, 128)),
        jnp.broadcast_to(cumc[:, 2 * pair + 1 : 2 * pair + 2], (rows, 128)),
    )


def scan_kernel(xc_ref, ct_ref, b_ref, cumr_ref, cumc_ref, stp_ref, dsk_ref, y_ref, e_ref):
    chunk = pl.program_id(1)
    block_len = xc_ref.shape[0]
    pairs = e_ref.shape[0]
    heads = 2 * pairs

    @pl.when(chunk == 0)
    def _():
        e_ref[...] = jnp.zeros_like(e_ref)

    ct = split(ct_ref[0])
    bm = b_ref[0]
    scores = dot3(ct, split(bm))
    rows = lax.broadcasted_iota(jnp.int32, (block_len, block_len), 0)
    cols = lax.broadcasted_iota(jnp.int32, (block_len, block_len), 1)
    causal = rows >= cols
    cumr = cumr_ref[0]
    cumc = cumc_ref[0]
    stp = stp_ref[0]
    left = lax.broadcasted_iota(jnp.int32, (1, 128), 1) < HEAD_DIM
    for pair in range(pairs):
        lanes = slice(pair * 128, (pair + 1) * 128)
        xp = xc_ref[:, lanes]
        xs = split(xp)
        s_old = e_ref[pair]
        ys = []
        us = []
        for side in range(2):
            head = 2 * pair + side
            dq = jnp.broadcast_to(cumc[:, head : head + 1], (block_len, block_len))
            ck = cumr[head : head + 1, :]
            sk = stp[head : head + 1, :]
            dec = jnp.exp(jnp.where(causal, dq - ck, -jnp.inf))
            ys.append(dot3(split(scores * dec * sk), xs))
            wk = jnp.exp(dq[block_len - 1 : block_len, :] - ck) * sk
            us.append(dot3(split(bm * wk), xs))
        cq = pair_columns(cumc, pair, block_len)
        inflow = dot3(ct, split(s_old)) * jnp.exp(cq)
        y = jnp.where(left, ys[0], ys[1]) + inflow
        y_ref[:, lanes] = y + xp * dsk_ref[:, lanes]
        e_ref[pair] = jnp.exp(cq[block_len - 1 : block_len, :]) * s_old + jnp.where(
            left, us[0], us[1]
        )


def end_kernel(xc_ref, b_ref, wk_ref, e_ref):
    pairs = e_ref.shape[1]
    bm = b_ref[0]
    wk = wk_ref[0]
    left = lax.broadcasted_iota(jnp.int32, (1, 128), 1) < HEAD_DIM
    for pair in range(pairs):
        xs = split(xc_ref[:, pair * 128 : (pair + 1) * 128])
        us = [
            dot3(split(bm * wk[2 * pair + side : 2 * pair + side + 1, :]), xs) for side in range(2)
        ]
        e_ref[0, pair] = jnp.where(left, us[0], us[1])


def out_kernel(y_ref, ct_ref, cumc_ref, v_ref, z_ref, nw_ref, o_ref, g_ref):
    pairs = v_ref.shape[1]
    heads = 2 * pairs
    ct = split(ct_ref[0])
    cumc = cumc_ref[0]
    total = jnp.zeros((y_ref.shape[0], 1), F32)
    for pair in range(pairs):
        lanes = slice(pair * 128, (pair + 1) * 128)
        cq = pair_columns(cumc, pair, y_ref.shape[0])
        y = y_ref[:, lanes] + dot3(ct, split(v_ref[0, pair])) * jnp.exp(cq)
        z = z_ref[:, lanes].astype(F32)
        gated = y * (z / (1.0 + jnp.exp(-z)))
        g_ref[:, lanes] = gated
        total = total + jnp.sum(gated * gated, axis=-1, keepdims=True)
    mean_square = total / g_ref.shape[1]
    o_ref[...] = (g_ref[...] * lax.rsqrt(mean_square + 1e-05) * nw_ref[...]).astype(o_ref.dtype)


def per_device(
    x_raw,
    bc_raw,
    z_gate,
    dt_raw,
    conv_x_w,
    conv_x_b,
    conv_bc_w,
    conv_bc_b,
    dt_bias,
    a_log,
    d_skip,
    norm_w,
):
    tokens = x_raw.shape[0]
    heads_dev = dt_raw.shape[0]
    per_group = HEADS // GROUPS
    set_groups = heads_dev // per_group
    pairs = per_group // 2
    group_width = per_group * HEAD_DIM
    nsub = lax.axis_size("sub")
    sub_index = lax.axis_index("sub")
    own = tokens // nsub
    half = bc_raw.shape[2]
    state = half * nsub
    channels = heads_dev * HEAD_DIM
    rim_len = CONV_K - 1

    bc_tail = bc_raw[..., tokens - rim_len :]
    rims = passed_along(
        jnp.concatenate(
            [x_raw[tokens - rim_len :], bc_tail.reshape(-1, rim_len).transpose(1, 0)], 1
        ),
        "ctx",
        1,
    )
    x_rim = rims[:, :channels]
    bc_rim = rims[:, channels:].transpose(1, 0).reshape(bc_tail.shape)
    x_pad = jnp.concatenate([x_rim, x_raw], 0)
    x_all = conv_rows(x_pad, conv_x_w, conv_x_b)
    bc_weights = lax.dynamic_slice_in_dim(conv_bc_w, sub_index * half, half, 3)
    bc_bias = lax.dynamic_slice_in_dim(conv_bc_b, sub_index * half, half, 2)
    bc_conv = conv_cols(jnp.concatenate([bc_rim, bc_raw], 3), bc_weights, bc_bias)
    bc_halves = bc_conv.reshape(2, set_groups, half, nsub, own)
    bc_mine = lax.dynamic_index_in_dim(bc_halves, sub_index, 3, keepdims=False)
    bc_theirs = swapped(
        lax.dynamic_index_in_dim(bc_halves, 1 - sub_index, 3, keepdims=False), "sub"
    )
    bc_own = jnp.stack(
        [
            jnp.where(sub_index == 0, bc_mine, bc_theirs),
            jnp.where(sub_index == 0, bc_theirs, bc_mine),
        ],
        2,
    ).reshape(2, set_groups, state, own)
    b_rows = bc_own[0]
    c_cols = bc_own[1].transpose(0, 2, 1)

    step_sizes = jax.nn.softplus(dt_raw + dt_bias[:, None])
    log_decay = -jnp.exp(a_log)[:, None] * step_sizes
    half_totals = jnp.exp(log_decay.reshape(heads_dev, nsub, own).sum(-1))
    step_own = lax.dynamic_slice_in_dim(step_sizes, sub_index * own, own, 1)
    decay_own = lax.dynamic_slice_in_dim(log_decay, sub_index * own, own, 1)
    block_len = min(256, own)
    blocks = own // block_len
    upper = (
        lax.broadcasted_iota(jnp.int32, (block_len, block_len), 0)
        <= lax.broadcasted_iota(jnp.int32, (block_len, block_len), 1)
    ).astype(F32)
    cum_local = jnp.einsum(
        "hct,tu->hcu", decay_own.reshape(heads_dev, blocks, block_len), upper, precision=HIGHEST
    )
    block_totals = cum_local[..., -1]
    offsets = jnp.cumsum(block_totals, axis=-1) - block_totals
    cum_device = (cum_local + offsets[..., None]).reshape(set_groups, per_group, own)
    cum_rows = cum_local.reshape(set_groups, per_group, own)
    cum_cols = cum_rows.transpose(0, 2, 1)
    step_rows = step_own.reshape(set_groups, per_group, own)
    skip_row = jnp.repeat(d_skip, HEAD_DIM)[None, :]

    cum_all = jnp.einsum(
        "hjct,tu->hjcu",
        log_decay.reshape(heads_dev, nsub, blocks, block_len),
        upper,
        precision=HIGHEST,
    )
    all_totals = cum_all[..., -1]
    cum_all = (cum_all + (jnp.cumsum(all_totals, axis=-1) - all_totals)[..., None]).reshape(
        heads_dev, nsub, own
    )
    to_end = jnp.exp(cum_all[..., own - 1 :] - cum_all) * step_sizes.reshape(heads_dev, nsub, own)
    to_end = to_end.reshape(set_groups, per_group, tokens)
    ends = pl.pallas_call(
        end_kernel,
        grid=(nsub, set_groups),
        in_specs=[
            pl.BlockSpec((own, group_width), lambda j, g: (j, g)),
            pl.BlockSpec((1, half, own), lambda j, g: (g, 0, j)),
            pl.BlockSpec((1, per_group, own), lambda j, g: (g, 0, j)),
        ],
        out_specs=pl.BlockSpec((1, pairs, half, 128), lambda j, g: (j * set_groups + g, 0, 0, 0)),
        out_shape=jax.ShapeDtypeStruct((nsub * set_groups, pairs, half, 128), F32),
    )(x_all, bc_conv[0], to_end)
    ends = ends.reshape(nsub, set_groups, pairs, half, 128)

    def pair_layout(values):
        return jnp.repeat(values.reshape(set_groups, pairs, 2), HEAD_DIM, axis=-1)[:, :, None, :]

    decay_first = pair_layout(half_totals[:, 0])
    decay_second = pair_layout(half_totals[:, 1])
    first_end = ends[0]
    second_end = ends[1]
    chip_end = decay_second * first_end + second_end
    chip_decay = decay_first * decay_second
    ctx_index = lax.axis_index("ctx")
    ctx_size = lax.axis_size("ctx")
    x_own = lax.dynamic_slice_in_dim(x_all, sub_index * own, own, 0)
    scan_inputs = (x_own, c_cols, b_rows, cum_rows, cum_cols, step_rows, skip_row)

    def scan_group(group, inputs, target):
        extra = {} if target is None else {"input_output_aliases": {len(inputs): 0}}
        in_specs = [
            pl.BlockSpec((block_len, group_width), lambda g, c: (c, group)),
            pl.BlockSpec((1, block_len, state), lambda g, c: (group, c, 0)),
            pl.BlockSpec((1, state, block_len), lambda g, c: (group, 0, c)),
            pl.BlockSpec((1, per_group, block_len), lambda g, c: (group, 0, c)),
            pl.BlockSpec((1, block_len, per_group), lambda g, c: (group, c, 0)),
            pl.BlockSpec((1, per_group, block_len), lambda g, c: (group, 0, c)),
            pl.BlockSpec((1, group_width), lambda g, c: (0, group)),
        ]
        operands = tuple(inputs)
        if target is not None:
            in_specs.append(pl.BlockSpec(memory_space=pl.ANY))
            operands = operands + (target,)
        kernel = scan_kernel if target is None else (lambda *refs: scan_kernel(*refs[:7], *refs[8:]))
        return pl.pallas_call(
            kernel,
            grid=(1, blocks),
            in_specs=in_specs,
            out_specs=pl.BlockSpec((block_len, group_width), lambda g, c: (c, group)),
            out_shape=jax.ShapeDtypeStruct((own, channels), F32),
            scratch_shapes=[pltpu.VMEM((pairs, state, 128), F32)],
            **extra,
        )(*operands)

    pieces = 2 if (set_groups * pairs) % 2 == 0 else 1
    rounds = ctx_size + pieces - 2
    piece_shape = (pieces, set_groups * pairs // pieces, half, 128)
    end_pieces = chip_end.reshape(piece_shape)
    decay_pieces = jnp.broadcast_to(chip_decay, chip_end.shape).reshape(piece_shape)
    received = jnp.zeros(piece_shape, F32)
    y_local = None
    placed = [min(group, max(rounds, 1) - 1) for group in range(set_groups)]
    for step_index in range(max(rounds, 1)):
        send_at = jnp.clip(step_index - ctx_index, 0, pieces - 1)
        outgoing = lax.dynamic_index_in_dim(
            end_pieces, send_at, 0, keepdims=False
        ) + lax.dynamic_index_in_dim(decay_pieces, send_at, 0, keepdims=False) * (
            lax.dynamic_index_in_dim(received, send_at, 0, keepdims=False)
        )
        held = scan_inputs
        if any(p == step_index for p in placed):
            outgoing, held = lax.optimization_barrier((outgoing, scan_inputs))
        if rounds > 0:
            arrived = passed_along(outgoing, "ctx", 1)
        for group in range(set_groups):
            if placed[group] == step_index:
                y_local = scan_group(group, held, y_local)
        if rounds == 0:
            break
        if any(p == step_index for p in placed):
            arrived, y_local = lax.optimization_barrier((arrived, y_local))
        recv_at = step_index - ctx_index + 1
        valid = (recv_at >= 0) & (recv_at < pieces) & (ctx_index > 0)
        updated = lax.dynamic_update_index_in_dim(
            received, arrived, jnp.clip(recv_at, 0, pieces - 1), 0
        )
        received = jnp.where(valid, updated, received)
    carried = received.reshape(chip_end.shape)
    into_second = decay_first * carried + first_end
    keep = jnp.where(sub_index == 0, carried, into_second)
    got = swapped(jnp.where(sub_index == 0, into_second, carried), "sub")
    low = jnp.where(sub_index == 0, keep, got)
    high = jnp.where(sub_index == 0, got, keep)
    incoming = jnp.stack([low, high], 2).reshape(set_groups, pairs, state, 128)

    out_len = min(256, own)
    return pl.pallas_call(
        out_kernel,
        grid=(set_groups, own // out_len),
        in_specs=[
            pl.BlockSpec((out_len, group_width), lambda g, c: (c, g)),
            pl.BlockSpec((1, out_len, state), lambda g, c: (g, c, 0)),
            pl.BlockSpec((1, out_len, per_group), lambda g, c: (g, c, 0)),
            pl.BlockSpec((1, pairs, state, 128), lambda g, c: (g, 0, 0, 0)),
            pl.BlockSpec((out_len, group_width), lambda g, c: (c, g)),
            pl.BlockSpec((1, group_width), lambda g, c: (0, g)),
        ],
        out_specs=pl.BlockSpec((out_len, group_width), lambda g, c: (c, g)),
        out_shape=jax.ShapeDtypeStruct((own, channels), jnp.bfloat16),
        scratch_shapes=[pltpu.VMEM((out_len, group_width), F32)],
    )(y_local, c_cols, cum_device.transpose(0, 2, 1), incoming, z_gate, norm_w[None, :])


def solution(mesh):
    in_specs = (
        P(("groups", "ctx"), "head"),
        P(None, "head", "sub", ("groups", "ctx")),
        P(("groups", "ctx", "sub"), "head"),
        P("head", ("groups", "ctx")),
        P(None, "head"),
        P("head"),
        P(None, None, "head", None),
        P(None, "head", None),
        P("head"),
        P("head"),
        P("head"),
        P("head"),
    )
    out_specs = P(("groups", "ctx", "sub"), "head")
    return jax.shard_map(
        per_device, mesh=mesh, in_specs=in_specs, out_specs=out_specs, check_vma=False
    )
```

```python
import jax
import jax.numpy as jnp
from jax import lax
from jax.experimental import pallas as pl
from jax.experimental.pallas import tpu as pltpu
from jax.sharding import PartitionSpec as P

HEADS = 128
HEAD_DIM = 64
GROUPS = 8
CONV_K = 4


HIGHEST = lax.Precision.HIGHEST
F32 = jnp.float32


def passed_along(x, axis, by):
    length = lax.axis_size(axis)
    pairs = [(i, i + by) for i in range(length) if 0 <= i + by < length]
    return lax.ppermute(x, axis, pairs)


def swapped(x, axis):
    return lax.ppermute(x, axis, [(0, 1), (1, 0)])


def conv_rows(padded, weights, bias_row):
    sequence_length = padded.shape[0] - (CONV_K - 1)
    total = jnp.zeros((sequence_length, padded.shape[1]), jnp.float32) + bias_row[None, :]
    for tap_index in range(CONV_K):
        total = total + weights[tap_index][None, :] * padded[
            tap_index : tap_index + sequence_length
        ].astype(jnp.float32)
    return jax.nn.silu(total)


def conv_cols(padded, weights, bias_block):
    sequence_length = padded.shape[-1] - (CONV_K - 1)
    total = jnp.zeros(padded.shape[:-1] + (sequence_length,), jnp.float32) + bias_block[..., None]
    for tap_index in range(CONV_K):
        total = total + weights[tap_index][..., None] * padded[
            ..., tap_index : tap_index + sequence_length
        ].astype(jnp.float32)
    return jax.nn.silu(total)


def dot(a, b):
    return jnp.dot(a, b, precision=HIGHEST, preferred_element_type=F32)


def split(a):
    high = a.astype(jnp.bfloat16)
    return high, (a - high.astype(F32)).astype(jnp.bfloat16)


def dot3(a_parts, b_parts):
    a_high, a_low = a_parts
    b_high, b_low = b_parts
    flat = lambda u, v: jnp.dot(u, v, preferred_element_type=F32)
    return flat(a_high, b_high) + (flat(a_high, b_low) + flat(a_low, b_high))


def pair_columns(cumc, pair, rows):
    left = lax.broadcasted_iota(jnp.int32, (1, 128), 1) < HEAD_DIM
    return jnp.where(
        left,
        jnp.broadcast_to(cumc[:, 2 * pair : 2 * pair + 1], (rows, 128)),
        jnp.broadcast_to(cumc[:, 2 * pair + 1 : 2 * pair + 2], (rows, 128)),
    )


def scan_kernel(xc_ref, ct_ref, b_ref, cumr_ref, cumc_ref, stp_ref, dsk_ref, y_ref, e_ref):
    chunk = pl.program_id(1)
    block_len = xc_ref.shape[1]
    pairs = e_ref.shape[0]
    heads = 2 * pairs

    @pl.when(chunk == 0)
    def _():
        e_ref[...] = jnp.zeros_like(e_ref)

    ct = split(ct_ref[0])
    bm = b_ref[0]
    scores = dot3(ct, split(bm))
    rows = lax.broadcasted_iota(jnp.int32, (block_len, block_len), 0)
    cols = lax.broadcasted_iota(jnp.int32, (block_len, block_len), 1)
    causal = rows >= cols
    cumr = cumr_ref[0]
    cumc = cumc_ref[0]
    stp = stp_ref[0]
    left = lax.broadcasted_iota(jnp.int32, (1, 128), 1) < HEAD_DIM
    for pair in range(pairs):
        lanes = slice(pair * 128, (pair + 1) * 128)
        xs = (xc_ref[0, :, lanes], xc_ref[1, :, lanes])
        xp = xs[0].astype(F32) + xs[1].astype(F32)
        s_old = e_ref[pair]
        ys = []
        us = []
        for side in range(2):
            head = 2 * pair + side
            dq = jnp.broadcast_to(cumc[:, head : head + 1], (block_len, block_len))
            ck = cumr[head : head + 1, :]
            sk = stp[head : head + 1, :]
            dec = jnp.exp(jnp.where(causal, dq - ck, -jnp.inf))
            ys.append(dot3(split(scores * dec * sk), xs))
            wk = jnp.exp(dq[block_len - 1 : block_len, :] - ck) * sk
            us.append(dot3(split(bm * wk), xs))
        cq = pair_columns(cumc, pair, block_len)
        inflow = dot3(ct, split(s_old)) * jnp.exp(cq)
        y = jnp.where(left, ys[0], ys[1]) + inflow
        y_ref[:, lanes] = y + xp * dsk_ref[:, lanes]
        e_ref[pair] = jnp.exp(cq[block_len - 1 : block_len, :]) * s_old + jnp.where(
            left, us[0], us[1]
        )


def conv_kernel(flag_ref, rim_ref, x_ref, w_ref, b_ref, all_ref, own_ref):
    rows = x_ref.shape[0]
    own = own_ref.shape[1]
    lead = rim_ref.shape[0] - (CONV_K - 1)
    padded = jnp.concatenate([rim_ref[...].astype(F32), x_ref[...].astype(F32)], 0)
    total = b_ref[...] + w_ref[0:1, :] * padded[lead : lead + rows]
    for tap_index in range(1, CONV_K):
        total = total + w_ref[tap_index : tap_index + 1, :] * padded[
            lead + tap_index : lead + tap_index + rows
        ]
    high, low = split(total / (1.0 + jnp.exp(-total)))
    all_ref[0] = high
    all_ref[1] = low
    first = flag_ref[0:1, 0:1] > 0.5
    own_ref[0] = jnp.where(first, high[:own], high[own:])
    own_ref[1] = jnp.where(first, low[:own], low[own:])


def end_kernel(xc_ref, b_ref, wk_ref, e_ref):
    pairs = e_ref.shape[1]
    bm = b_ref[0]
    wk = wk_ref[0]
    left = lax.broadcasted_iota(jnp.int32, (1, 128), 1) < HEAD_DIM
    for pair in range(pairs):
        lanes = slice(pair * 128, (pair + 1) * 128)
        xs = (xc_ref[0, :, lanes], xc_ref[1, :, lanes])
        us = [
            dot3(split(bm * wk[2 * pair + side : 2 * pair + side + 1, :]), xs) for side in range(2)
        ]
        e_ref[0, pair] = jnp.where(left, us[0], us[1])


def out_kernel(y_ref, ct_ref, cumc_ref, v_ref, z_ref, nw_ref, o_ref, g_ref):
    pairs = v_ref.shape[1]
    heads = 2 * pairs
    ct = split(ct_ref[0])
    cumc = cumc_ref[0]
    total = jnp.zeros((y_ref.shape[0], 1), F32)
    for pair in range(pairs):
        lanes = slice(pair * 128, (pair + 1) * 128)
        cq = pair_columns(cumc, pair, y_ref.shape[0])
        y = y_ref[:, lanes] + dot3(ct, split(v_ref[0, pair])) * jnp.exp(cq)
        z = z_ref[:, lanes].astype(F32)
        gated = y * (z / (1.0 + jnp.exp(-z)))
        g_ref[:, lanes] = gated
        total = total + jnp.sum(gated * gated, axis=-1, keepdims=True)
    mean_square = total / g_ref.shape[1]
    o_ref[...] = (g_ref[...] * lax.rsqrt(mean_square + 1e-05) * nw_ref[...]).astype(o_ref.dtype)


def per_device(
    x_raw,
    bc_raw,
    z_gate,
    dt_raw,
    conv_x_w,
    conv_x_b,
    conv_bc_w,
    conv_bc_b,
    dt_bias,
    a_log,
    d_skip,
    norm_w,
):
    tokens = x_raw.shape[0]
    heads_dev = dt_raw.shape[0]
    per_group = HEADS // GROUPS
    set_groups = heads_dev // per_group
    pairs = per_group // 2
    group_width = per_group * HEAD_DIM
    nsub = lax.axis_size("sub")
    sub_index = lax.axis_index("sub")
    own = tokens // nsub
    half = bc_raw.shape[2]
    state = half * nsub
    channels = heads_dev * HEAD_DIM
    rim_len = CONV_K - 1

    bc_tail = bc_raw[..., tokens - rim_len :]
    rims = passed_along(
        jnp.concatenate(
            [x_raw[tokens - rim_len :], bc_tail.reshape(-1, rim_len).transpose(1, 0)], 1
        ),
        "ctx",
        1,
    )
    x_rim = rims[:, :channels]
    bc_rim = rims[:, channels:].transpose(1, 0).reshape(bc_tail.shape)
    rim_block = jnp.concatenate([jnp.zeros((8 - rim_len, channels), x_raw.dtype), x_rim], 0)
    first_flag = jnp.full((8, 128), sub_index == 0, F32)
    conv_width = min(512, channels)
    x_all, x_own = pl.pallas_call(
        conv_kernel,
        grid=(channels // conv_width,),
        in_specs=[
            pl.BlockSpec((8, 128), lambda i: (0, 0)),
            pl.BlockSpec((8, conv_width), lambda i: (0, i)),
            pl.BlockSpec((tokens, conv_width), lambda i: (0, i)),
            pl.BlockSpec((CONV_K, conv_width), lambda i: (0, i)),
            pl.BlockSpec((1, conv_width), lambda i: (0, i)),
        ],
        out_specs=[
            pl.BlockSpec((2, tokens, conv_width), lambda i: (0, 0, i)),
            pl.BlockSpec((2, own, conv_width), lambda i: (0, 0, i)),
        ],
        out_shape=[
            jax.ShapeDtypeStruct((2, tokens, channels), jnp.bfloat16),
            jax.ShapeDtypeStruct((2, own, channels), jnp.bfloat16),
        ],
    )(first_flag, rim_block, x_raw, conv_x_w, conv_x_b[None, :])
    bc_weights = lax.dynamic_slice_in_dim(conv_bc_w, sub_index * half, half, 3)
    bc_bias = lax.dynamic_slice_in_dim(conv_bc_b, sub_index * half, half, 2)
    bc_conv = conv_cols(jnp.concatenate([bc_rim, bc_raw], 3), bc_weights, bc_bias)
    bc_halves = bc_conv.reshape(2, set_groups, half, nsub, own)
    bc_mine = lax.dynamic_index_in_dim(bc_halves, sub_index, 3, keepdims=False)
    bc_theirs = swapped(
        lax.dynamic_index_in_dim(bc_halves, 1 - sub_index, 3, keepdims=False), "sub"
    )
    bc_own = jnp.stack(
        [
            jnp.where(sub_index == 0, bc_mine, bc_theirs),
            jnp.where(sub_index == 0, bc_theirs, bc_mine),
        ],
        2,
    ).reshape(2, set_groups, state, own)
    b_rows = bc_own[0]
    c_cols = bc_own[1].transpose(0, 2, 1)

    step_sizes = jax.nn.softplus(dt_raw + dt_bias[:, None])
    log_decay = -jnp.exp(a_log)[:, None] * step_sizes
    half_totals = jnp.exp(log_decay.reshape(heads_dev, nsub, own).sum(-1))
    step_own = lax.dynamic_slice_in_dim(step_sizes, sub_index * own, own, 1)
    decay_own = lax.dynamic_slice_in_dim(log_decay, sub_index * own, own, 1)
    block_len = min(256, own)
    blocks = own // block_len
    upper = (
        lax.broadcasted_iota(jnp.int32, (block_len, block_len), 0)
        <= lax.broadcasted_iota(jnp.int32, (block_len, block_len), 1)
    ).astype(F32)
    cum_local = jnp.einsum(
        "hct,tu->hcu", decay_own.reshape(heads_dev, blocks, block_len), upper, precision=HIGHEST
    )
    block_totals = cum_local[..., -1]
    offsets = jnp.cumsum(block_totals, axis=-1) - block_totals
    cum_device = (cum_local + offsets[..., None]).reshape(set_groups, per_group, own)
    cum_rows = cum_local.reshape(set_groups, per_group, own)
    cum_cols = cum_rows.transpose(0, 2, 1)
    step_rows = step_own.reshape(set_groups, per_group, own)
    skip_row = jnp.repeat(d_skip, HEAD_DIM)[None, :]

    cum_all = jnp.einsum(
        "hjct,tu->hjcu",
        log_decay.reshape(heads_dev, nsub, blocks, block_len),
        upper,
        precision=HIGHEST,
    )
    all_totals = cum_all[..., -1]
    cum_all = (cum_all + (jnp.cumsum(all_totals, axis=-1) - all_totals)[..., None]).reshape(
        heads_dev, nsub, own
    )
    to_end = jnp.exp(cum_all[..., own - 1 :] - cum_all) * step_sizes.reshape(heads_dev, nsub, own)
    to_end = to_end.reshape(set_groups, per_group, tokens)
    ends = pl.pallas_call(
        end_kernel,
        grid=(nsub, set_groups),
        in_specs=[
            pl.BlockSpec((2, own, group_width), lambda j, g: (0, j, g)),
            pl.BlockSpec((1, half, own), lambda j, g: (g, 0, j)),
            pl.BlockSpec((1, per_group, own), lambda j, g: (g, 0, j)),
        ],
        out_specs=pl.BlockSpec((1, pairs, half, 128), lambda j, g: (j * set_groups + g, 0, 0, 0)),
        out_shape=jax.ShapeDtypeStruct((nsub * set_groups, pairs, half, 128), F32),
    )(x_all, bc_conv[0], to_end)
    ends = ends.reshape(nsub, set_groups, pairs, half, 128)

    def pair_layout(values):
        return jnp.repeat(values.reshape(set_groups, pairs, 2), HEAD_DIM, axis=-1)[:, :, None, :]

    decay_first = pair_layout(half_totals[:, 0])
    decay_second = pair_layout(half_totals[:, 1])
    first_end = ends[0]
    second_end = ends[1]
    chip_end = decay_second * first_end + second_end
    chip_decay = decay_first * decay_second
    ctx_index = lax.axis_index("ctx")
    ctx_size = lax.axis_size("ctx")
    scan_inputs = (x_own, c_cols, b_rows, cum_rows, cum_cols, step_rows, skip_row)

    def scan_group(group, inputs, target):
        extra = {} if target is None else {"input_output_aliases": {len(inputs): 0}}
        in_specs = [
            pl.BlockSpec((2, block_len, group_width), lambda g, c: (0, c, group)),
            pl.BlockSpec((1, block_len, state), lambda g, c: (group, c, 0)),
            pl.BlockSpec((1, state, block_len), lambda g, c: (group, 0, c)),
            pl.BlockSpec((1, per_group, block_len), lambda g, c: (group, 0, c)),
            pl.BlockSpec((1, block_len, per_group), lambda g, c: (group, c, 0)),
            pl.BlockSpec((1, per_group, block_len), lambda g, c: (group, 0, c)),
            pl.BlockSpec((1, group_width), lambda g, c: (0, group)),
        ]
        operands = tuple(inputs)
        if target is not None:
            in_specs.append(pl.BlockSpec(memory_space=pl.ANY))
            operands = operands + (target,)
        kernel = scan_kernel if target is None else (lambda *refs: scan_kernel(*refs[:7], *refs[8:]))
        return pl.pallas_call(
            kernel,
            grid=(1, blocks),
            in_specs=in_specs,
            out_specs=pl.BlockSpec((block_len, group_width), lambda g, c: (c, group)),
            out_shape=jax.ShapeDtypeStruct((own, channels), F32),
            scratch_shapes=[pltpu.VMEM((pairs, state, 128), F32)],
            **extra,
        )(*operands)

    pieces = 2 if (set_groups * pairs) % 2 == 0 else 1
    rounds = ctx_size + pieces - 2
    piece_shape = (pieces, set_groups * pairs // pieces, half, 128)
    end_pieces = chip_end.reshape(piece_shape)
    decay_pieces = jnp.broadcast_to(chip_decay, chip_end.shape).reshape(piece_shape)
    received = jnp.zeros(piece_shape, F32)
    y_local = None
    placed = [min(group, max(rounds, 1) - 1) for group in range(set_groups)]
    for step_index in range(max(rounds, 1)):
        send_at = jnp.clip(step_index - ctx_index, 0, pieces - 1)
        outgoing = lax.dynamic_index_in_dim(
            end_pieces, send_at, 0, keepdims=False
        ) + lax.dynamic_index_in_dim(decay_pieces, send_at, 0, keepdims=False) * (
            lax.dynamic_index_in_dim(received, send_at, 0, keepdims=False)
        )
        held = scan_inputs
        if any(p == step_index for p in placed):
            outgoing, held = lax.optimization_barrier((outgoing, scan_inputs))
        if rounds > 0:
            arrived = passed_along(outgoing, "ctx", 1)
        for group in range(set_groups):
            if placed[group] == step_index:
                y_local = scan_group(group, held, y_local)
        if rounds == 0:
            break
        if any(p == step_index for p in placed):
            arrived, y_local = lax.optimization_barrier((arrived, y_local))
        recv_at = step_index - ctx_index + 1
        valid = (recv_at >= 0) & (recv_at < pieces) & (ctx_index > 0)
        updated = lax.dynamic_update_index_in_dim(
            received, arrived, jnp.clip(recv_at, 0, pieces - 1), 0
        )
        received = jnp.where(valid, updated, received)
    carried = received.reshape(chip_end.shape)
    into_second = decay_first * carried + first_end
    keep = jnp.where(sub_index == 0, carried, into_second)
    got = swapped(jnp.where(sub_index == 0, into_second, carried), "sub")
    low = jnp.where(sub_index == 0, keep, got)
    high = jnp.where(sub_index == 0, got, keep)
    incoming = jnp.stack([low, high], 2).reshape(set_groups, pairs, state, 128)

    out_len = min(256, own)
    return pl.pallas_call(
        out_kernel,
        grid=(set_groups, own // out_len),
        in_specs=[
            pl.BlockSpec((out_len, group_width), lambda g, c: (c, g)),
            pl.BlockSpec((1, out_len, state), lambda g, c: (g, c, 0)),
            pl.BlockSpec((1, out_len, per_group), lambda g, c: (g, c, 0)),
            pl.BlockSpec((1, pairs, state, 128), lambda g, c: (g, 0, 0, 0)),
            pl.BlockSpec((out_len, group_width), lambda g, c: (c, g)),
            pl.BlockSpec((1, group_width), lambda g, c: (0, g)),
        ],
        out_specs=pl.BlockSpec((out_len, group_width), lambda g, c: (c, g)),
        out_shape=jax.ShapeDtypeStruct((own, channels), jnp.bfloat16),
        scratch_shapes=[pltpu.VMEM((out_len, group_width), F32)],
    )(y_local, c_cols, cum_device.transpose(0, 2, 1), incoming, z_gate, norm_w[None, :])


def solution(mesh):
    in_specs = (
        P(("groups", "ctx"), "head"),
        P(None, "head", "sub", ("groups", "ctx")),
        P(("groups", "ctx", "sub"), "head"),
        P("head", ("groups", "ctx")),
        P(None, "head"),
        P("head"),
        P(None, None, "head", None),
        P(None, "head", None),
        P("head"),
        P("head"),
        P("head"),
        P("head"),
    )
    out_specs = P(("groups", "ctx", "sub"), "head")
    return jax.shard_map(
        per_device, mesh=mesh, in_specs=in_specs, out_specs=out_specs, check_vma=False
    )
```

```python
import jax
import jax.numpy as jnp
from jax import lax
from jax.experimental import pallas as pl
from jax.experimental.pallas import tpu as pltpu
from jax.sharding import PartitionSpec as P

HEADS = 128
HEAD_DIM = 64
GROUPS = 8
CONV_K = 4


HIGHEST = lax.Precision.HIGHEST
F32 = jnp.float32


def passed_along(x, axis, by):
    length = lax.axis_size(axis)
    pairs = [(i, i + by) for i in range(length) if 0 <= i + by < length]
    return lax.ppermute(x, axis, pairs)


def swapped(x, axis):
    return lax.ppermute(x, axis, [(0, 1), (1, 0)])


def conv_rows(padded, weights, bias_row):
    sequence_length = padded.shape[0] - (CONV_K - 1)
    total = jnp.zeros((sequence_length, padded.shape[1]), jnp.float32) + bias_row[None, :]
    for tap_index in range(CONV_K):
        total = total + weights[tap_index][None, :] * padded[
            tap_index : tap_index + sequence_length
        ].astype(jnp.float32)
    return jax.nn.silu(total)


def conv_cols(padded, weights, bias_block):
    sequence_length = padded.shape[-1] - (CONV_K - 1)
    total = jnp.zeros(padded.shape[:-1] + (sequence_length,), jnp.float32) + bias_block[..., None]
    for tap_index in range(CONV_K):
        total = total + weights[tap_index][..., None] * padded[
            ..., tap_index : tap_index + sequence_length
        ].astype(jnp.float32)
    return jax.nn.silu(total)


def dot(a, b):
    return jnp.dot(a, b, precision=HIGHEST, preferred_element_type=F32)


def split(a):
    high = a.astype(jnp.bfloat16)
    return high, (a - high.astype(F32)).astype(jnp.bfloat16)


def dot3(a_parts, b_parts):
    a_high, a_low = a_parts
    b_high, b_low = b_parts
    flat = lambda u, v: jnp.dot(u, v, preferred_element_type=F32)
    return flat(a_high, b_high) + (flat(a_high, b_low) + flat(a_low, b_high))


def pair_columns(cumc, pair, rows):
    left = lax.broadcasted_iota(jnp.int32, (1, 128), 1) < HEAD_DIM
    return jnp.where(
        left,
        jnp.broadcast_to(cumc[:, 2 * pair : 2 * pair + 1], (rows, 128)),
        jnp.broadcast_to(cumc[:, 2 * pair + 1 : 2 * pair + 2], (rows, 128)),
    )


def scan_kernel(xc_ref, ct_ref, b_ref, cumr_ref, cumc_ref, stp_ref, dsk_ref, y_ref, e_ref):
    chunk = pl.program_id(1)
    block_len = xc_ref.shape[0]
    pairs = e_ref.shape[0]
    heads = 2 * pairs

    @pl.when(chunk == 0)
    def _():
        e_ref[...] = jnp.zeros_like(e_ref)

    ct = split(ct_ref[0])
    bm = b_ref[0]
    scores = dot3(ct, split(bm))
    rows = lax.broadcasted_iota(jnp.int32, (block_len, block_len), 0)
    cols = lax.broadcasted_iota(jnp.int32, (block_len, block_len), 1)
    causal = rows >= cols
    cumr = cumr_ref[0]
    cumc = cumc_ref[0]
    stp = stp_ref[0]
    left = lax.broadcasted_iota(jnp.int32, (1, 128), 1) < HEAD_DIM
    for pair in range(pairs):
        lanes = slice(pair * 128, (pair + 1) * 128)
        xp = xc_ref[:, lanes]
        xs = split(xp)
        s_old = e_ref[pair]
        ys = []
        us = []
        for side in range(2):
            head = 2 * pair + side
            dq = jnp.broadcast_to(cumc[:, head : head + 1], (block_len, block_len))
            ck = cumr[head : head + 1, :]
            sk = stp[head : head + 1, :]
            dec = jnp.exp(jnp.where(causal, dq - ck, -jnp.inf))
            ys.append(dot3(split(scores * dec * sk), xs))
            wk = jnp.exp(dq[block_len - 1 : block_len, :] - ck) * sk
            us.append(dot3(split(bm * wk), xs))
        cq = pair_columns(cumc, pair, block_len)
        inflow = dot3(ct, split(s_old)) * jnp.exp(cq)
        y = jnp.where(left, ys[0], ys[1]) + inflow
        y_ref[:, lanes] = y + xp * dsk_ref[:, lanes]
        e_ref[pair] = jnp.exp(cq[block_len - 1 : block_len, :]) * s_old + jnp.where(
            left, us[0], us[1]
        )


def end_kernel(xc_ref, b_ref, wk_ref, e_ref):
    pairs = e_ref.shape[1]
    bm = b_ref[0]
    wk = wk_ref[0]
    left = lax.broadcasted_iota(jnp.int32, (1, 128), 1) < HEAD_DIM
    for pair in range(pairs):
        xs = split(xc_ref[:, pair * 128 : (pair + 1) * 128])
        us = [
            dot3(split(bm * wk[2 * pair + side : 2 * pair + side + 1, :]), xs) for side in range(2)
        ]
        e_ref[0, pair] = jnp.where(left, us[0], us[1])


def out_kernel(y_ref, ct_ref, cumc_ref, v_ref, z_ref, nw_ref, o_ref, g_ref):
    pairs = v_ref.shape[1]
    heads = 2 * pairs
    ct = split(ct_ref[0])
    cumc = cumc_ref[0]
    total = jnp.zeros((y_ref.shape[0], 1), F32)
    for pair in range(pairs):
        lanes = slice(pair * 128, (pair + 1) * 128)
        cq = pair_columns(cumc, pair, y_ref.shape[0])
        y = y_ref[:, lanes] + dot3(ct, split(v_ref[0, pair])) * jnp.exp(cq)
        z = z_ref[:, lanes].astype(F32)
        gated = y * (z / (1.0 + jnp.exp(-z)))
        g_ref[:, lanes] = gated
        total = total + jnp.sum(gated * gated, axis=-1, keepdims=True)
    mean_square = total / g_ref.shape[1]
    o_ref[...] = (g_ref[...] * lax.rsqrt(mean_square + 1e-05) * nw_ref[...]).astype(o_ref.dtype)


def per_device(
    x_raw,
    bc_raw,
    z_gate,
    dt_raw,
    conv_x_w,
    conv_x_b,
    conv_bc_w,
    conv_bc_b,
    dt_bias,
    a_log,
    d_skip,
    norm_w,
):
    tokens = x_raw.shape[0]
    heads_dev = dt_raw.shape[0]
    per_group = HEADS // GROUPS
    set_groups = heads_dev // per_group
    pairs = per_group // 2
    group_width = per_group * HEAD_DIM
    nsub = lax.axis_size("sub")
    sub_index = lax.axis_index("sub")
    own = tokens // nsub
    half = bc_raw.shape[2]
    state = half * nsub
    channels = heads_dev * HEAD_DIM
    rim_len = CONV_K - 1

    bc_tail = bc_raw[..., tokens - rim_len :]
    rims = passed_along(
        jnp.concatenate(
            [x_raw[tokens - rim_len :], bc_tail.reshape(-1, rim_len).transpose(1, 0)], 1
        ),
        "ctx",
        1,
    )
    x_rim = rims[:, :channels]
    bc_rim = rims[:, channels:].transpose(1, 0).reshape(bc_tail.shape)
    x_pad = jnp.concatenate([x_rim, x_raw], 0)
    x_own = conv_rows(
        lax.dynamic_slice_in_dim(x_pad, sub_index * own, own + rim_len, 0), conv_x_w, conv_x_b
    )
    x_other = conv_rows(
        lax.dynamic_slice_in_dim(x_pad, (1 - sub_index) * own, own + rim_len, 0),
        conv_x_w,
        conv_x_b,
    )
    bc_weights = lax.dynamic_slice_in_dim(conv_bc_w, sub_index * half, half, 3)
    bc_bias = lax.dynamic_slice_in_dim(conv_bc_b, sub_index * half, half, 2)
    bc_conv = conv_cols(jnp.concatenate([bc_rim, bc_raw], 3), bc_weights, bc_bias)
    bc_halves = bc_conv.reshape(2, set_groups, half, nsub, own)
    bc_mine = lax.dynamic_index_in_dim(bc_halves, sub_index, 3, keepdims=False)
    bc_theirs = swapped(
        lax.dynamic_index_in_dim(bc_halves, 1 - sub_index, 3, keepdims=False), "sub"
    )
    bc_own = jnp.stack(
        [
            jnp.where(sub_index == 0, bc_mine, bc_theirs),
            jnp.where(sub_index == 0, bc_theirs, bc_mine),
        ],
        2,
    ).reshape(2, set_groups, state, own)
    b_rows = bc_own[0]
    c_cols = bc_own[1].transpose(0, 2, 1)

    step_sizes = jax.nn.softplus(dt_raw + dt_bias[:, None])
    log_decay = -jnp.exp(a_log)[:, None] * step_sizes
    half_totals = jnp.exp(log_decay.reshape(heads_dev, nsub, own).sum(-1))
    step_own = lax.dynamic_slice_in_dim(step_sizes, sub_index * own, own, 1)
    decay_own = lax.dynamic_slice_in_dim(log_decay, sub_index * own, own, 1)
    block_len = min(128, own)
    blocks = own // block_len
    upper = (
        lax.broadcasted_iota(jnp.int32, (block_len, block_len), 0)
        <= lax.broadcasted_iota(jnp.int32, (block_len, block_len), 1)
    ).astype(F32)
    cum_local = jnp.einsum(
        "hct,tu->hcu", decay_own.reshape(heads_dev, blocks, block_len), upper, precision=HIGHEST
    )
    block_totals = cum_local[..., -1]
    offsets = jnp.cumsum(block_totals, axis=-1) - block_totals
    cum_device = (cum_local + offsets[..., None]).reshape(set_groups, per_group, own)
    cum_rows = cum_local.reshape(set_groups, per_group, own)
    cum_cols = cum_rows.transpose(0, 2, 1)
    step_rows = step_own.reshape(set_groups, per_group, own)
    skip_row = jnp.repeat(d_skip, HEAD_DIM)[None, :]

    cum_all = jnp.einsum(
        "hjct,tu->hjcu",
        log_decay.reshape(heads_dev, nsub, blocks, block_len),
        upper,
        precision=HIGHEST,
    )
    all_totals = cum_all[..., -1]
    cum_all = (cum_all + (jnp.cumsum(all_totals, axis=-1) - all_totals)[..., None]).reshape(
        heads_dev, nsub, own
    )
    to_end = jnp.exp(cum_all[..., own - 1 :] - cum_all) * step_sizes.reshape(heads_dev, nsub, own)
    to_end = to_end.reshape(set_groups, per_group, tokens)

    def end_states(x_half, at):
        return pl.pallas_call(
            end_kernel,
            grid=(set_groups,),
            in_specs=[
                pl.BlockSpec((own, group_width), lambda g: (0, g)),
                pl.BlockSpec((1, half, own), lambda g: (g, 0, 0)),
                pl.BlockSpec((1, per_group, own), lambda g: (g, 0, 0)),
            ],
            out_specs=pl.BlockSpec((1, pairs, half, 128), lambda g: (g, 0, 0, 0)),
            out_shape=jax.ShapeDtypeStruct((set_groups, pairs, half, 128), F32),
        )(
            x_half,
            lax.dynamic_slice_in_dim(bc_conv[0], at * own, own, 2),
            lax.dynamic_slice_in_dim(to_end, at * own, own, 2),
        )

    own_end = end_states(x_own, sub_index)
    other_end = end_states(x_other, 1 - sub_index)

    def pair_layout(values):
        return jnp.repeat(values.reshape(set_groups, pairs, 2), HEAD_DIM, axis=-1)[:, :, None, :]

    decay_first = pair_layout(half_totals[:, 0])
    decay_second = pair_layout(half_totals[:, 1])
    first_end = jnp.where(sub_index == 0, own_end, other_end)
    second_end = jnp.where(sub_index == 0, other_end, own_end)
    chip_end = decay_second * first_end + second_end
    chip_decay = decay_first * decay_second
    ctx_index = lax.axis_index("ctx")
    ctx_size = lax.axis_size("ctx")
    scan_inputs = (x_own, c_cols, b_rows, cum_rows, cum_cols, step_rows, skip_row)

    def scan_group(group, inputs, target):
        extra = {} if target is None else {"input_output_aliases": {len(inputs): 0}}
        in_specs = [
            pl.BlockSpec((block_len, group_width), lambda g, c: (c, group)),
            pl.BlockSpec((1, block_len, state), lambda g, c: (group, c, 0)),
            pl.BlockSpec((1, state, block_len), lambda g, c: (group, 0, c)),
            pl.BlockSpec((1, per_group, block_len), lambda g, c: (group, 0, c)),
            pl.BlockSpec((1, block_len, per_group), lambda g, c: (group, c, 0)),
            pl.BlockSpec((1, per_group, block_len), lambda g, c: (group, 0, c)),
            pl.BlockSpec((1, group_width), lambda g, c: (0, group)),
        ]
        operands = tuple(inputs)
        if target is not None:
            in_specs.append(pl.BlockSpec(memory_space=pl.ANY))
            operands = operands + (target,)
        kernel = scan_kernel if target is None else (lambda *refs: scan_kernel(*refs[:7], *refs[8:]))
        return pl.pallas_call(
            kernel,
            grid=(1, blocks),
            in_specs=in_specs,
            out_specs=pl.BlockSpec((block_len, group_width), lambda g, c: (c, group)),
            out_shape=jax.ShapeDtypeStruct((own, channels), F32),
            scratch_shapes=[pltpu.VMEM((pairs, state, 128), F32)],
            **extra,
        )(*operands)

    pieces = 2 if (set_groups * pairs) % 2 == 0 else 1
    rounds = ctx_size + pieces - 2
    piece_shape = (pieces, set_groups * pairs // pieces, half, 128)
    end_pieces = chip_end.reshape(piece_shape)
    decay_pieces = jnp.broadcast_to(chip_decay, chip_end.shape).reshape(piece_shape)
    received = jnp.zeros(piece_shape, F32)
    y_local = None
    placed = [min(group, max(rounds, 1) - 1) for group in range(set_groups)]
    for step_index in range(max(rounds, 1)):
        send_at = jnp.clip(step_index - ctx_index, 0, pieces - 1)
        outgoing = lax.dynamic_index_in_dim(
            end_pieces, send_at, 0, keepdims=False
        ) + lax.dynamic_index_in_dim(decay_pieces, send_at, 0, keepdims=False) * (
            lax.dynamic_index_in_dim(received, send_at, 0, keepdims=False)
        )
        held = scan_inputs
        if any(p == step_index for p in placed):
            outgoing, held = lax.optimization_barrier((outgoing, scan_inputs))
        if rounds > 0:
            arrived = passed_along(outgoing, "ctx", 1)
        for group in range(set_groups):
            if placed[group] == step_index:
                y_local = scan_group(group, held, y_local)
        if rounds == 0:
            break
        if any(p == step_index for p in placed):
            arrived, y_local = lax.optimization_barrier((arrived, y_local))
        recv_at = step_index - ctx_index + 1
        valid = (recv_at >= 0) & (recv_at < pieces) & (ctx_index > 0)
        updated = lax.dynamic_update_index_in_dim(
            received, arrived, jnp.clip(recv_at, 0, pieces - 1), 0
        )
        received = jnp.where(valid, updated, received)
    carried = received.reshape(chip_end.shape)
    into_second = decay_first * carried + first_end
    keep = jnp.where(sub_index == 0, carried, into_second)
    got = swapped(jnp.where(sub_index == 0, into_second, carried), "sub")
    low = jnp.where(sub_index == 0, keep, got)
    high = jnp.where(sub_index == 0, got, keep)
    incoming = jnp.stack([low, high], 2).reshape(set_groups, pairs, state, 128)

    out_len = min(256, own)
    return pl.pallas_call(
        out_kernel,
        grid=(set_groups, own // out_len),
        in_specs=[
            pl.BlockSpec((out_len, group_width), lambda g, c: (c, g)),
            pl.BlockSpec((1, out_len, state), lambda g, c: (g, c, 0)),
            pl.BlockSpec((1, out_len, per_group), lambda g, c: (g, c, 0)),
            pl.BlockSpec((1, pairs, state, 128), lambda g, c: (g, 0, 0, 0)),
            pl.BlockSpec((out_len, group_width), lambda g, c: (c, g)),
            pl.BlockSpec((1, group_width), lambda g, c: (0, g)),
        ],
        out_specs=pl.BlockSpec((out_len, group_width), lambda g, c: (c, g)),
        out_shape=jax.ShapeDtypeStruct((own, channels), jnp.bfloat16),
        scratch_shapes=[pltpu.VMEM((out_len, group_width), F32)],
    )(y_local, c_cols, cum_device.transpose(0, 2, 1), incoming, z_gate, norm_w[None, :])


def solution(mesh):
    in_specs = (
        P(("groups", "ctx"), "head"),
        P(None, "head", "sub", ("groups", "ctx")),
        P(("groups", "ctx", "sub"), "head"),
        P("head", ("groups", "ctx")),
        P(None, "head"),
        P("head"),
        P(None, None, "head", None),
        P(None, "head", None),
        P("head"),
        P("head"),
        P("head"),
        P("head"),
    )
    out_specs = P(("groups", "ctx", "sub"), "head")
    return jax.shard_map(
        per_device, mesh=mesh, in_specs=in_specs, out_specs=out_specs, check_vma=False
    )
```

```python
import jax
import jax.numpy as jnp
from jax import lax
from jax.experimental import pallas as pl
from jax.experimental.pallas import tpu as pltpu
from jax.sharding import PartitionSpec as P

HEADS = 128
HEAD_DIM = 64
GROUPS = 8
CONV_K = 4


HIGHEST = lax.Precision.HIGHEST
F32 = jnp.float32


def passed_along(x, axis, by):
    length = lax.axis_size(axis)
    pairs = [(i, i + by) for i in range(length) if 0 <= i + by < length]
    return lax.ppermute(x, axis, pairs)


def swapped(x, axis):
    return lax.ppermute(x, axis, [(0, 1), (1, 0)])


def conv_rows(padded, weights, bias_row):
    sequence_length = padded.shape[0] - (CONV_K - 1)
    total = jnp.zeros((sequence_length, padded.shape[1]), jnp.float32) + bias_row[None, :]
    for tap_index in range(CONV_K):
        total = total + weights[tap_index][None, :] * padded[
            tap_index : tap_index + sequence_length
        ].astype(jnp.float32)
    return jax.nn.silu(total)


def conv_cols(padded, weights, bias_block):
    sequence_length = padded.shape[-1] - (CONV_K - 1)
    total = jnp.zeros(padded.shape[:-1] + (sequence_length,), jnp.float32) + bias_block[..., None]
    for tap_index in range(CONV_K):
        total = total + weights[tap_index][..., None] * padded[
            ..., tap_index : tap_index + sequence_length
        ].astype(jnp.float32)
    return jax.nn.silu(total)


def dot(a, b):
    return jnp.dot(a, b, precision=HIGHEST, preferred_element_type=F32)


def split(a):
    high = a.astype(jnp.bfloat16)
    return high, (a - high.astype(F32)).astype(jnp.bfloat16)


def dot3(a_parts, b_parts):
    a_high, a_low = a_parts
    b_high, b_low = b_parts
    flat = lambda u, v: jnp.dot(u, v, preferred_element_type=F32)
    return flat(a_high, b_high) + (flat(a_high, b_low) + flat(a_low, b_high))


def pair_columns(cumc, pair, rows):
    left = lax.broadcasted_iota(jnp.int32, (1, 128), 1) < HEAD_DIM
    return jnp.where(
        left,
        jnp.broadcast_to(cumc[:, 2 * pair : 2 * pair + 1], (rows, 128)),
        jnp.broadcast_to(cumc[:, 2 * pair + 1 : 2 * pair + 2], (rows, 128)),
    )


def scan_kernel(xc_ref, ct_ref, b_ref, cumr_ref, cumc_ref, stp_ref, dsk_ref, z_ref, y_ref, sz_ref, e_ref):
    chunk = pl.program_id(1)
    block_len = xc_ref.shape[0]
    pairs = e_ref.shape[0]
    heads = 2 * pairs

    @pl.when(chunk == 0)
    def _():
        e_ref[...] = jnp.zeros_like(e_ref)

    ct = split(ct_ref[0])
    bm = b_ref[0]
    scores = dot3(ct, split(bm))
    rows = lax.broadcasted_iota(jnp.int32, (block_len, block_len), 0)
    cols = lax.broadcasted_iota(jnp.int32, (block_len, block_len), 1)
    causal = rows >= cols
    cumr = cumr_ref[0]
    cumc = cumc_ref[0]
    stp = stp_ref[0]
    left = lax.broadcasted_iota(jnp.int32, (1, 128), 1) < HEAD_DIM
    for pair in range(pairs):
        lanes = slice(pair * 128, (pair + 1) * 128)
        xp = xc_ref[:, lanes]
        xs = split(xp)
        s_old = e_ref[pair]
        ys = []
        us = []
        for side in range(2):
            head = 2 * pair + side
            dq = jnp.broadcast_to(cumc[:, head : head + 1], (block_len, block_len))
            ck = cumr[head : head + 1, :]
            sk = stp[head : head + 1, :]
            dec = jnp.exp(jnp.where(causal, dq - ck, -jnp.inf))
            ys.append(dot3(split(scores * dec * sk), xs))
            wk = jnp.exp(dq[block_len - 1 : block_len, :] - ck) * sk
            us.append(dot3(split(bm * wk), xs))
        cq = pair_columns(cumc, pair, block_len)
        inflow = dot3(ct, split(s_old)) * jnp.exp(cq)
        y = jnp.where(left, ys[0], ys[1]) + inflow
        z = z_ref[:, lanes].astype(F32)
        gate = z / (1.0 + jnp.exp(-z))
        sz_ref[:, lanes] = gate
        y_ref[:, lanes] = (y + xp * dsk_ref[:, lanes]) * gate
        e_ref[pair] = jnp.exp(cq[block_len - 1 : block_len, :]) * s_old + jnp.where(
            left, us[0], us[1]
        )


def end_kernel(xc_ref, b_ref, wk_ref, e_ref):
    pairs = e_ref.shape[1]
    bm = b_ref[0]
    wk = wk_ref[0]
    left = lax.broadcasted_iota(jnp.int32, (1, 128), 1) < HEAD_DIM
    for pair in range(pairs):
        xs = split(xc_ref[:, pair * 128 : (pair + 1) * 128])
        us = [
            dot3(split(bm * wk[2 * pair + side : 2 * pair + side + 1, :]), xs) for side in range(2)
        ]
        e_ref[0, pair] = jnp.where(left, us[0], us[1])


def out_kernel(y_ref, ct_ref, cumc_ref, v_ref, sz_ref, nw_ref, o_ref, g_ref):
    pairs = v_ref.shape[1]
    heads = 2 * pairs
    ct = split(ct_ref[0])
    cumc = cumc_ref[0]
    total = jnp.zeros((y_ref.shape[0], 1), F32)
    for pair in range(pairs):
        lanes = slice(pair * 128, (pair + 1) * 128)
        cq = pair_columns(cumc, pair, y_ref.shape[0])
        gated = y_ref[:, lanes] + dot3(ct, split(v_ref[0, pair])) * jnp.exp(cq) * sz_ref[:, lanes]
        g_ref[:, lanes] = gated
        total = total + jnp.sum(gated * gated, axis=-1, keepdims=True)
    mean_square = total / g_ref.shape[1]
    o_ref[...] = (g_ref[...] * lax.rsqrt(mean_square + 1e-05) * nw_ref[...]).astype(o_ref.dtype)


def per_device(
    x_raw,
    bc_raw,
    z_gate,
    dt_raw,
    conv_x_w,
    conv_x_b,
    conv_bc_w,
    conv_bc_b,
    dt_bias,
    a_log,
    d_skip,
    norm_w,
):
    tokens = x_raw.shape[0]
    heads_dev = dt_raw.shape[0]
    per_group = HEADS // GROUPS
    set_groups = heads_dev // per_group
    pairs = per_group // 2
    group_width = per_group * HEAD_DIM
    nsub = lax.axis_size("sub")
    sub_index = lax.axis_index("sub")
    own = tokens // nsub
    half = bc_raw.shape[2]
    state = half * nsub
    channels = heads_dev * HEAD_DIM
    rim_len = CONV_K - 1

    bc_tail = bc_raw[..., tokens - rim_len :]
    rims = passed_along(
        jnp.concatenate(
            [x_raw[tokens - rim_len :], bc_tail.reshape(-1, rim_len).transpose(1, 0)], 1
        ),
        "ctx",
        1,
    )
    x_rim = rims[:, :channels]
    bc_rim = rims[:, channels:].transpose(1, 0).reshape(bc_tail.shape)
    x_pad = jnp.concatenate([x_rim, x_raw], 0)
    x_own = conv_rows(
        lax.dynamic_slice_in_dim(x_pad, sub_index * own, own + rim_len, 0), conv_x_w, conv_x_b
    )
    x_other = conv_rows(
        lax.dynamic_slice_in_dim(x_pad, (1 - sub_index) * own, own + rim_len, 0),
        conv_x_w,
        conv_x_b,
    )
    bc_weights = lax.dynamic_slice_in_dim(conv_bc_w, sub_index * half, half, 3)
    bc_bias = lax.dynamic_slice_in_dim(conv_bc_b, sub_index * half, half, 2)
    bc_conv = conv_cols(jnp.concatenate([bc_rim, bc_raw], 3), bc_weights, bc_bias)
    bc_mine = lax.dynamic_slice_in_dim(bc_conv, sub_index * own, own, 3)
    bc_theirs = swapped(lax.dynamic_slice_in_dim(bc_conv, (1 - sub_index) * own, own, 3), "sub")
    bc_own = jnp.stack(
        [
            jnp.where(sub_index == 0, bc_mine, bc_theirs),
            jnp.where(sub_index == 0, bc_theirs, bc_mine),
        ],
        2,
    ).reshape(2, set_groups, state, own)
    b_rows = bc_own[0]
    c_cols = bc_own[1].transpose(0, 2, 1)

    step_sizes = jax.nn.softplus(dt_raw + dt_bias[:, None])
    log_decay = -jnp.exp(a_log)[:, None] * step_sizes
    half_totals = jnp.exp(log_decay.reshape(heads_dev, nsub, own).sum(-1))
    step_own = lax.dynamic_slice_in_dim(step_sizes, sub_index * own, own, 1)
    decay_own = lax.dynamic_slice_in_dim(log_decay, sub_index * own, own, 1)
    block_len = min(128, own)
    blocks = own // block_len
    upper = (
        lax.broadcasted_iota(jnp.int32, (block_len, block_len), 0)
        <= lax.broadcasted_iota(jnp.int32, (block_len, block_len), 1)
    ).astype(F32)
    cum_local = jnp.einsum(
        "hct,tu->hcu", decay_own.reshape(heads_dev, blocks, block_len), upper, precision=HIGHEST
    )
    block_totals = cum_local[..., -1]
    offsets = jnp.cumsum(block_totals, axis=-1) - block_totals
    cum_device = (cum_local + offsets[..., None]).reshape(set_groups, per_group, own)
    cum_rows = cum_local.reshape(set_groups, per_group, own)
    cum_cols = cum_rows.transpose(0, 2, 1)
    step_rows = step_own.reshape(set_groups, per_group, own)
    skip_row = jnp.repeat(d_skip, HEAD_DIM)[None, :]

    cum_all = jnp.einsum(
        "hjct,tu->hjcu",
        log_decay.reshape(heads_dev, nsub, blocks, block_len),
        upper,
        precision=HIGHEST,
    )
    all_totals = cum_all[..., -1]
    cum_all = (cum_all + (jnp.cumsum(all_totals, axis=-1) - all_totals)[..., None]).reshape(
        heads_dev, nsub, own
    )
    to_end = jnp.exp(cum_all[..., own - 1 :] - cum_all) * step_sizes.reshape(heads_dev, nsub, own)
    to_end = to_end.reshape(set_groups, per_group, tokens)

    def end_states(x_half, at):
        return pl.pallas_call(
            end_kernel,
            grid=(set_groups,),
            in_specs=[
                pl.BlockSpec((own, group_width), lambda g: (0, g)),
                pl.BlockSpec((1, half, own), lambda g: (g, 0, 0)),
                pl.BlockSpec((1, per_group, own), lambda g: (g, 0, 0)),
            ],
            out_specs=pl.BlockSpec((1, pairs, half, 128), lambda g: (g, 0, 0, 0)),
            out_shape=jax.ShapeDtypeStruct((set_groups, pairs, half, 128), F32),
        )(
            x_half,
            lax.dynamic_slice_in_dim(bc_conv[0], at * own, own, 2),
            lax.dynamic_slice_in_dim(to_end, at * own, own, 2),
        )

    own_end = end_states(x_own, sub_index)
    other_end = end_states(x_other, 1 - sub_index)

    def pair_layout(values):
        return jnp.repeat(values.reshape(set_groups, pairs, 2), HEAD_DIM, axis=-1)[:, :, None, :]

    decay_first = pair_layout(half_totals[:, 0])
    decay_second = pair_layout(half_totals[:, 1])
    first_end = jnp.where(sub_index == 0, own_end, other_end)
    second_end = jnp.where(sub_index == 0, other_end, own_end)
    chip_end = decay_second * first_end + second_end
    chip_decay = decay_first * decay_second
    ctx_index = lax.axis_index("ctx")
    ctx_size = lax.axis_size("ctx")
    scan_inputs = (x_own, c_cols, b_rows, cum_rows, cum_cols, step_rows, skip_row, z_gate)

    def scan_group(group, inputs, target):
        count = len(inputs)
        extra = {} if target is None else {"input_output_aliases": {count: 0, count + 1: 1}}
        tile = pl.BlockSpec((block_len, group_width), lambda g, c: (c, group))
        in_specs = [
            tile,
            pl.BlockSpec((1, block_len, state), lambda g, c: (group, c, 0)),
            pl.BlockSpec((1, state, block_len), lambda g, c: (group, 0, c)),
            pl.BlockSpec((1, per_group, block_len), lambda g, c: (group, 0, c)),
            pl.BlockSpec((1, block_len, per_group), lambda g, c: (group, c, 0)),
            pl.BlockSpec((1, per_group, block_len), lambda g, c: (group, 0, c)),
            pl.BlockSpec((1, group_width), lambda g, c: (0, group)),
            tile,
        ]
        operands = tuple(inputs)
        kernel = scan_kernel
        if target is not None:
            in_specs = in_specs + [pl.BlockSpec(memory_space=pl.ANY)] * 2
            operands = operands + tuple(target)
            kernel = lambda *refs: scan_kernel(*refs[:count], *refs[count + 2 :])
        return pl.pallas_call(
            kernel,
            grid=(1, blocks),
            in_specs=in_specs,
            out_specs=[tile, tile],
            out_shape=[jax.ShapeDtypeStruct((own, channels), F32)] * 2,
            scratch_shapes=[pltpu.VMEM((pairs, state, 128), F32)],
            **extra,
        )(*operands)

    pieces = 2 if (set_groups * pairs) % 2 == 0 else 1
    rounds = ctx_size + pieces - 2
    piece_shape = (pieces, set_groups * pairs // pieces, half, 128)
    end_pieces = chip_end.reshape(piece_shape)
    decay_pieces = jnp.broadcast_to(chip_decay, chip_end.shape).reshape(piece_shape)
    received = jnp.zeros(piece_shape, F32)
    y_local = None
    placed = [min(group, max(rounds, 1) - 1) for group in range(set_groups)]
    for step_index in range(max(rounds, 1)):
        send_at = jnp.clip(step_index - ctx_index, 0, pieces - 1)
        outgoing = lax.dynamic_index_in_dim(
            end_pieces, send_at, 0, keepdims=False
        ) + lax.dynamic_index_in_dim(decay_pieces, send_at, 0, keepdims=False) * (
            lax.dynamic_index_in_dim(received, send_at, 0, keepdims=False)
        )
        held = scan_inputs
        if any(p == step_index for p in placed):
            outgoing, held = lax.optimization_barrier((outgoing, scan_inputs))
        if rounds > 0:
            arrived = passed_along(outgoing, "ctx", 1)
        for group in range(set_groups):
            if placed[group] == step_index:
                y_local = scan_group(group, held, y_local)
        if rounds == 0:
            break
        if any(p == step_index for p in placed):
            arrived, y_local = lax.optimization_barrier((arrived, y_local))
        recv_at = step_index - ctx_index + 1
        valid = (recv_at >= 0) & (recv_at < pieces) & (ctx_index > 0)
        updated = lax.dynamic_update_index_in_dim(
            received, arrived, jnp.clip(recv_at, 0, pieces - 1), 0
        )
        received = jnp.where(valid, updated, received)
    carried = received.reshape(chip_end.shape)
    into_second = decay_first * carried + first_end
    keep = jnp.where(sub_index == 0, carried, into_second)
    got = swapped(jnp.where(sub_index == 0, into_second, carried), "sub")
    low = jnp.where(sub_index == 0, keep, got)
    high = jnp.where(sub_index == 0, got, keep)
    incoming = jnp.stack([low, high], 2).reshape(set_groups, pairs, state, 128)

    out_len = min(256, own)
    return pl.pallas_call(
        out_kernel,
        grid=(set_groups, own // out_len),
        in_specs=[
            pl.BlockSpec((out_len, group_width), lambda g, c: (c, g)),
            pl.BlockSpec((1, out_len, state), lambda g, c: (g, c, 0)),
            pl.BlockSpec((1, out_len, per_group), lambda g, c: (g, c, 0)),
            pl.BlockSpec((1, pairs, state, 128), lambda g, c: (g, 0, 0, 0)),
            pl.BlockSpec((out_len, group_width), lambda g, c: (c, g)),
            pl.BlockSpec((1, group_width), lambda g, c: (0, g)),
        ],
        out_specs=pl.BlockSpec((out_len, group_width), lambda g, c: (c, g)),
        out_shape=jax.ShapeDtypeStruct((own, channels), jnp.bfloat16),
        scratch_shapes=[pltpu.VMEM((out_len, group_width), F32)],
    )(y_local[0], c_cols, cum_device.transpose(0, 2, 1), incoming, y_local[1], norm_w[None, :])


def solution(mesh):
    in_specs = (
        P(("groups", "ctx"), "head"),
        P(None, "head", "sub", ("groups", "ctx")),
        P(("groups", "ctx", "sub"), "head"),
        P("head", ("groups", "ctx")),
        P(None, "head"),
        P("head"),
        P(None, None, "head", None),
        P(None, "head", None),
        P("head"),
        P("head"),
        P("head"),
        P("head"),
    )
    out_specs = P(("groups", "ctx", "sub"), "head")
    return jax.shard_map(
        per_device, mesh=mesh, in_specs=in_specs, out_specs=out_specs, check_vma=False
    )
```

```python
import jax
import jax.numpy as jnp
from jax import lax
from jax.experimental import pallas as pl
from jax.experimental.pallas import tpu as pltpu
from jax.sharding import PartitionSpec as P

HEADS = 128
HEAD_DIM = 64
GROUPS = 8
CONV_K = 4


HIGHEST = lax.Precision.HIGHEST
F32 = jnp.float32


def passed_along(x, axis, by):
    length = lax.axis_size(axis)
    pairs = [(i, i + by) for i in range(length) if 0 <= i + by < length]
    return lax.ppermute(x, axis, pairs)


def swapped(x, axis):
    return lax.ppermute(x, axis, [(0, 1), (1, 0)])


def conv_rows(padded, weights, bias_row):
    sequence_length = padded.shape[0] - (CONV_K - 1)
    total = jnp.zeros((sequence_length, padded.shape[1]), jnp.float32) + bias_row[None, :]
    for tap_index in range(CONV_K):
        total = total + weights[tap_index][None, :] * padded[
            tap_index : tap_index + sequence_length
        ].astype(jnp.float32)
    return jax.nn.silu(total)


def conv_cols(padded, weights, bias_block):
    sequence_length = padded.shape[-1] - (CONV_K - 1)
    total = jnp.zeros(padded.shape[:-1] + (sequence_length,), jnp.float32) + bias_block[..., None]
    for tap_index in range(CONV_K):
        total = total + weights[tap_index][..., None] * padded[
            ..., tap_index : tap_index + sequence_length
        ].astype(jnp.float32)
    return jax.nn.silu(total)


def dot(a, b):
    return jnp.dot(a, b, precision=HIGHEST, preferred_element_type=F32)


def split(a):
    high = a.astype(jnp.bfloat16)
    return high, (a - high.astype(F32)).astype(jnp.bfloat16)


def dot3(a_parts, b_parts):
    a_high, a_low = a_parts
    b_high, b_low = b_parts
    flat = lambda u, v: jnp.dot(u, v, preferred_element_type=F32)
    return flat(a_high, b_high) + (flat(a_high, b_low) + flat(a_low, b_high))


def pair_columns(cumc, pair, rows):
    left = lax.broadcasted_iota(jnp.int32, (1, 128), 1) < HEAD_DIM
    return jnp.where(
        left,
        jnp.broadcast_to(cumc[:, 2 * pair : 2 * pair + 1], (rows, 128)),
        jnp.broadcast_to(cumc[:, 2 * pair + 1 : 2 * pair + 2], (rows, 128)),
    )


def scan_kernel(xc_ref, ct_ref, b_ref, cumr_ref, cumc_ref, stp_ref, dsk_ref, z_ref, y_ref, sz_ref, e_ref):
    chunk = pl.program_id(1)
    block_len = xc_ref.shape[0]
    pairs = e_ref.shape[0]
    heads = 2 * pairs

    @pl.when(chunk == 0)
    def _():
        e_ref[...] = jnp.zeros_like(e_ref)

    ct = split(ct_ref[0])
    bm = b_ref[0]
    scores = dot3(ct, split(bm))
    rows = lax.broadcasted_iota(jnp.int32, (block_len, block_len), 0)
    cols = lax.broadcasted_iota(jnp.int32, (block_len, block_len), 1)
    causal = rows >= cols
    cumr = cumr_ref[0]
    cumc = cumc_ref[0]
    stp = stp_ref[0]
    left = lax.broadcasted_iota(jnp.int32, (1, 128), 1) < HEAD_DIM
    for pair in range(pairs):
        lanes = slice(pair * 128, (pair + 1) * 128)
        xp = xc_ref[:, lanes]
        xs = split(xp)
        s_old = e_ref[pair]
        ys = []
        us = []
        for side in range(2):
            head = 2 * pair + side
            dq = jnp.broadcast_to(cumc[:, head : head + 1], (block_len, block_len))
            ck = cumr[head : head + 1, :]
            sk = stp[head : head + 1, :]
            dec = jnp.exp(jnp.where(causal, dq - ck, -jnp.inf))
            ys.append(dot3(split(scores * dec * sk), xs))
            wk = jnp.exp(dq[block_len - 1 : block_len, :] - ck) * sk
            us.append(dot3(split(bm * wk), xs))
        cq = pair_columns(cumc, pair, block_len)
        inflow = dot3(ct, split(s_old)) * jnp.exp(cq)
        y = jnp.where(left, ys[0], ys[1]) + inflow
        z = z_ref[:, lanes].astype(F32)
        gate = z / (1.0 + jnp.exp(-z))
        sz_ref[:, lanes] = gate
        y_ref[:, lanes] = (y + xp * dsk_ref[:, lanes]) * gate
        e_ref[pair] = jnp.exp(cq[block_len - 1 : block_len, :]) * s_old + jnp.where(
            left, us[0], us[1]
        )


def end_kernel(xc_ref, b_ref, wk_ref, e_ref):
    pairs = e_ref.shape[1]
    bm = b_ref[0]
    wk = wk_ref[0]
    left = lax.broadcasted_iota(jnp.int32, (1, 128), 1) < HEAD_DIM
    for pair in range(pairs):
        xs = split(xc_ref[:, pair * 128 : (pair + 1) * 128])
        us = [
            dot3(split(bm * wk[2 * pair + side : 2 * pair + side + 1, :]), xs) for side in range(2)
        ]
        e_ref[0, pair] = jnp.where(left, us[0], us[1])


def out_kernel(y_ref, ct_ref, cumc_ref, v_ref, sz_ref, nw_ref, o_ref, g_ref):
    pairs = v_ref.shape[1]
    heads = 2 * pairs
    ct = split(ct_ref[0])
    cumc = cumc_ref[0]
    total = jnp.zeros((y_ref.shape[0], 1), F32)
    for pair in range(pairs):
        lanes = slice(pair * 128, (pair + 1) * 128)
        cq = pair_columns(cumc, pair, y_ref.shape[0])
        gated = y_ref[:, lanes] + dot3(ct, split(v_ref[0, pair])) * jnp.exp(cq) * sz_ref[:, lanes]
        g_ref[:, lanes] = gated
        total = total + jnp.sum(gated * gated, axis=-1, keepdims=True)
    mean_square = total / g_ref.shape[1]
    o_ref[...] = (g_ref[...] * lax.rsqrt(mean_square + 1e-05) * nw_ref[...]).astype(o_ref.dtype)


def per_device(
    x_raw,
    bc_raw,
    z_gate,
    dt_raw,
    conv_x_w,
    conv_x_b,
    conv_bc_w,
    conv_bc_b,
    dt_bias,
    a_log,
    d_skip,
    norm_w,
):
    tokens = x_raw.shape[0]
    heads_dev = dt_raw.shape[0]
    per_group = HEADS // GROUPS
    set_groups = heads_dev // per_group
    pairs = per_group // 2
    group_width = per_group * HEAD_DIM
    nsub = lax.axis_size("sub")
    sub_index = lax.axis_index("sub")
    own = tokens // nsub
    half = bc_raw.shape[2]
    state = half * nsub
    channels = heads_dev * HEAD_DIM
    rim_len = CONV_K - 1

    bc_tail = bc_raw[..., tokens - rim_len :]
    rims = passed_along(
        jnp.concatenate(
            [x_raw[tokens - rim_len :], bc_tail.reshape(-1, rim_len).transpose(1, 0)], 1
        ),
        "ctx",
        1,
    )
    x_rim = rims[:, :channels]
    bc_rim = rims[:, channels:].transpose(1, 0).reshape(bc_tail.shape)
    x_pad = jnp.concatenate([jnp.zeros_like(x_rim), x_raw], 0)
    x_start = conv_rows(jnp.concatenate([x_rim, x_raw[:rim_len]], 0), conv_x_w, conv_x_b)

    def x_window(at):
        body = conv_rows(
            lax.dynamic_slice_in_dim(x_pad, at * own, own + rim_len, 0), conv_x_w, conv_x_b
        )
        head_rows = jnp.where(at == 0, x_start, body[:rim_len])
        return lax.dynamic_update_slice_in_dim(body, head_rows, 0, 0)

    x_own = x_window(sub_index)
    x_other = x_window(1 - sub_index)
    bc_weights = lax.dynamic_slice_in_dim(conv_bc_w, sub_index * half, half, 3)
    bc_bias = lax.dynamic_slice_in_dim(conv_bc_b, sub_index * half, half, 2)
    bc_body = conv_cols(
        jnp.concatenate([jnp.zeros_like(bc_rim), bc_raw], 3), bc_weights, bc_bias
    )
    bc_start = conv_cols(
        jnp.concatenate([bc_rim, bc_raw[..., :rim_len]], 3), bc_weights, bc_bias
    )
    bc_conv = lax.dynamic_update_slice_in_dim(bc_body, bc_start, 0, 3)
    bc_mine = lax.dynamic_slice_in_dim(bc_conv, sub_index * own, own, 3)
    bc_theirs = swapped(lax.dynamic_slice_in_dim(bc_conv, (1 - sub_index) * own, own, 3), "sub")
    bc_own = jnp.stack(
        [
            jnp.where(sub_index == 0, bc_mine, bc_theirs),
            jnp.where(sub_index == 0, bc_theirs, bc_mine),
        ],
        2,
    ).reshape(2, set_groups, state, own)
    b_rows = bc_own[0]
    c_cols = bc_own[1].transpose(0, 2, 1)

    step_sizes = jax.nn.softplus(dt_raw + dt_bias[:, None])
    log_decay = -jnp.exp(a_log)[:, None] * step_sizes
    half_totals = jnp.exp(log_decay.reshape(heads_dev, nsub, own).sum(-1))
    step_own = lax.dynamic_slice_in_dim(step_sizes, sub_index * own, own, 1)
    decay_own = lax.dynamic_slice_in_dim(log_decay, sub_index * own, own, 1)
    block_len = min(128, own)
    blocks = own // block_len
    upper = (
        lax.broadcasted_iota(jnp.int32, (block_len, block_len), 0)
        <= lax.broadcasted_iota(jnp.int32, (block_len, block_len), 1)
    ).astype(F32)
    cum_local = jnp.einsum(
        "hct,tu->hcu", decay_own.reshape(heads_dev, blocks, block_len), upper, precision=HIGHEST
    )
    block_totals = cum_local[..., -1]
    offsets = jnp.cumsum(block_totals, axis=-1) - block_totals
    cum_device = (cum_local + offsets[..., None]).reshape(set_groups, per_group, own)
    cum_rows = cum_local.reshape(set_groups, per_group, own)
    cum_cols = cum_rows.transpose(0, 2, 1)
    step_rows = step_own.reshape(set_groups, per_group, own)
    skip_row = jnp.repeat(d_skip, HEAD_DIM)[None, :]

    cum_all = jnp.einsum(
        "hjct,tu->hjcu",
        log_decay.reshape(heads_dev, nsub, blocks, block_len),
        upper,
        precision=HIGHEST,
    )
    all_totals = cum_all[..., -1]
    cum_all = (cum_all + (jnp.cumsum(all_totals, axis=-1) - all_totals)[..., None]).reshape(
        heads_dev, nsub, own
    )
    to_end = jnp.exp(cum_all[..., own - 1 :] - cum_all) * step_sizes.reshape(heads_dev, nsub, own)
    to_end = to_end.reshape(set_groups, per_group, tokens)

    def end_states(x_half, at):
        return pl.pallas_call(
            end_kernel,
            grid=(set_groups,),
            in_specs=[
                pl.BlockSpec((own, group_width), lambda g: (0, g)),
                pl.BlockSpec((1, half, own), lambda g: (g, 0, 0)),
                pl.BlockSpec((1, per_group, own), lambda g: (g, 0, 0)),
            ],
            out_specs=pl.BlockSpec((1, pairs, half, 128), lambda g: (g, 0, 0, 0)),
            out_shape=jax.ShapeDtypeStruct((set_groups, pairs, half, 128), F32),
        )(
            x_half,
            lax.dynamic_slice_in_dim(bc_conv[0], at * own, own, 2),
            lax.dynamic_slice_in_dim(to_end, at * own, own, 2),
        )

    own_end = end_states(x_own, sub_index)
    other_end = end_states(x_other, 1 - sub_index)

    def pair_layout(values):
        return jnp.repeat(values.reshape(set_groups, pairs, 2), HEAD_DIM, axis=-1)[:, :, None, :]

    decay_first = pair_layout(half_totals[:, 0])
    decay_second = pair_layout(half_totals[:, 1])
    first_end = jnp.where(sub_index == 0, own_end, other_end)
    second_end = jnp.where(sub_index == 0, other_end, own_end)
    chip_end = decay_second * first_end + second_end
    chip_decay = decay_first * decay_second
    ctx_index = lax.axis_index("ctx")
    ctx_size = lax.axis_size("ctx")
    scan_inputs = (x_own, c_cols, b_rows, cum_rows, cum_cols, step_rows, skip_row, z_gate)

    def scan_group(group, inputs, target):
        count = len(inputs)
        extra = {} if target is None else {"input_output_aliases": {count: 0, count + 1: 1}}
        tile = pl.BlockSpec((block_len, group_width), lambda g, c: (c, group))
        in_specs = [
            tile,
            pl.BlockSpec((1, block_len, state), lambda g, c: (group, c, 0)),
            pl.BlockSpec((1, state, block_len), lambda g, c: (group, 0, c)),
            pl.BlockSpec((1, per_group, block_len), lambda g, c: (group, 0, c)),
            pl.BlockSpec((1, block_len, per_group), lambda g, c: (group, c, 0)),
            pl.BlockSpec((1, per_group, block_len), lambda g, c: (group, 0, c)),
            pl.BlockSpec((1, group_width), lambda g, c: (0, group)),
            tile,
        ]
        operands = tuple(inputs)
        kernel = scan_kernel
        if target is not None:
            in_specs = in_specs + [pl.BlockSpec(memory_space=pl.ANY)] * 2
            operands = operands + tuple(target)
            kernel = lambda *refs: scan_kernel(*refs[:count], *refs[count + 2 :])
        return pl.pallas_call(
            kernel,
            grid=(1, blocks),
            in_specs=in_specs,
            out_specs=[tile, tile],
            out_shape=[jax.ShapeDtypeStruct((own, channels), F32)] * 2,
            scratch_shapes=[pltpu.VMEM((pairs, state, 128), F32)],
            **extra,
        )(*operands)

    pieces = 2 if (set_groups * pairs) % 2 == 0 else 1
    rounds = ctx_size + pieces - 2
    piece_shape = (pieces, set_groups * pairs // pieces, half, 128)
    end_pieces = chip_end.reshape(piece_shape)
    decay_pieces = jnp.broadcast_to(chip_decay, chip_end.shape).reshape(piece_shape)
    received = jnp.zeros(piece_shape, F32)
    y_local = None
    placed = [min(group, max(rounds, 1) - 1) for group in range(set_groups)]
    for step_index in range(max(rounds, 1)):
        send_at = jnp.clip(step_index - ctx_index, 0, pieces - 1)
        outgoing = lax.dynamic_index_in_dim(
            end_pieces, send_at, 0, keepdims=False
        ) + lax.dynamic_index_in_dim(decay_pieces, send_at, 0, keepdims=False) * (
            lax.dynamic_index_in_dim(received, send_at, 0, keepdims=False)
        )
        held = scan_inputs
        if any(p == step_index for p in placed):
            outgoing, held = lax.optimization_barrier((outgoing, scan_inputs))
        if rounds > 0:
            arrived = passed_along(outgoing, "ctx", 1)
        for group in range(set_groups):
            if placed[group] == step_index:
                y_local = scan_group(group, held, y_local)
        if rounds == 0:
            break
        if any(p == step_index for p in placed):
            arrived, y_local = lax.optimization_barrier((arrived, y_local))
        recv_at = step_index - ctx_index + 1
        valid = (recv_at >= 0) & (recv_at < pieces) & (ctx_index > 0)
        updated = lax.dynamic_update_index_in_dim(
            received, arrived, jnp.clip(recv_at, 0, pieces - 1), 0
        )
        received = jnp.where(valid, updated, received)
    carried = received.reshape(chip_end.shape)
    into_second = decay_first * carried + first_end
    keep = jnp.where(sub_index == 0, carried, into_second)
    got = swapped(jnp.where(sub_index == 0, into_second, carried), "sub")
    low = jnp.where(sub_index == 0, keep, got)
    high = jnp.where(sub_index == 0, got, keep)
    incoming = jnp.stack([low, high], 2).reshape(set_groups, pairs, state, 128)

    out_len = min(256, own)
    return pl.pallas_call(
        out_kernel,
        grid=(set_groups, own // out_len),
        in_specs=[
            pl.BlockSpec((out_len, group_width), lambda g, c: (c, g)),
            pl.BlockSpec((1, out_len, state), lambda g, c: (g, c, 0)),
            pl.BlockSpec((1, out_len, per_group), lambda g, c: (g, c, 0)),
            pl.BlockSpec((1, pairs, state, 128), lambda g, c: (g, 0, 0, 0)),
            pl.BlockSpec((out_len, group_width), lambda g, c: (c, g)),
            pl.BlockSpec((1, group_width), lambda g, c: (0, g)),
        ],
        out_specs=pl.BlockSpec((out_len, group_width), lambda g, c: (c, g)),
        out_shape=jax.ShapeDtypeStruct((own, channels), jnp.bfloat16),
        scratch_shapes=[pltpu.VMEM((out_len, group_width), F32)],
    )(y_local[0], c_cols, cum_device.transpose(0, 2, 1), incoming, y_local[1], norm_w[None, :])


def solution(mesh):
    in_specs = (
        P(("groups", "ctx"), "head"),
        P(None, "head", "sub", ("groups", "ctx")),
        P(("groups", "ctx", "sub"), "head"),
        P("head", ("groups", "ctx")),
        P(None, "head"),
        P("head"),
        P(None, None, "head", None),
        P(None, "head", None),
        P("head"),
        P("head"),
        P("head"),
        P("head"),
    )
    out_specs = P(("groups", "ctx", "sub"), "head")
    return jax.shard_map(
        per_device, mesh=mesh, in_specs=in_specs, out_specs=out_specs, check_vma=False
    )
```

```python
import jax
import jax.numpy as jnp
from jax import lax
from jax.experimental import pallas as pl
from jax.experimental.pallas import tpu as pltpu
from jax.sharding import PartitionSpec as P

HEADS = 128
HEAD_DIM = 64
GROUPS = 8
CONV_K = 4


HIGHEST = lax.Precision.HIGHEST
F32 = jnp.float32


def passed_along(x, axis, by):
    length = lax.axis_size(axis)
    pairs = [(i, i + by) for i in range(length) if 0 <= i + by < length]
    return lax.ppermute(x, axis, pairs)


def swapped(x, axis):
    return lax.ppermute(x, axis, [(0, 1), (1, 0)])


def conv_rows(padded, weights, bias_row):
    sequence_length = padded.shape[0] - (CONV_K - 1)
    total = jnp.zeros((sequence_length, padded.shape[1]), jnp.float32) + bias_row[None, :]
    for tap_index in range(CONV_K):
        total = total + weights[tap_index][None, :] * padded[
            tap_index : tap_index + sequence_length
        ].astype(jnp.float32)
    return jax.nn.silu(total)


def conv_cols(padded, weights, bias_block):
    sequence_length = padded.shape[-1] - (CONV_K - 1)
    total = jnp.zeros(padded.shape[:-1] + (sequence_length,), jnp.float32) + bias_block[..., None]
    for tap_index in range(CONV_K):
        total = total + weights[tap_index][..., None] * padded[
            ..., tap_index : tap_index + sequence_length
        ].astype(jnp.float32)
    return jax.nn.silu(total)


def dot(a, b):
    return jnp.dot(a, b, precision=HIGHEST, preferred_element_type=F32)


def split(a):
    high = a.astype(jnp.bfloat16)
    return high, (a - high.astype(F32)).astype(jnp.bfloat16)


def dot3(a_parts, b_parts):
    a_high, a_low = a_parts
    b_high, b_low = b_parts
    flat = lambda u, v: jnp.dot(u, v, preferred_element_type=F32)
    return flat(a_high, b_high) + (flat(a_high, b_low) + flat(a_low, b_high))


def pair_columns(cumc, pair, rows):
    left = lax.broadcasted_iota(jnp.int32, (1, 128), 1) < HEAD_DIM
    return jnp.where(
        left,
        jnp.broadcast_to(cumc[:, 2 * pair : 2 * pair + 1], (rows, 128)),
        jnp.broadcast_to(cumc[:, 2 * pair + 1 : 2 * pair + 2], (rows, 128)),
    )


def scan_kernel(xc_ref, ct_ref, b_ref, cumr_ref, cumc_ref, stp_ref, dsk_ref, z_ref, y_ref, sz_ref, e_ref):
    chunk = pl.program_id(1)
    block_len = xc_ref.shape[0]
    pairs = e_ref.shape[0]
    heads = 2 * pairs

    @pl.when(chunk == 0)
    def _():
        e_ref[...] = jnp.zeros_like(e_ref)

    ct = split(ct_ref[0])
    bm = b_ref[0]
    scores = dot3(ct, split(bm))
    rows = lax.broadcasted_iota(jnp.int32, (block_len, block_len), 0)
    cols = lax.broadcasted_iota(jnp.int32, (block_len, block_len), 1)
    causal = rows >= cols
    cumr = cumr_ref[0]
    cumc = cumc_ref[0]
    stp = stp_ref[0]
    left = lax.broadcasted_iota(jnp.int32, (1, 128), 1) < HEAD_DIM
    for pair in range(pairs):
        lanes = slice(pair * 128, (pair + 1) * 128)
        xp = xc_ref[:, lanes]
        xs = split(xp)
        s_old = e_ref[pair]
        ys = []
        us = []
        for side in range(2):
            head = 2 * pair + side
            dq = jnp.broadcast_to(cumc[:, head : head + 1], (block_len, block_len))
            ck = cumr[head : head + 1, :]
            sk = stp[head : head + 1, :]
            dec = jnp.exp(jnp.where(causal, dq - ck, -jnp.inf))
            ys.append(dot3(split(scores * dec * sk), xs))
            wk = jnp.exp(dq[block_len - 1 : block_len, :] - ck) * sk
            us.append(dot3(split(bm * wk), xs))
        cq = pair_columns(cumc, pair, block_len)
        inflow = dot3(ct, split(s_old)) * jnp.exp(cq)
        y = jnp.where(left, ys[0], ys[1]) + inflow
        z = z_ref[:, lanes].astype(F32)
        gate = z / (1.0 + jnp.exp(-z))
        sz_ref[:, lanes] = gate
        y_ref[:, lanes] = (y + xp * dsk_ref[:, lanes]) * gate
        e_ref[pair] = jnp.exp(cq[block_len - 1 : block_len, :]) * s_old + jnp.where(
            left, us[0], us[1]
        )


def end_kernel(xc_ref, b_ref, wk_ref, e_ref):
    pairs = e_ref.shape[1]
    bm = b_ref[0]
    wk = wk_ref[0]
    left = lax.broadcasted_iota(jnp.int32, (1, 128), 1) < HEAD_DIM
    for pair in range(pairs):
        xs = split(xc_ref[:, pair * 128 : (pair + 1) * 128])
        us = [
            dot3(split(bm * wk[2 * pair + side : 2 * pair + side + 1, :]), xs) for side in range(2)
        ]
        e_ref[0, pair] = jnp.where(left, us[0], us[1])


def out_kernel(y_ref, ct_ref, cumc_ref, v_ref, sz_ref, nw_ref, o_ref, g_ref):
    pairs = v_ref.shape[1]
    heads = 2 * pairs
    ct = split(ct_ref[0])
    cumc = cumc_ref[0]
    total = jnp.zeros((y_ref.shape[0], 128), F32)
    for pair in range(pairs):
        lanes = slice(pair * 128, (pair + 1) * 128)
        cq = pair_columns(cumc, pair, y_ref.shape[0])
        gated = y_ref[:, lanes] + dot3(ct, split(v_ref[0, pair])) * jnp.exp(cq) * sz_ref[:, lanes]
        g_ref[:, lanes] = gated
        total = total + gated * gated
    mean_square = jnp.sum(total, axis=-1, keepdims=True) / g_ref.shape[1]
    o_ref[...] = (g_ref[...] * lax.rsqrt(mean_square + 1e-05) * nw_ref[...]).astype(o_ref.dtype)


def per_device(
    x_raw,
    bc_raw,
    z_gate,
    dt_raw,
    conv_x_w,
    conv_x_b,
    conv_bc_w,
    conv_bc_b,
    dt_bias,
    a_log,
    d_skip,
    norm_w,
):
    tokens = x_raw.shape[0]
    heads_dev = dt_raw.shape[0]
    per_group = HEADS // GROUPS
    set_groups = heads_dev // per_group
    pairs = per_group // 2
    group_width = per_group * HEAD_DIM
    nsub = lax.axis_size("sub")
    sub_index = lax.axis_index("sub")
    own = tokens // nsub
    half = bc_raw.shape[2]
    state = half * nsub
    channels = heads_dev * HEAD_DIM
    rim_len = CONV_K - 1

    bc_tail = bc_raw[..., tokens - rim_len :]
    rims = passed_along(
        jnp.concatenate(
            [x_raw[tokens - rim_len :], bc_tail.reshape(-1, rim_len).transpose(1, 0)], 1
        ),
        "ctx",
        1,
    )
    x_rim = rims[:, :channels]
    bc_rim = rims[:, channels:].transpose(1, 0).reshape(bc_tail.shape)
    x_pad = jnp.concatenate([x_rim, x_raw], 0)
    windows = lax.optimization_barrier(
        tuple(
            lax.dynamic_slice_in_dim(x_pad, at * own, own + rim_len, 0).astype(F32)
            for at in (sub_index, 1 - sub_index)
        )
    )
    x_own, x_other = (conv_rows(window, conv_x_w, conv_x_b) for window in windows)
    bc_weights = lax.dynamic_slice_in_dim(conv_bc_w, sub_index * half, half, 3)
    bc_bias = lax.dynamic_slice_in_dim(conv_bc_b, sub_index * half, half, 2)
    bc_conv = conv_cols(jnp.concatenate([bc_rim, bc_raw], 3), bc_weights, bc_bias)
    bc_mine = lax.dynamic_slice_in_dim(bc_conv, sub_index * own, own, 3)
    bc_theirs = swapped(lax.dynamic_slice_in_dim(bc_conv, (1 - sub_index) * own, own, 3), "sub")
    bc_own = jnp.stack(
        [
            jnp.where(sub_index == 0, bc_mine, bc_theirs),
            jnp.where(sub_index == 0, bc_theirs, bc_mine),
        ],
        2,
    ).reshape(2, set_groups, state, own)
    b_rows = bc_own[0]
    c_cols = bc_own[1].transpose(0, 2, 1)

    step_sizes = jax.nn.softplus(dt_raw + dt_bias[:, None])
    log_decay = -jnp.exp(a_log)[:, None] * step_sizes
    half_totals = jnp.exp(log_decay.reshape(heads_dev, nsub, own).sum(-1))
    step_own = lax.dynamic_slice_in_dim(step_sizes, sub_index * own, own, 1)
    decay_own = lax.dynamic_slice_in_dim(log_decay, sub_index * own, own, 1)
    block_len = min(128, own)
    blocks = own // block_len
    upper = (
        lax.broadcasted_iota(jnp.int32, (block_len, block_len), 0)
        <= lax.broadcasted_iota(jnp.int32, (block_len, block_len), 1)
    ).astype(F32)
    cum_local = jnp.einsum(
        "hct,tu->hcu", decay_own.reshape(heads_dev, blocks, block_len), upper, precision=HIGHEST
    )
    block_totals = cum_local[..., -1]
    offsets = jnp.cumsum(block_totals, axis=-1) - block_totals
    cum_device = (cum_local + offsets[..., None]).reshape(set_groups, per_group, own)
    cum_rows = cum_local.reshape(set_groups, per_group, own)
    cum_cols = cum_rows.transpose(0, 2, 1)
    step_rows = step_own.reshape(set_groups, per_group, own)
    skip_row = jnp.repeat(d_skip, HEAD_DIM)[None, :]

    cum_all = jnp.einsum(
        "hjct,tu->hjcu",
        log_decay.reshape(heads_dev, nsub, blocks, block_len),
        upper,
        precision=HIGHEST,
    )
    all_totals = cum_all[..., -1]
    cum_all = (cum_all + (jnp.cumsum(all_totals, axis=-1) - all_totals)[..., None]).reshape(
        heads_dev, nsub, own
    )
    to_end = jnp.exp(cum_all[..., own - 1 :] - cum_all) * step_sizes.reshape(heads_dev, nsub, own)
    to_end = to_end.reshape(set_groups, per_group, tokens)

    def end_states(x_half, at):
        return pl.pallas_call(
            end_kernel,
            grid=(set_groups,),
            in_specs=[
                pl.BlockSpec((own, group_width), lambda g: (0, g)),
                pl.BlockSpec((1, half, own), lambda g: (g, 0, 0)),
                pl.BlockSpec((1, per_group, own), lambda g: (g, 0, 0)),
            ],
            out_specs=pl.BlockSpec((1, pairs, half, 128), lambda g: (g, 0, 0, 0)),
            out_shape=jax.ShapeDtypeStruct((set_groups, pairs, half, 128), F32),
        )(
            x_half,
            lax.dynamic_slice_in_dim(bc_conv[0], at * own, own, 2),
            lax.dynamic_slice_in_dim(to_end, at * own, own, 2),
        )

    own_end = end_states(x_own, sub_index)
    other_end = end_states(x_other, 1 - sub_index)

    def pair_layout(values):
        return jnp.repeat(values.reshape(set_groups, pairs, 2), HEAD_DIM, axis=-1)[:, :, None, :]

    decay_first = pair_layout(half_totals[:, 0])
    decay_second = pair_layout(half_totals[:, 1])
    first_end = jnp.where(sub_index == 0, own_end, other_end)
    second_end = jnp.where(sub_index == 0, other_end, own_end)
    chip_end = decay_second * first_end + second_end
    chip_decay = decay_first * decay_second
    ctx_index = lax.axis_index("ctx")
    ctx_size = lax.axis_size("ctx")
    scan_inputs = (x_own, c_cols, b_rows, cum_rows, cum_cols, step_rows, skip_row, z_gate)

    def scan_group(group, inputs, target):
        count = len(inputs)
        extra = {} if target is None else {"input_output_aliases": {count: 0, count + 1: 1}}
        tile = pl.BlockSpec((block_len, group_width), lambda g, c: (c, group))
        in_specs = [
            tile,
            pl.BlockSpec((1, block_len, state), lambda g, c: (group, c, 0)),
            pl.BlockSpec((1, state, block_len), lambda g, c: (group, 0, c)),
            pl.BlockSpec((1, per_group, block_len), lambda g, c: (group, 0, c)),
            pl.BlockSpec((1, block_len, per_group), lambda g, c: (group, c, 0)),
            pl.BlockSpec((1, per_group, block_len), lambda g, c: (group, 0, c)),
            pl.BlockSpec((1, group_width), lambda g, c: (0, group)),
            tile,
        ]
        operands = tuple(inputs)
        kernel = scan_kernel
        if target is not None:
            in_specs = in_specs + [pl.BlockSpec(memory_space=pl.ANY)] * 2
            operands = operands + tuple(target)
            kernel = lambda *refs: scan_kernel(*refs[:count], *refs[count + 2 :])
        return pl.pallas_call(
            kernel,
            grid=(1, blocks),
            in_specs=in_specs,
            out_specs=[tile, tile],
            out_shape=[jax.ShapeDtypeStruct((own, channels), F32)] * 2,
            scratch_shapes=[pltpu.VMEM((pairs, state, 128), F32)],
            **extra,
        )(*operands)

    pieces = 2 if (set_groups * pairs) % 2 == 0 else 1
    rounds = ctx_size + pieces - 2
    piece_shape = (pieces, set_groups * pairs // pieces, half, 128)
    end_pieces = chip_end.reshape(piece_shape)
    decay_pieces = jnp.broadcast_to(chip_decay, chip_end.shape).reshape(piece_shape)
    received = jnp.zeros(piece_shape, F32)
    y_local = None
    placed = [min(group, max(rounds, 1) - 1) for group in range(set_groups)]
    for step_index in range(max(rounds, 1)):
        send_at = jnp.clip(step_index - ctx_index, 0, pieces - 1)
        outgoing = lax.dynamic_index_in_dim(
            end_pieces, send_at, 0, keepdims=False
        ) + lax.dynamic_index_in_dim(decay_pieces, send_at, 0, keepdims=False) * (
            lax.dynamic_index_in_dim(received, send_at, 0, keepdims=False)
        )
        held = scan_inputs
        if any(p == step_index for p in placed):
            outgoing, held = lax.optimization_barrier((outgoing, scan_inputs))
        if rounds > 0:
            arrived = passed_along(outgoing, "ctx", 1)
        for group in range(set_groups):
            if placed[group] == step_index:
                y_local = scan_group(group, held, y_local)
        if rounds == 0:
            break
        if any(p == step_index for p in placed):
            arrived, y_local = lax.optimization_barrier((arrived, y_local))
        recv_at = step_index - ctx_index + 1
        valid = (recv_at >= 0) & (recv_at < pieces) & (ctx_index > 0)
        updated = lax.dynamic_update_index_in_dim(
            received, arrived, jnp.clip(recv_at, 0, pieces - 1), 0
        )
        received = jnp.where(valid, updated, received)
    carried = received.reshape(chip_end.shape)
    into_second = decay_first * carried + first_end
    keep = jnp.where(sub_index == 0, carried, into_second)
    got = swapped(jnp.where(sub_index == 0, into_second, carried), "sub")
    low = jnp.where(sub_index == 0, keep, got)
    high = jnp.where(sub_index == 0, got, keep)
    incoming = jnp.stack([low, high], 2).reshape(set_groups, pairs, state, 128)

    out_len = min(256, own)
    return pl.pallas_call(
        out_kernel,
        grid=(set_groups, own // out_len),
        in_specs=[
            pl.BlockSpec((out_len, group_width), lambda g, c: (c, g)),
            pl.BlockSpec((1, out_len, state), lambda g, c: (g, c, 0)),
            pl.BlockSpec((1, out_len, per_group), lambda g, c: (g, c, 0)),
            pl.BlockSpec((1, pairs, state, 128), lambda g, c: (g, 0, 0, 0)),
            pl.BlockSpec((out_len, group_width), lambda g, c: (c, g)),
            pl.BlockSpec((1, group_width), lambda g, c: (0, g)),
        ],
        out_specs=pl.BlockSpec((out_len, group_width), lambda g, c: (c, g)),
        out_shape=jax.ShapeDtypeStruct((own, channels), jnp.bfloat16),
        scratch_shapes=[pltpu.VMEM((out_len, group_width), F32)],
    )(y_local[0], c_cols, cum_device.transpose(0, 2, 1), incoming, y_local[1], norm_w[None, :])


def solution(mesh):
    in_specs = (
        P(("groups", "ctx"), "head"),
        P(None, "head", "sub", ("groups", "ctx")),
        P(("groups", "ctx", "sub"), "head"),
        P("head", ("groups", "ctx")),
        P(None, "head"),
        P("head"),
        P(None, None, "head", None),
        P(None, "head", None),
        P("head"),
        P("head"),
        P("head"),
        P("head"),
    )
    out_specs = P(("groups", "ctx", "sub"), "head")
    return jax.shard_map(
        per_device, mesh=mesh, in_specs=in_specs, out_specs=out_specs, check_vma=False
    )
```

```python
import jax
import jax.numpy as jnp
from jax import lax
from jax.experimental import pallas as pl
from jax.experimental.pallas import tpu as pltpu
from jax.sharding import PartitionSpec as P

HEADS = 128
HEAD_DIM = 64
GROUPS = 8
CONV_K = 4


HIGHEST = lax.Precision.HIGHEST
F32 = jnp.float32


def passed_along(x, axis, by):
    length = lax.axis_size(axis)
    pairs = [(i, i + by) for i in range(length) if 0 <= i + by < length]
    return lax.ppermute(x, axis, pairs)


def swapped(x, axis):
    return lax.ppermute(x, axis, [(0, 1), (1, 0)])


def conv_rows(padded, weights, bias_row):
    sequence_length = padded.shape[0] - (CONV_K - 1)
    total = jnp.zeros((sequence_length, padded.shape[1]), jnp.float32) + bias_row[None, :]
    for tap_index in range(CONV_K):
        total = total + weights[tap_index][None, :] * padded[
            tap_index : tap_index + sequence_length
        ].astype(jnp.float32)
    return jax.nn.silu(total)


def conv_cols(padded, weights, bias_block):
    sequence_length = padded.shape[-1] - (CONV_K - 1)
    total = jnp.zeros(padded.shape[:-1] + (sequence_length,), jnp.float32) + bias_block[..., None]
    for tap_index in range(CONV_K):
        total = total + weights[tap_index][..., None] * padded[
            ..., tap_index : tap_index + sequence_length
        ].astype(jnp.float32)
    return jax.nn.silu(total)


def dot(a, b):
    return jnp.dot(a, b, precision=HIGHEST, preferred_element_type=F32)


def split(a):
    high = a.astype(jnp.bfloat16)
    return high, (a - high.astype(F32)).astype(jnp.bfloat16)


def dot3(a_parts, b_parts):
    a_high, a_low = a_parts
    b_high, b_low = b_parts
    flat = lambda u, v: jnp.dot(u, v, preferred_element_type=F32)
    return flat(a_high, b_high) + (flat(a_high, b_low) + flat(a_low, b_high))


def pair_columns(cumc, pair, rows):
    left = lax.broadcasted_iota(jnp.int32, (1, 128), 1) < HEAD_DIM
    return jnp.where(
        left,
        jnp.broadcast_to(cumc[:, 2 * pair : 2 * pair + 1], (rows, 128)),
        jnp.broadcast_to(cumc[:, 2 * pair + 1 : 2 * pair + 2], (rows, 128)),
    )


def scan_kernel(xc_ref, ct_ref, b_ref, cumr_ref, cumc_ref, stp_ref, dsk_ref, z_ref, y_ref, sz_ref, e_ref):
    chunk = pl.program_id(1)
    block_len = xc_ref.shape[0]
    pairs = e_ref.shape[0]
    heads = 2 * pairs

    @pl.when(chunk == 0)
    def _():
        e_ref[...] = jnp.zeros_like(e_ref)

    ct = split(ct_ref[0])
    bm = b_ref[0]
    scores = dot3(ct, split(bm))
    rows = lax.broadcasted_iota(jnp.int32, (block_len, block_len), 0)
    cols = lax.broadcasted_iota(jnp.int32, (block_len, block_len), 1)
    causal = rows >= cols
    cumr = cumr_ref[0]
    cumc = cumc_ref[0]
    stp = stp_ref[0]
    left = lax.broadcasted_iota(jnp.int32, (1, 128), 1) < HEAD_DIM
    for pair in range(pairs):
        lanes = slice(pair * 128, (pair + 1) * 128)
        xp = xc_ref[:, lanes]
        xs = split(xp)
        s_old = e_ref[pair]
        ys = []
        us = []
        for side in range(2):
            head = 2 * pair + side
            dq = jnp.broadcast_to(cumc[:, head : head + 1], (block_len, block_len))
            ck = cumr[head : head + 1, :]
            sk = stp[head : head + 1, :]
            dec = jnp.exp(jnp.where(causal, dq - ck, -jnp.inf))
            ys.append(dot3(split(scores * dec * sk), xs))
            wk = jnp.exp(dq[block_len - 1 : block_len, :] - ck) * sk
            us.append(dot3(split(bm * wk), xs))
        cq = pair_columns(cumc, pair, block_len)
        inflow = dot3(ct, split(s_old)) * jnp.exp(cq)
        y = jnp.where(left, ys[0], ys[1]) + inflow
        z = z_ref[:, lanes].astype(F32)
        gate = z / (1.0 + jnp.exp(-z))
        sz_ref[:, lanes] = gate
        y_ref[:, lanes] = (y + xp * dsk_ref[:, lanes]) * gate
        e_ref[pair] = jnp.exp(cq[block_len - 1 : block_len, :]) * s_old + jnp.where(
            left, us[0], us[1]
        )


def end_kernel(xc_ref, b_ref, wk_ref, e_ref):
    pairs = e_ref.shape[1]
    bm = b_ref[0]
    wk = wk_ref[0]
    left = lax.broadcasted_iota(jnp.int32, (1, 128), 1) < HEAD_DIM
    for pair in range(pairs):
        xs = split(xc_ref[:, pair * 128 : (pair + 1) * 128])
        us = [
            dot3(split(bm * wk[2 * pair + side : 2 * pair + side + 1, :]), xs) for side in range(2)
        ]
        e_ref[0, pair] = jnp.where(left, us[0], us[1])


def out_kernel(y_ref, ct_ref, cumc_ref, v_ref, sz_ref, nw_ref, o_ref, g_ref):
    pairs = v_ref.shape[1]
    heads = 2 * pairs
    ct = split(ct_ref[0])
    cumc = cumc_ref[0]
    total = jnp.zeros((y_ref.shape[0], 128), F32)
    for pair in range(pairs):
        lanes = slice(pair * 128, (pair + 1) * 128)
        cq = pair_columns(cumc, pair, y_ref.shape[0])
        gated = y_ref[:, lanes] + dot3(ct, split(v_ref[0, pair])) * jnp.exp(cq) * sz_ref[:, lanes]
        g_ref[:, lanes] = gated
        total = total + gated * gated
    mean_square = jnp.sum(total, axis=-1, keepdims=True) / g_ref.shape[1]
    o_ref[...] = (g_ref[...] * lax.rsqrt(mean_square + 1e-05) * nw_ref[...]).astype(o_ref.dtype)


def per_device(
    x_raw,
    bc_raw,
    z_gate,
    dt_raw,
    conv_x_w,
    conv_x_b,
    conv_bc_w,
    conv_bc_b,
    dt_bias,
    a_log,
    d_skip,
    norm_w,
):
    tokens = x_raw.shape[0]
    heads_dev = dt_raw.shape[0]
    per_group = HEADS // GROUPS
    set_groups = heads_dev // per_group
    pairs = per_group // 2
    group_width = per_group * HEAD_DIM
    nsub = lax.axis_size("sub")
    sub_index = lax.axis_index("sub")
    own = tokens // nsub
    half = bc_raw.shape[2]
    state = half * nsub
    channels = heads_dev * HEAD_DIM
    rim_len = CONV_K - 1

    bc_tail = bc_raw[..., tokens - rim_len :]
    rims = passed_along(
        jnp.concatenate(
            [x_raw[tokens - rim_len :], bc_tail.reshape(-1, rim_len).transpose(1, 0)], 1
        ),
        "ctx",
        1,
    )
    x_rim = rims[:, :channels]
    bc_rim = rims[:, channels:].transpose(1, 0).reshape(bc_tail.shape)
    x_pad = jnp.concatenate([x_rim, x_raw], 0)
    x_own = conv_rows(
        lax.dynamic_slice_in_dim(x_pad, sub_index * own, own + rim_len, 0), conv_x_w, conv_x_b
    )
    x_other = conv_rows(
        lax.dynamic_slice_in_dim(x_pad, (1 - sub_index) * own, own + rim_len, 0),
        conv_x_w,
        conv_x_b,
    )
    bc_weights = lax.dynamic_slice_in_dim(conv_bc_w, sub_index * half, half, 3)
    bc_bias = lax.dynamic_slice_in_dim(conv_bc_b, sub_index * half, half, 2)
    bc_conv = conv_cols(jnp.concatenate([bc_rim, bc_raw], 3), bc_weights, bc_bias)
    bc_mine = lax.dynamic_slice_in_dim(bc_conv, sub_index * own, own, 3)
    bc_theirs = swapped(lax.dynamic_slice_in_dim(bc_conv, (1 - sub_index) * own, own, 3), "sub")
    bc_own = jnp.stack(
        [
            jnp.where(sub_index == 0, bc_mine, bc_theirs),
            jnp.where(sub_index == 0, bc_theirs, bc_mine),
        ],
        2,
    ).reshape(2, set_groups, state, own)
    b_rows = bc_own[0]
    c_cols = bc_own[1].transpose(0, 2, 1)

    step_sizes = jax.nn.softplus(dt_raw + dt_bias[:, None])
    log_decay = -jnp.exp(a_log)[:, None] * step_sizes
    half_totals = jnp.exp(log_decay.reshape(heads_dev, nsub, own).sum(-1))
    step_own = lax.dynamic_slice_in_dim(step_sizes, sub_index * own, own, 1)
    decay_own = lax.dynamic_slice_in_dim(log_decay, sub_index * own, own, 1)
    block_len = min(128, own)
    blocks = own // block_len
    upper = (
        lax.broadcasted_iota(jnp.int32, (block_len, block_len), 0)
        <= lax.broadcasted_iota(jnp.int32, (block_len, block_len), 1)
    ).astype(F32)
    cum_local = jnp.einsum(
        "hct,tu->hcu", decay_own.reshape(heads_dev, blocks, block_len), upper, precision=HIGHEST
    )
    block_totals = cum_local[..., -1]
    offsets = jnp.cumsum(block_totals, axis=-1) - block_totals
    cum_device = (cum_local + offsets[..., None]).reshape(set_groups, per_group, own)
    cum_rows = cum_local.reshape(set_groups, per_group, own)
    cum_cols = cum_rows.transpose(0, 2, 1)
    step_rows = step_own.reshape(set_groups, per_group, own)
    skip_row = jnp.repeat(d_skip, HEAD_DIM)[None, :]

    cum_all = jnp.einsum(
        "hjct,tu->hjcu",
        log_decay.reshape(heads_dev, nsub, blocks, block_len),
        upper,
        precision=HIGHEST,
    )
    all_totals = cum_all[..., -1]
    cum_all = (cum_all + (jnp.cumsum(all_totals, axis=-1) - all_totals)[..., None]).reshape(
        heads_dev, nsub, own
    )
    to_end = jnp.exp(cum_all[..., own - 1 :] - cum_all) * step_sizes.reshape(heads_dev, nsub, own)
    to_end = to_end.reshape(set_groups, per_group, tokens)

    def end_states(x_half, at):
        return pl.pallas_call(
            end_kernel,
            grid=(set_groups,),
            in_specs=[
                pl.BlockSpec((own, group_width), lambda g: (0, g)),
                pl.BlockSpec((1, half, own), lambda g: (g, 0, 0)),
                pl.BlockSpec((1, per_group, own), lambda g: (g, 0, 0)),
            ],
            out_specs=pl.BlockSpec((1, pairs, half, 128), lambda g: (g, 0, 0, 0)),
            out_shape=jax.ShapeDtypeStruct((set_groups, pairs, half, 128), F32),
        )(
            x_half,
            lax.dynamic_slice_in_dim(bc_conv[0], at * own, own, 2),
            lax.dynamic_slice_in_dim(to_end, at * own, own, 2),
        )

    own_end = end_states(x_own, sub_index)
    other_end = end_states(x_other, 1 - sub_index)

    def pair_layout(values):
        return jnp.repeat(values.reshape(set_groups, pairs, 2), HEAD_DIM, axis=-1)[:, :, None, :]

    decay_first = pair_layout(half_totals[:, 0])
    decay_second = pair_layout(half_totals[:, 1])
    first_end = jnp.where(sub_index == 0, own_end, other_end)
    second_end = jnp.where(sub_index == 0, other_end, own_end)
    chip_end = decay_second * first_end + second_end
    chip_decay = decay_first * decay_second
    ctx_index = lax.axis_index("ctx")
    ctx_size = lax.axis_size("ctx")
    scan_inputs = (x_own, c_cols, b_rows, cum_rows, cum_cols, step_rows, skip_row, z_gate)

    def scan_group(group, inputs, target):
        count = len(inputs)
        extra = {} if target is None else {"input_output_aliases": {count: 0, count + 1: 1}}
        tile = pl.BlockSpec((block_len, group_width), lambda g, c: (c, group))
        in_specs = [
            tile,
            pl.BlockSpec((1, block_len, state), lambda g, c: (group, c, 0)),
            pl.BlockSpec((1, state, block_len), lambda g, c: (group, 0, c)),
            pl.BlockSpec((1, per_group, block_len), lambda g, c: (group, 0, c)),
            pl.BlockSpec((1, block_len, per_group), lambda g, c: (group, c, 0)),
            pl.BlockSpec((1, per_group, block_len), lambda g, c: (group, 0, c)),
            pl.BlockSpec((1, group_width), lambda g, c: (0, group)),
            tile,
        ]
        operands = tuple(inputs)
        kernel = scan_kernel
        if target is not None:
            in_specs = in_specs + [pl.BlockSpec(memory_space=pl.ANY)] * 2
            operands = operands + tuple(target)
            kernel = lambda *refs: scan_kernel(*refs[:count], *refs[count + 2 :])
        return pl.pallas_call(
            kernel,
            grid=(1, blocks),
            in_specs=in_specs,
            out_specs=[tile, tile],
            out_shape=[jax.ShapeDtypeStruct((own, channels), F32)] * 2,
            scratch_shapes=[pltpu.VMEM((pairs, state, 128), F32)],
            **extra,
        )(*operands)

    pieces = 2 if (set_groups * pairs) % 2 == 0 else 1
    rounds = ctx_size + pieces - 2
    piece_shape = (pieces, set_groups * pairs // pieces, half, 128)
    end_pieces = chip_end.reshape(piece_shape)
    decay_pieces = jnp.broadcast_to(chip_decay, chip_end.shape).reshape(piece_shape)
    received = jnp.zeros(piece_shape, F32)
    y_local = None
    placed = [min(group, max(rounds, 1) - 1) for group in range(set_groups)]
    for step_index in range(max(rounds, 1)):
        send_at = jnp.clip(step_index - ctx_index, 0, pieces - 1)
        outgoing = lax.dynamic_index_in_dim(
            end_pieces, send_at, 0, keepdims=False
        ) + lax.dynamic_index_in_dim(decay_pieces, send_at, 0, keepdims=False) * (
            lax.dynamic_index_in_dim(received, send_at, 0, keepdims=False)
        )
        held = scan_inputs
        if any(p == step_index for p in placed):
            outgoing, held = lax.optimization_barrier((outgoing, scan_inputs))
        if rounds > 0:
            arrived = passed_along(outgoing, "ctx", 1)
        for group in range(set_groups):
            if placed[group] == step_index:
                y_local = scan_group(group, held, y_local)
        if rounds == 0:
            break
        if any(p == step_index for p in placed):
            arrived, y_local = lax.optimization_barrier((arrived, y_local))
        recv_at = step_index - ctx_index + 1
        valid = (recv_at >= 0) & (recv_at < pieces) & (ctx_index > 0)
        updated = lax.dynamic_update_index_in_dim(
            received, arrived, jnp.clip(recv_at, 0, pieces - 1), 0
        )
        received = jnp.where(valid, updated, received)
    carried = received.reshape(chip_end.shape)
    into_second = decay_first * carried + first_end
    keep = jnp.where(sub_index == 0, carried, into_second)
    got = swapped(jnp.where(sub_index == 0, into_second, carried), "sub")
    low = jnp.where(sub_index == 0, keep, got)
    high = jnp.where(sub_index == 0, got, keep)
    incoming = jnp.stack([low, high], 2).reshape(set_groups, pairs, state, 128)

    out_len = min(256, own)
    return pl.pallas_call(
        out_kernel,
        grid=(set_groups, own // out_len),
        in_specs=[
            pl.BlockSpec((out_len, group_width), lambda g, c: (c, g)),
            pl.BlockSpec((1, out_len, state), lambda g, c: (g, c, 0)),
            pl.BlockSpec((1, out_len, per_group), lambda g, c: (g, c, 0)),
            pl.BlockSpec((1, pairs, state, 128), lambda g, c: (g, 0, 0, 0)),
            pl.BlockSpec((out_len, group_width), lambda g, c: (c, g)),
            pl.BlockSpec((1, group_width), lambda g, c: (0, g)),
        ],
        out_specs=pl.BlockSpec((out_len, group_width), lambda g, c: (c, g)),
        out_shape=jax.ShapeDtypeStruct((own, channels), jnp.bfloat16),
        scratch_shapes=[pltpu.VMEM((out_len, group_width), F32)],
    )(y_local[0], c_cols, cum_device.transpose(0, 2, 1), incoming, y_local[1], norm_w[None, :])


def solution(mesh):
    in_specs = (
        P(("groups", "ctx"), "head"),
        P(None, "head", "sub", ("groups", "ctx")),
        P(("groups", "ctx", "sub"), "head"),
        P("head", ("groups", "ctx")),
        P(None, "head"),
        P("head"),
        P(None, None, "head", None),
        P(None, "head", None),
        P("head"),
        P("head"),
        P("head"),
        P("head"),
    )
    out_specs = P(("groups", "ctx", "sub"), "head")
    return jax.shard_map(
        per_device, mesh=mesh, in_specs=in_specs, out_specs=out_specs, check_vma=False
    )
```

```python
import jax
import jax.numpy as jnp
from jax import lax
from jax.experimental import pallas as pl
from jax.experimental.pallas import tpu as pltpu
from jax.sharding import PartitionSpec as P

HEADS = 128
HEAD_DIM = 64
GROUPS = 8
CONV_K = 4


HIGHEST = lax.Precision.HIGHEST
F32 = jnp.float32


def passed_along(x, axis, by):
    length = lax.axis_size(axis)
    pairs = [(i, i + by) for i in range(length) if 0 <= i + by < length]
    return lax.ppermute(x, axis, pairs)


def swapped(x, axis):
    return lax.ppermute(x, axis, [(0, 1), (1, 0)])


def conv_rows(padded, weights, bias_row):
    sequence_length = padded.shape[0] - (CONV_K - 1)
    total = jnp.zeros((sequence_length, padded.shape[1]), jnp.float32) + bias_row[None, :]
    for tap_index in range(CONV_K):
        total = total + weights[tap_index][None, :] * padded[
            tap_index : tap_index + sequence_length
        ].astype(jnp.float32)
    return jax.nn.silu(total)


def conv_cols(padded, weights, bias_block):
    sequence_length = padded.shape[-1] - (CONV_K - 1)
    total = jnp.zeros(padded.shape[:-1] + (sequence_length,), jnp.float32) + bias_block[..., None]
    for tap_index in range(CONV_K):
        total = total + weights[tap_index][..., None] * padded[
            ..., tap_index : tap_index + sequence_length
        ].astype(jnp.float32)
    return jax.nn.silu(total)


def dot(a, b):
    return jnp.dot(a, b, precision=HIGHEST, preferred_element_type=F32)


def split(a):
    high = a.astype(jnp.bfloat16)
    return high, (a - high.astype(F32)).astype(jnp.bfloat16)


def dot3(a_parts, b_parts):
    a_high, a_low = a_parts
    b_high, b_low = b_parts
    flat = lambda u, v: jnp.dot(u, v, preferred_element_type=F32)
    return flat(a_high, b_high) + (flat(a_high, b_low) + flat(a_low, b_high))


def pair_columns(cumc, pair, rows):
    left = lax.broadcasted_iota(jnp.int32, (1, 128), 1) < HEAD_DIM
    return jnp.where(
        left,
        jnp.broadcast_to(cumc[:, 2 * pair : 2 * pair + 1], (rows, 128)),
        jnp.broadcast_to(cumc[:, 2 * pair + 1 : 2 * pair + 2], (rows, 128)),
    )


def scan_kernel(xc_ref, ct_ref, b_ref, cumr_ref, cumc_ref, stp_ref, dsk_ref, y_ref, e_ref):
    chunk = pl.program_id(1)
    block_len = xc_ref.shape[0]
    pairs = e_ref.shape[0]
    heads = 2 * pairs

    @pl.when(chunk == 0)
    def _():
        e_ref[...] = jnp.zeros_like(e_ref)

    ct = split(ct_ref[0])
    bm = b_ref[0]
    scores = dot3(ct, split(bm))
    rows = lax.broadcasted_iota(jnp.int32, (block_len, block_len), 0)
    cols = lax.broadcasted_iota(jnp.int32, (block_len, block_len), 1)
    causal = rows >= cols
    cumr = cumr_ref[0]
    cumc = cumc_ref[0]
    stp = stp_ref[0]
    left = lax.broadcasted_iota(jnp.int32, (1, 128), 1) < HEAD_DIM
    for pair in range(pairs):
        lanes = slice(pair * 128, (pair + 1) * 128)
        xp = xc_ref[:, lanes]
        xs = split(xp)
        s_old = e_ref[pair]
        ys = []
        us = []
        for side in range(2):
            head = 2 * pair + side
            dq = jnp.broadcast_to(cumc[:, head : head + 1], (block_len, block_len))
            ck = cumr[head : head + 1, :]
            sk = stp[head : head + 1, :]
            dec = jnp.exp(jnp.where(causal, dq - ck, -jnp.inf))
            ys.append(dot3(split(scores * dec * sk), xs))
            wk = jnp.exp(dq[block_len - 1 : block_len, :] - ck) * sk
            us.append(dot3(split(bm * wk), xs))
        cq = pair_columns(cumc, pair, block_len)
        inflow = dot3(ct, split(s_old)) * jnp.exp(cq)
        y = jnp.where(left, ys[0], ys[1]) + inflow
        y_ref[:, lanes] = y + xp * dsk_ref[:, lanes]
        e_ref[pair] = jnp.exp(cq[block_len - 1 : block_len, :]) * s_old + jnp.where(
            left, us[0], us[1]
        )


def end_kernel(xc_ref, b_ref, wk_ref, e_ref):
    pairs = e_ref.shape[1]
    bm = b_ref[0]
    wk = wk_ref[0]
    left = lax.broadcasted_iota(jnp.int32, (1, 128), 1) < HEAD_DIM
    for pair in range(pairs):
        xs = split(xc_ref[:, pair * 128 : (pair + 1) * 128])
        us = [
            dot3(split(bm * wk[2 * pair + side : 2 * pair + side + 1, :]), xs) for side in range(2)
        ]
        e_ref[0, pair] = jnp.where(left, us[0], us[1])


def out_kernel(y_ref, ct_ref, cumc_ref, v_ref, z_ref, nw_ref, o_ref, g_ref):
    pairs = v_ref.shape[1]
    heads = 2 * pairs
    ct = split(ct_ref[0])
    cumc = cumc_ref[0]
    total = jnp.zeros((y_ref.shape[0], 128), F32)
    for pair in range(pairs):
        lanes = slice(pair * 128, (pair + 1) * 128)
        cq = pair_columns(cumc, pair, y_ref.shape[0])
        y = y_ref[:, lanes] + dot3(ct, split(v_ref[0, pair])) * jnp.exp(cq)
        z = z_ref[:, lanes].astype(F32)
        gated = y * (z / (1.0 + jnp.exp(-z)))
        g_ref[:, lanes] = gated
        total = total + gated * gated
    mean_square = jnp.sum(total, axis=-1, keepdims=True) / g_ref.shape[1]
    o_ref[...] = (g_ref[...] * lax.rsqrt(mean_square + 1e-05) * nw_ref[...]).astype(o_ref.dtype)


def per_device(
    x_raw,
    bc_raw,
    z_gate,
    dt_raw,
    conv_x_w,
    conv_x_b,
    conv_bc_w,
    conv_bc_b,
    dt_bias,
    a_log,
    d_skip,
    norm_w,
):
    tokens = x_raw.shape[0]
    heads_dev = dt_raw.shape[0]
    per_group = HEADS // GROUPS
    set_groups = heads_dev // per_group
    pairs = per_group // 2
    group_width = per_group * HEAD_DIM
    nsub = lax.axis_size("sub")
    sub_index = lax.axis_index("sub")
    own = tokens // nsub
    half = bc_raw.shape[2]
    state = half * nsub
    channels = heads_dev * HEAD_DIM
    rim_len = CONV_K - 1

    bc_tail = bc_raw[..., tokens - rim_len :]
    rims = passed_along(
        jnp.concatenate(
            [x_raw[tokens - rim_len :], bc_tail.reshape(-1, rim_len).transpose(1, 0)], 1
        ),
        "ctx",
        1,
    )
    x_rim = rims[:, :channels]
    bc_rim = rims[:, channels:].transpose(1, 0).reshape(bc_tail.shape)
    x_pad = jnp.concatenate([x_rim, x_raw], 0)
    x_own = conv_rows(
        lax.dynamic_slice_in_dim(x_pad, sub_index * own, own + rim_len, 0), conv_x_w, conv_x_b
    )
    x_other = conv_rows(
        lax.dynamic_slice_in_dim(x_pad, (1 - sub_index) * own, own + rim_len, 0),
        conv_x_w,
        conv_x_b,
    )
    bc_weights = lax.dynamic_slice_in_dim(conv_bc_w, sub_index * half, half, 3)
    bc_bias = lax.dynamic_slice_in_dim(conv_bc_b, sub_index * half, half, 2)
    bc_conv = conv_cols(jnp.concatenate([bc_rim, bc_raw], 3), bc_weights, bc_bias)
    bc_mine = lax.dynamic_slice_in_dim(bc_conv, sub_index * own, own, 3)
    bc_theirs = swapped(lax.dynamic_slice_in_dim(bc_conv, (1 - sub_index) * own, own, 3), "sub")
    bc_own = jnp.stack(
        [
            jnp.where(sub_index == 0, bc_mine, bc_theirs),
            jnp.where(sub_index == 0, bc_theirs, bc_mine),
        ],
        2,
    ).reshape(2, set_groups, state, own)
    b_rows = bc_own[0]
    c_cols = bc_own[1].transpose(0, 2, 1)

    step_sizes = jax.nn.softplus(dt_raw + dt_bias[:, None])
    log_decay = -jnp.exp(a_log)[:, None] * step_sizes
    half_totals = jnp.exp(log_decay.reshape(heads_dev, nsub, own).sum(-1))
    step_own = lax.dynamic_slice_in_dim(step_sizes, sub_index * own, own, 1)
    decay_own = lax.dynamic_slice_in_dim(log_decay, sub_index * own, own, 1)
    block_len = min(128, own)
    blocks = own // block_len
    upper = (
        lax.broadcasted_iota(jnp.int32, (block_len, block_len), 0)
        <= lax.broadcasted_iota(jnp.int32, (block_len, block_len), 1)
    ).astype(F32)
    cum_local = jnp.einsum(
        "hct,tu->hcu", decay_own.reshape(heads_dev, blocks, block_len), upper, precision=HIGHEST
    )
    block_totals = cum_local[..., -1]
    offsets = jnp.cumsum(block_totals, axis=-1) - block_totals
    cum_device = (cum_local + offsets[..., None]).reshape(set_groups, per_group, own)
    cum_rows = cum_local.reshape(set_groups, per_group, own)
    cum_cols = cum_rows.transpose(0, 2, 1)
    step_rows = step_own.reshape(set_groups, per_group, own)
    skip_row = jnp.repeat(d_skip, HEAD_DIM)[None, :]

    cum_all = jnp.einsum(
        "hjct,tu->hjcu",
        log_decay.reshape(heads_dev, nsub, blocks, block_len),
        upper,
        precision=HIGHEST,
    )
    all_totals = cum_all[..., -1]
    cum_all = (cum_all + (jnp.cumsum(all_totals, axis=-1) - all_totals)[..., None]).reshape(
        heads_dev, nsub, own
    )
    to_end = jnp.exp(cum_all[..., own - 1 :] - cum_all) * step_sizes.reshape(heads_dev, nsub, own)
    to_end = to_end.reshape(set_groups, per_group, tokens)

    def end_states(x_half, at):
        return pl.pallas_call(
            end_kernel,
            grid=(set_groups,),
            in_specs=[
                pl.BlockSpec((own, group_width), lambda g: (0, g)),
                pl.BlockSpec((1, half, own), lambda g: (g, 0, 0)),
                pl.BlockSpec((1, per_group, own), lambda g: (g, 0, 0)),
            ],
            out_specs=pl.BlockSpec((1, pairs, half, 128), lambda g: (g, 0, 0, 0)),
            out_shape=jax.ShapeDtypeStruct((set_groups, pairs, half, 128), F32),
        )(
            x_half,
            lax.dynamic_slice_in_dim(bc_conv[0], at * own, own, 2),
            lax.dynamic_slice_in_dim(to_end, at * own, own, 2),
        )

    own_end = end_states(x_own, sub_index)
    other_end = end_states(x_other, 1 - sub_index)

    def pair_layout(values):
        return jnp.repeat(values.reshape(set_groups, pairs, 2), HEAD_DIM, axis=-1)[:, :, None, :]

    decay_first = pair_layout(half_totals[:, 0])
    decay_second = pair_layout(half_totals[:, 1])
    first_end = jnp.where(sub_index == 0, own_end, other_end)
    second_end = jnp.where(sub_index == 0, other_end, own_end)
    chip_end = decay_second * first_end + second_end
    chip_decay = decay_first * decay_second
    ctx_index = lax.axis_index("ctx")
    ctx_size = lax.axis_size("ctx")
    scan_inputs = (x_own, c_cols, b_rows, cum_rows, cum_cols, step_rows, skip_row)

    def scan_group(group, inputs, target):
        count = len(inputs)
        extra = {} if target is None else {"input_output_aliases": {count: 0}}
        tile = pl.BlockSpec((block_len, group_width), lambda g, c: (c, group))
        in_specs = [
            tile,
            pl.BlockSpec((1, block_len, state), lambda g, c: (group, c, 0)),
            pl.BlockSpec((1, state, block_len), lambda g, c: (group, 0, c)),
            pl.BlockSpec((1, per_group, block_len), lambda g, c: (group, 0, c)),
            pl.BlockSpec((1, block_len, per_group), lambda g, c: (group, c, 0)),
            pl.BlockSpec((1, per_group, block_len), lambda g, c: (group, 0, c)),
            pl.BlockSpec((1, group_width), lambda g, c: (0, group)),
        ]
        operands = tuple(inputs)
        kernel = scan_kernel
        if target is not None:
            in_specs = in_specs + [pl.BlockSpec(memory_space=pl.ANY)]
            operands = operands + (target,)
            kernel = lambda *refs: scan_kernel(*refs[:count], *refs[count + 1 :])
        return pl.pallas_call(
            kernel,
            grid=(1, blocks),
            in_specs=in_specs,
            out_specs=tile,
            out_shape=jax.ShapeDtypeStruct((own, channels), F32),
            scratch_shapes=[pltpu.VMEM((pairs, state, 128), F32)],
            **extra,
        )(*operands)

    pieces = 2 if (set_groups * pairs) % 2 == 0 else 1
    rounds = ctx_size + pieces - 2
    piece_shape = (pieces, set_groups * pairs // pieces, half, 128)
    end_pieces = chip_end.reshape(piece_shape)
    decay_pieces = jnp.broadcast_to(chip_decay, chip_end.shape).reshape(piece_shape)
    received = jnp.zeros(piece_shape, F32)
    y_local = None
    placed = [min(group, max(rounds, 1) - 1) for group in range(set_groups)]
    for step_index in range(max(rounds, 1)):
        send_at = jnp.clip(step_index - ctx_index, 0, pieces - 1)
        outgoing = lax.dynamic_index_in_dim(
            end_pieces, send_at, 0, keepdims=False
        ) + lax.dynamic_index_in_dim(decay_pieces, send_at, 0, keepdims=False) * (
            lax.dynamic_index_in_dim(received, send_at, 0, keepdims=False)
        )
        held = scan_inputs
        if any(p == step_index for p in placed):
            outgoing, held = lax.optimization_barrier((outgoing, scan_inputs))
        if rounds > 0:
            arrived = passed_along(outgoing, "ctx", 1)
        for group in range(set_groups):
            if placed[group] == step_index:
                y_local = scan_group(group, held, y_local)
        if rounds == 0:
            break
        if any(p == step_index for p in placed):
            arrived, y_local = lax.optimization_barrier((arrived, y_local))
        recv_at = step_index - ctx_index + 1
        valid = (recv_at >= 0) & (recv_at < pieces) & (ctx_index > 0)
        updated = lax.dynamic_update_index_in_dim(
            received, arrived, jnp.clip(recv_at, 0, pieces - 1), 0
        )
        received = jnp.where(valid, updated, received)
    carried = received.reshape(chip_end.shape)
    into_second = decay_first * carried + first_end
    keep = jnp.where(sub_index == 0, carried, into_second)
    got = swapped(jnp.where(sub_index == 0, into_second, carried), "sub")
    low = jnp.where(sub_index == 0, keep, got)
    high = jnp.where(sub_index == 0, got, keep)
    incoming = jnp.stack([low, high], 2).reshape(set_groups, pairs, state, 128)

    out_len = min(256, own)
    return pl.pallas_call(
        out_kernel,
        grid=(set_groups, own // out_len),
        in_specs=[
            pl.BlockSpec((out_len, group_width), lambda g, c: (c, g)),
            pl.BlockSpec((1, out_len, state), lambda g, c: (g, c, 0)),
            pl.BlockSpec((1, out_len, per_group), lambda g, c: (g, c, 0)),
            pl.BlockSpec((1, pairs, state, 128), lambda g, c: (g, 0, 0, 0)),
            pl.BlockSpec((out_len, group_width), lambda g, c: (c, g)),
            pl.BlockSpec((1, group_width), lambda g, c: (0, g)),
        ],
        out_specs=pl.BlockSpec((out_len, group_width), lambda g, c: (c, g)),
        out_shape=jax.ShapeDtypeStruct((own, channels), jnp.bfloat16),
        scratch_shapes=[pltpu.VMEM((out_len, group_width), F32)],
    )(y_local, c_cols, cum_device.transpose(0, 2, 1), incoming, z_gate, norm_w[None, :])


def solution(mesh):
    in_specs = (
        P(("groups", "ctx"), "head"),
        P(None, "head", "sub", ("groups", "ctx")),
        P(("groups", "ctx", "sub"), "head"),
        P("head", ("groups", "ctx")),
        P(None, "head"),
        P("head"),
        P(None, None, "head", None),
        P(None, "head", None),
        P("head"),
        P("head"),
        P("head"),
        P("head"),
    )
    out_specs = P(("groups", "ctx", "sub"), "head")
    return jax.shard_map(
        per_device, mesh=mesh, in_specs=in_specs, out_specs=out_specs, check_vma=False
    )
```

```python
import jax
import jax.numpy as jnp
from jax import lax
from jax.experimental import pallas as pl
from jax.experimental.pallas import tpu as pltpu
from jax.sharding import PartitionSpec as P

HEADS = 128
HEAD_DIM = 64
GROUPS = 8
CONV_K = 4


HIGHEST = lax.Precision.HIGHEST
F32 = jnp.float32


def passed_along(x, axis, by):
    length = lax.axis_size(axis)
    pairs = [(i, i + by) for i in range(length) if 0 <= i + by < length]
    return lax.ppermute(x, axis, pairs)


def swapped(x, axis):
    return lax.ppermute(x, axis, [(0, 1), (1, 0)])


def conv_rows(padded, weights, bias_row):
    sequence_length = padded.shape[0] - (CONV_K - 1)
    total = jnp.zeros((sequence_length, padded.shape[1]), jnp.float32) + bias_row[None, :]
    for tap_index in range(CONV_K):
        total = total + weights[tap_index][None, :] * padded[
            tap_index : tap_index + sequence_length
        ].astype(jnp.float32)
    return jax.nn.silu(total)


def conv_cols(padded, weights, bias_block):
    sequence_length = padded.shape[-1] - (CONV_K - 1)
    total = jnp.zeros(padded.shape[:-1] + (sequence_length,), jnp.float32) + bias_block[..., None]
    for tap_index in range(CONV_K):
        total = total + weights[tap_index][..., None] * padded[
            ..., tap_index : tap_index + sequence_length
        ].astype(jnp.float32)
    return jax.nn.silu(total)


def dot(a, b):
    return jnp.dot(a, b, precision=HIGHEST, preferred_element_type=F32)


def split(a):
    high = a.astype(jnp.bfloat16)
    return high, (a - high.astype(F32)).astype(jnp.bfloat16)


def dot3(a_parts, b_parts):
    a_high, a_low = a_parts
    b_high, b_low = b_parts
    flat = lambda u, v: jnp.dot(u, v, preferred_element_type=F32)
    return flat(a_high, b_high) + (flat(a_high, b_low) + flat(a_low, b_high))


def pair_columns(cumc, pair, rows):
    left = lax.broadcasted_iota(jnp.int32, (1, 128), 1) < HEAD_DIM
    return jnp.where(
        left,
        jnp.broadcast_to(cumc[:, 2 * pair : 2 * pair + 1], (rows, 128)),
        jnp.broadcast_to(cumc[:, 2 * pair + 1 : 2 * pair + 2], (rows, 128)),
    )


def scan_kernel(xc_ref, ct_ref, b_ref, cumr_ref, cumc_ref, stp_ref, dsk_ref, y_ref, e_ref):
    chunk = pl.program_id(1)
    block_len = xc_ref.shape[0]
    pairs = e_ref.shape[0]
    heads = 2 * pairs

    @pl.when(chunk == 0)
    def _():
        e_ref[...] = jnp.zeros_like(e_ref)

    ct = split(ct_ref[0])
    bm = b_ref[0]
    scores = dot3(ct, split(bm))
    rows = lax.broadcasted_iota(jnp.int32, (block_len, block_len), 0)
    cols = lax.broadcasted_iota(jnp.int32, (block_len, block_len), 1)
    causal = rows >= cols
    cumr = cumr_ref[0]
    cumc = cumc_ref[0]
    stp = stp_ref[0]
    left = lax.broadcasted_iota(jnp.int32, (1, 128), 1) < HEAD_DIM
    for pair in range(pairs):
        lanes = slice(pair * 128, (pair + 1) * 128)
        xp = xc_ref[:, lanes]
        xs = split(xp)
        s_old = e_ref[pair]
        ys = []
        us = []
        for side in range(2):
            head = 2 * pair + side
            dq = jnp.broadcast_to(cumc[:, head : head + 1], (block_len, block_len))
            ck = cumr[head : head + 1, :]
            sk = stp[head : head + 1, :]
            dec = jnp.exp(jnp.where(causal, dq - ck, -jnp.inf))
            ys.append(dot3(split(scores * dec * sk), xs))
            wk = jnp.exp(dq[block_len - 1 : block_len, :] - ck) * sk
            us.append(dot3(split(bm * wk), xs))
        cq = pair_columns(cumc, pair, block_len)
        inflow = dot3(ct, split(s_old)) * jnp.exp(cq)
        y = jnp.where(left, ys[0], ys[1]) + inflow
        y_ref[:, lanes] = y + xp * dsk_ref[:, lanes]
        e_ref[pair] = jnp.exp(cq[block_len - 1 : block_len, :]) * s_old + jnp.where(
            left, us[0], us[1]
        )


def end_kernel(xc_ref, b_ref, wk_ref, e_ref):
    pairs = e_ref.shape[1]
    bm = b_ref[0]
    wk = wk_ref[0]
    left = lax.broadcasted_iota(jnp.int32, (1, 128), 1) < HEAD_DIM
    for pair in range(pairs):
        xs = split(xc_ref[:, pair * 128 : (pair + 1) * 128])
        us = [
            dot3(split(bm * wk[2 * pair + side : 2 * pair + side + 1, :]), xs) for side in range(2)
        ]
        e_ref[0, pair] = jnp.where(left, us[0], us[1])


def out_kernel(y_ref, ct_ref, cumc_ref, v_ref, z_ref, nw_ref, o_ref, g_ref):
    pairs = v_ref.shape[1]
    heads = 2 * pairs
    ct = split(ct_ref[0])
    cumc = cumc_ref[0]
    total = jnp.zeros((y_ref.shape[0], 128), F32)
    for pair in range(pairs):
        lanes = slice(pair * 128, (pair + 1) * 128)
        cq = pair_columns(cumc, pair, y_ref.shape[0])
        y = y_ref[:, lanes] + dot3(ct, split(v_ref[0, pair])) * jnp.exp(cq)
        z = z_ref[:, lanes].astype(F32)
        gated = y * (z / (1.0 + jnp.exp(-z)))
        g_ref[:, lanes] = gated
        total = total + gated * gated
    mean_square = jnp.sum(total, axis=-1, keepdims=True) / g_ref.shape[1]
    o_ref[...] = (g_ref[...] * lax.rsqrt(mean_square + 1e-05) * nw_ref[...]).astype(o_ref.dtype)


def per_device(
    x_raw,
    bc_raw,
    z_gate,
    dt_raw,
    conv_x_w,
    conv_x_b,
    conv_bc_w,
    conv_bc_b,
    dt_bias,
    a_log,
    d_skip,
    norm_w,
):
    tokens = x_raw.shape[0]
    heads_dev = dt_raw.shape[0]
    per_group = HEADS // GROUPS
    set_groups = heads_dev // per_group
    pairs = per_group // 2
    group_width = per_group * HEAD_DIM
    nsub = lax.axis_size("sub")
    ctx_size = lax.axis_size("ctx")
    sub_index = lax.axis_index("sub")
    own = tokens // nsub
    half = bc_raw.shape[2]
    state = half * nsub
    channels = heads_dev * HEAD_DIM
    rim_len = CONV_K - 1

    bc_tail = bc_raw[..., tokens - rim_len :]
    rims = passed_along(
        jnp.concatenate(
            [x_raw[tokens - rim_len :], bc_tail.reshape(-1, rim_len).transpose(1, 0)], 1
        ),
        "ctx",
        1,
    )
    x_rim = rims[:, :channels]
    bc_rim = rims[:, channels:].transpose(1, 0).reshape(bc_tail.shape)
    x_pad = jnp.concatenate([x_rim, x_raw], 0)
    x_own = conv_rows(
        lax.dynamic_slice_in_dim(x_pad, sub_index * own, own + rim_len, 0), conv_x_w, conv_x_b
    )
    x_other = conv_rows(
        lax.dynamic_slice_in_dim(x_pad, (1 - sub_index) * own, own + rim_len, 0),
        conv_x_w,
        conv_x_b,
    )
    bc_weights = lax.dynamic_slice_in_dim(conv_bc_w, sub_index * half, half, 3)
    bc_bias = lax.dynamic_slice_in_dim(conv_bc_b, sub_index * half, half, 2)
    bc_conv = conv_cols(jnp.concatenate([bc_rim, bc_raw], 3), bc_weights, bc_bias)
    bc_mine = lax.dynamic_slice_in_dim(bc_conv, sub_index * own, own, 3)
    bc_theirs = swapped(lax.dynamic_slice_in_dim(bc_conv, (1 - sub_index) * own, own, 3), "sub")
    bc_own = jnp.stack(
        [
            jnp.where(sub_index == 0, bc_mine, bc_theirs),
            jnp.where(sub_index == 0, bc_theirs, bc_mine),
        ],
        2,
    ).reshape(2, set_groups, state, own)
    b_rows = bc_own[0]
    c_cols = bc_own[1].transpose(0, 2, 1)

    step_sizes = jax.nn.softplus(dt_raw + dt_bias[:, None])
    log_decay = -jnp.exp(a_log)[:, None] * step_sizes
    half_totals = jnp.exp(log_decay.reshape(heads_dev, nsub, own).sum(-1))
    step_own = lax.dynamic_slice_in_dim(step_sizes, sub_index * own, own, 1)
    decay_own = lax.dynamic_slice_in_dim(log_decay, sub_index * own, own, 1)
    block_len = min(128, own)
    blocks = own // block_len
    upper = (
        lax.broadcasted_iota(jnp.int32, (block_len, block_len), 0)
        <= lax.broadcasted_iota(jnp.int32, (block_len, block_len), 1)
    ).astype(F32)
    cum_local = jnp.einsum(
        "hct,tu->hcu", decay_own.reshape(heads_dev, blocks, block_len), upper, precision=HIGHEST
    )
    block_totals = cum_local[..., -1]
    offsets = jnp.cumsum(block_totals, axis=-1) - block_totals
    cum_device = (cum_local + offsets[..., None]).reshape(set_groups, per_group, own)
    cum_rows = cum_local.reshape(set_groups, per_group, own)
    cum_cols = cum_rows.transpose(0, 2, 1)
    step_rows = step_own.reshape(set_groups, per_group, own)
    skip_row = jnp.repeat(d_skip, HEAD_DIM)[None, :]

    cum_all = jnp.einsum(
        "hjct,tu->hjcu",
        log_decay.reshape(heads_dev, nsub, blocks, block_len),
        upper,
        precision=HIGHEST,
    )
    all_totals = cum_all[..., -1]
    cum_all = (cum_all + (jnp.cumsum(all_totals, axis=-1) - all_totals)[..., None]).reshape(
        heads_dev, nsub, own
    )
    to_end = jnp.exp(cum_all[..., own - 1 :] - cum_all) * step_sizes.reshape(heads_dev, nsub, own)
    to_end = to_end.reshape(set_groups, per_group, tokens)

    def end_states(x_half, at, start, count):
        return pl.pallas_call(
            end_kernel,
            grid=(count,),
            in_specs=[
                pl.BlockSpec((own, group_width), lambda g: (0, g + start)),
                pl.BlockSpec((1, half, own), lambda g: (g + start, 0, 0)),
                pl.BlockSpec((1, per_group, own), lambda g: (g + start, 0, 0)),
            ],
            out_specs=pl.BlockSpec((1, pairs, half, 128), lambda g: (g, 0, 0, 0)),
            out_shape=jax.ShapeDtypeStruct((count, pairs, half, 128), F32),
        )(
            x_half,
            lax.dynamic_slice_in_dim(bc_conv[0], at * own, own, 2),
            lax.dynamic_slice_in_dim(to_end, at * own, own, 2),
        )

    def pair_layout(values):
        return jnp.repeat(values.reshape(set_groups, pairs, 2), HEAD_DIM, axis=-1)[:, :, None, :]

    decay_first = pair_layout(half_totals[:, 0])
    decay_second = pair_layout(half_totals[:, 1])
    chip_decay = decay_first * decay_second

    def chip_ends(x_pair, start, count):
        own_end = end_states(x_pair[0], sub_index, start, count)
        other_end = end_states(x_pair[1], 1 - sub_index, start, count)
        first = jnp.where(sub_index == 0, own_end, other_end)
        second = jnp.where(sub_index == 0, other_end, own_end)
        return first, decay_second[start : start + count] * first + second

    pieces = 2 if (set_groups * pairs) % 2 == 0 else 1
    rounds = ctx_size + pieces - 2
    early = set_groups // 2 if (pieces == 2 and set_groups % 2 == 0 and rounds > 0) else set_groups
    first_end, chip_end = chip_ends((x_own, x_other), 0, early)
    ctx_index = lax.axis_index("ctx")
    scan_inputs = (x_own, c_cols, b_rows, cum_rows, cum_cols, step_rows, skip_row)

    def scan_group(group, inputs, target):
        count = len(inputs)
        extra = {} if target is None else {"input_output_aliases": {count: 0}}
        tile = pl.BlockSpec((block_len, group_width), lambda g, c: (c, group))
        in_specs = [
            tile,
            pl.BlockSpec((1, block_len, state), lambda g, c: (group, c, 0)),
            pl.BlockSpec((1, state, block_len), lambda g, c: (group, 0, c)),
            pl.BlockSpec((1, per_group, block_len), lambda g, c: (group, 0, c)),
            pl.BlockSpec((1, block_len, per_group), lambda g, c: (group, c, 0)),
            pl.BlockSpec((1, per_group, block_len), lambda g, c: (group, 0, c)),
            pl.BlockSpec((1, group_width), lambda g, c: (0, group)),
        ]
        operands = tuple(inputs)
        kernel = scan_kernel
        if target is not None:
            in_specs = in_specs + [pl.BlockSpec(memory_space=pl.ANY)]
            operands = operands + (target,)
            kernel = lambda *refs: scan_kernel(*refs[:count], *refs[count + 1 :])
        return pl.pallas_call(
            kernel,
            grid=(1, blocks),
            in_specs=in_specs,
            out_specs=tile,
            out_shape=jax.ShapeDtypeStruct((own, channels), F32),
            scratch_shapes=[pltpu.VMEM((pairs, state, 128), F32)],
            **extra,
        )(*operands)

    piece_shape = (pieces, set_groups * pairs // pieces, half, 128)
    full_shape = (set_groups, pairs, half, 128)
    decay_pieces = jnp.broadcast_to(chip_decay, full_shape).reshape(piece_shape)
    if early == set_groups:
        end_pieces = chip_end.reshape(piece_shape)
    else:
        end_pieces = chip_end.reshape((1,) + piece_shape[1:])
    received = jnp.zeros(piece_shape, F32)
    y_local = None
    placed = [min(group, max(rounds, 1) - 1) for group in range(set_groups)]
    for step_index in range(max(rounds, 1)):
        send_at = jnp.clip(step_index - ctx_index, 0, pieces - 1)
        outgoing = lax.dynamic_index_in_dim(
            end_pieces, send_at, 0, keepdims=False
        ) + lax.dynamic_index_in_dim(decay_pieces, send_at, 0, keepdims=False) * (
            lax.dynamic_index_in_dim(received, send_at, 0, keepdims=False)
        )
        held = scan_inputs
        x_pair = (x_own, x_other)
        if any(p == step_index for p in placed):
            outgoing, held, x_pair = lax.optimization_barrier((outgoing, scan_inputs, x_pair))
        if rounds > 0:
            arrived = passed_along(outgoing, "ctx", 1)
        for group in range(set_groups):
            if placed[group] == step_index:
                y_local = scan_group(group, held, y_local)
        late = None
        if step_index == 0 and early < set_groups:
            late = chip_ends(x_pair, early, set_groups - early)
        if rounds == 0:
            break
        if any(p == step_index for p in placed):
            arrived, y_local, late = lax.optimization_barrier((arrived, y_local, late))
        if late is not None:
            first_end = jnp.concatenate([first_end, late[0]], 0)
            chip_end = jnp.concatenate([chip_end, late[1]], 0)
            end_pieces = chip_end.reshape(piece_shape)
        recv_at = step_index - ctx_index + 1
        valid = (recv_at >= 0) & (recv_at < pieces) & (ctx_index > 0)
        updated = lax.dynamic_update_index_in_dim(
            received, arrived, jnp.clip(recv_at, 0, pieces - 1), 0
        )
        received = jnp.where(valid, updated, received)
    carried = received.reshape(full_shape)
    into_second = decay_first * carried + first_end
    keep = jnp.where(sub_index == 0, carried, into_second)
    got = swapped(jnp.where(sub_index == 0, into_second, carried), "sub")
    low = jnp.where(sub_index == 0, keep, got)
    high = jnp.where(sub_index == 0, got, keep)
    incoming = jnp.stack([low, high], 2).reshape(set_groups, pairs, state, 128)

    out_len = min(256, own)
    return pl.pallas_call(
        out_kernel,
        grid=(set_groups, own // out_len),
        in_specs=[
            pl.BlockSpec((out_len, group_width), lambda g, c: (c, g)),
            pl.BlockSpec((1, out_len, state), lambda g, c: (g, c, 0)),
            pl.BlockSpec((1, out_len, per_group), lambda g, c: (g, c, 0)),
            pl.BlockSpec((1, pairs, state, 128), lambda g, c: (g, 0, 0, 0)),
            pl.BlockSpec((out_len, group_width), lambda g, c: (c, g)),
            pl.BlockSpec((1, group_width), lambda g, c: (0, g)),
        ],
        out_specs=pl.BlockSpec((out_len, group_width), lambda g, c: (c, g)),
        out_shape=jax.ShapeDtypeStruct((own, channels), jnp.bfloat16),
        scratch_shapes=[pltpu.VMEM((out_len, group_width), F32)],
    )(y_local, c_cols, cum_device.transpose(0, 2, 1), incoming, z_gate, norm_w[None, :])


def solution(mesh):
    in_specs = (
        P(("groups", "ctx"), "head"),
        P(None, "head", "sub", ("groups", "ctx")),
        P(("groups", "ctx", "sub"), "head"),
        P("head", ("groups", "ctx")),
        P(None, "head"),
        P("head"),
        P(None, None, "head", None),
        P(None, "head", None),
        P("head"),
        P("head"),
        P("head"),
        P("head"),
    )
    out_specs = P(("groups", "ctx", "sub"), "head")
    return jax.shard_map(
        per_device, mesh=mesh, in_specs=in_specs, out_specs=out_specs, check_vma=False
    )
```

```python
import jax
import jax.numpy as jnp
from jax import lax
from jax.experimental import pallas as pl
from jax.experimental.pallas import tpu as pltpu
from jax.sharding import PartitionSpec as P

HEADS = 128
HEAD_DIM = 64
GROUPS = 8
CONV_K = 4


HIGHEST = lax.Precision.HIGHEST
F32 = jnp.float32


def passed_along(x, axis, by):
    length = lax.axis_size(axis)
    pairs = [(i, i + by) for i in range(length) if 0 <= i + by < length]
    return lax.ppermute(x, axis, pairs)


def swapped(x, axis):
    return lax.ppermute(x, axis, [(0, 1), (1, 0)])


def conv_rows(padded, weights, bias_row):
    sequence_length = padded.shape[0] - (CONV_K - 1)
    total = jnp.zeros((sequence_length, padded.shape[1]), jnp.float32) + bias_row[None, :]
    for tap_index in range(CONV_K):
        total = total + weights[tap_index][None, :] * padded[
            tap_index : tap_index + sequence_length
        ].astype(jnp.float32)
    return jax.nn.silu(total)


def conv_cols(padded, weights, bias_block):
    sequence_length = padded.shape[-1] - (CONV_K - 1)
    total = jnp.zeros(padded.shape[:-1] + (sequence_length,), jnp.float32) + bias_block[..., None]
    for tap_index in range(CONV_K):
        total = total + weights[tap_index][..., None] * padded[
            ..., tap_index : tap_index + sequence_length
        ].astype(jnp.float32)
    return jax.nn.silu(total)


def dot(a, b):
    return jnp.dot(a, b, precision=HIGHEST, preferred_element_type=F32)


def split(a):
    high = a.astype(jnp.bfloat16)
    return high, (a - high.astype(F32)).astype(jnp.bfloat16)


def dot3(a_parts, b_parts):
    a_high, a_low = a_parts
    b_high, b_low = b_parts
    flat = lambda u, v: jnp.dot(u, v, preferred_element_type=F32)
    return flat(a_high, b_high) + (flat(a_high, b_low) + flat(a_low, b_high))


def pair_columns(cumc, pair, rows):
    left = lax.broadcasted_iota(jnp.int32, (1, 128), 1) < HEAD_DIM
    return jnp.where(
        left,
        jnp.broadcast_to(cumc[:, 2 * pair : 2 * pair + 1], (rows, 128)),
        jnp.broadcast_to(cumc[:, 2 * pair + 1 : 2 * pair + 2], (rows, 128)),
    )


def scan_kernel(xc_ref, ct_ref, b_ref, cumr_ref, cumc_ref, stp_ref, dsk_ref, y_ref, e_ref):
    chunk = pl.program_id(1)
    block_len = xc_ref.shape[0]
    pairs = e_ref.shape[0]
    heads = 2 * pairs

    @pl.when(chunk == 0)
    def _():
        e_ref[...] = jnp.zeros_like(e_ref)

    ct = split(ct_ref[0])
    bm = b_ref[0]
    scores = dot3(ct, split(bm))
    rows = lax.broadcasted_iota(jnp.int32, (block_len, block_len), 0)
    cols = lax.broadcasted_iota(jnp.int32, (block_len, block_len), 1)
    causal = rows >= cols
    cumr = cumr_ref[0]
    cumc = cumc_ref[0]
    stp = stp_ref[0]
    left = lax.broadcasted_iota(jnp.int32, (1, 128), 1) < HEAD_DIM
    for pair in range(pairs):
        lanes = slice(pair * 128, (pair + 1) * 128)
        xp = xc_ref[:, lanes]
        xs = split(xp)
        s_old = e_ref[pair]
        ys = []
        us = []
        for side in range(2):
            head = 2 * pair + side
            dq = jnp.broadcast_to(cumc[:, head : head + 1], (block_len, block_len))
            ck = cumr[head : head + 1, :]
            sk = stp[head : head + 1, :]
            dec = jnp.exp(jnp.where(causal, dq - ck, -jnp.inf))
            ys.append(dot3(split(scores * dec * sk), xs))
            wk = jnp.exp(dq[block_len - 1 : block_len, :] - ck) * sk
            us.append(dot3(split(bm * wk), xs))
        cq = pair_columns(cumc, pair, block_len)
        inflow = dot3(ct, split(s_old)) * jnp.exp(cq)
        y = jnp.where(left, ys[0], ys[1]) + inflow
        y_ref[:, lanes] = y + xp * dsk_ref[:, lanes]
        e_ref[pair] = jnp.exp(cq[block_len - 1 : block_len, :]) * s_old + jnp.where(
            left, us[0], us[1]
        )


def end_kernel(xc_ref, b_ref, wk_ref, e_ref):
    pairs = e_ref.shape[1]
    bm = b_ref[0]
    wk = wk_ref[0]
    left = lax.broadcasted_iota(jnp.int32, (1, 128), 1) < HEAD_DIM
    for pair in range(pairs):
        xs = split(xc_ref[:, pair * 128 : (pair + 1) * 128])
        us = [
            dot3(split(bm * wk[2 * pair + side : 2 * pair + side + 1, :]), xs) for side in range(2)
        ]
        e_ref[0, pair] = jnp.where(left, us[0], us[1])


def end_pair_kernel(xa_ref, xb_ref, ba_ref, bb_ref, wa_ref, wb_ref, ea_ref, eb_ref):
    end_kernel(xa_ref, ba_ref, wa_ref, ea_ref)
    end_kernel(xb_ref, bb_ref, wb_ref, eb_ref)


def out_kernel(y_ref, ct_ref, cumc_ref, v_ref, z_ref, nw_ref, o_ref, g_ref):
    pairs = v_ref.shape[1]
    heads = 2 * pairs
    ct = split(ct_ref[0])
    cumc = cumc_ref[0]
    total = jnp.zeros((y_ref.shape[0], 128), F32)
    for pair in range(pairs):
        lanes = slice(pair * 128, (pair + 1) * 128)
        cq = pair_columns(cumc, pair, y_ref.shape[0])
        y = y_ref[:, lanes] + dot3(ct, split(v_ref[0, pair])) * jnp.exp(cq)
        z = z_ref[:, lanes].astype(F32)
        gated = y * (z / (1.0 + jnp.exp(-z)))
        g_ref[:, lanes] = gated
        total = total + gated * gated
    mean_square = jnp.sum(total, axis=-1, keepdims=True) / g_ref.shape[1]
    o_ref[...] = (g_ref[...] * lax.rsqrt(mean_square + 1e-05) * nw_ref[...]).astype(o_ref.dtype)


def per_device(
    x_raw,
    bc_raw,
    z_gate,
    dt_raw,
    conv_x_w,
    conv_x_b,
    conv_bc_w,
    conv_bc_b,
    dt_bias,
    a_log,
    d_skip,
    norm_w,
):
    tokens = x_raw.shape[0]
    heads_dev = dt_raw.shape[0]
    per_group = HEADS // GROUPS
    set_groups = heads_dev // per_group
    pairs = per_group // 2
    group_width = per_group * HEAD_DIM
    nsub = lax.axis_size("sub")
    ctx_size = lax.axis_size("ctx")
    sub_index = lax.axis_index("sub")
    own = tokens // nsub
    half = bc_raw.shape[2]
    state = half * nsub
    channels = heads_dev * HEAD_DIM
    rim_len = CONV_K - 1

    bc_tail = bc_raw[..., tokens - rim_len :]
    rims = passed_along(
        jnp.concatenate(
            [x_raw[tokens - rim_len :], bc_tail.reshape(-1, rim_len).transpose(1, 0)], 1
        ),
        "ctx",
        1,
    )
    x_rim = rims[:, :channels]
    bc_rim = rims[:, channels:].transpose(1, 0).reshape(bc_tail.shape)
    x_pad = jnp.concatenate([x_rim, x_raw], 0)
    x_own = conv_rows(
        lax.dynamic_slice_in_dim(x_pad, sub_index * own, own + rim_len, 0), conv_x_w, conv_x_b
    )
    x_other = conv_rows(
        lax.dynamic_slice_in_dim(x_pad, (1 - sub_index) * own, own + rim_len, 0),
        conv_x_w,
        conv_x_b,
    )
    bc_weights = lax.dynamic_slice_in_dim(conv_bc_w, sub_index * half, half, 3)
    bc_bias = lax.dynamic_slice_in_dim(conv_bc_b, sub_index * half, half, 2)
    bc_conv = conv_cols(jnp.concatenate([bc_rim, bc_raw], 3), bc_weights, bc_bias)
    bc_mine = lax.dynamic_slice_in_dim(bc_conv, sub_index * own, own, 3)
    bc_theirs = swapped(lax.dynamic_slice_in_dim(bc_conv, (1 - sub_index) * own, own, 3), "sub")
    bc_own = jnp.stack(
        [
            jnp.where(sub_index == 0, bc_mine, bc_theirs),
            jnp.where(sub_index == 0, bc_theirs, bc_mine),
        ],
        2,
    ).reshape(2, set_groups, state, own)
    b_rows = bc_own[0]
    c_cols = bc_own[1].transpose(0, 2, 1)

    step_sizes = jax.nn.softplus(dt_raw + dt_bias[:, None])
    log_decay = -jnp.exp(a_log)[:, None] * step_sizes
    half_totals = jnp.exp(log_decay.reshape(heads_dev, nsub, own).sum(-1))
    step_own = lax.dynamic_slice_in_dim(step_sizes, sub_index * own, own, 1)
    decay_own = lax.dynamic_slice_in_dim(log_decay, sub_index * own, own, 1)
    block_len = min(128, own)
    blocks = own // block_len
    upper = (
        lax.broadcasted_iota(jnp.int32, (block_len, block_len), 0)
        <= lax.broadcasted_iota(jnp.int32, (block_len, block_len), 1)
    ).astype(F32)
    cum_local = jnp.einsum(
        "hct,tu->hcu", decay_own.reshape(heads_dev, blocks, block_len), upper, precision=HIGHEST
    )
    block_totals = cum_local[..., -1]
    offsets = jnp.cumsum(block_totals, axis=-1) - block_totals
    cum_device = (cum_local + offsets[..., None]).reshape(set_groups, per_group, own)
    cum_rows = cum_local.reshape(set_groups, per_group, own)
    cum_cols = cum_rows.transpose(0, 2, 1)
    step_rows = step_own.reshape(set_groups, per_group, own)
    skip_row = jnp.repeat(d_skip, HEAD_DIM)[None, :]

    cum_all = jnp.einsum(
        "hjct,tu->hjcu",
        log_decay.reshape(heads_dev, nsub, blocks, block_len),
        upper,
        precision=HIGHEST,
    )
    all_totals = cum_all[..., -1]
    cum_all = (cum_all + (jnp.cumsum(all_totals, axis=-1) - all_totals)[..., None]).reshape(
        heads_dev, nsub, own
    )
    to_end = jnp.exp(cum_all[..., own - 1 :] - cum_all) * step_sizes.reshape(heads_dev, nsub, own)
    to_end = to_end.reshape(set_groups, per_group, tokens)

    def end_states(x_pair, start, count):
        x_spec = pl.BlockSpec((own, group_width), lambda g: (0, g + start))
        b_spec = pl.BlockSpec((1, half, own), lambda g: (g + start, 0, 0))
        w_spec = pl.BlockSpec((1, per_group, own), lambda g: (g + start, 0, 0))
        e_spec = pl.BlockSpec((1, pairs, half, 128), lambda g: (g, 0, 0, 0))
        return pl.pallas_call(
            end_pair_kernel,
            grid=(count,),
            in_specs=[x_spec, x_spec, b_spec, b_spec, w_spec, w_spec],
            out_specs=[e_spec, e_spec],
            out_shape=[jax.ShapeDtypeStruct((count, pairs, half, 128), F32)] * 2,
        )(
            *x_pair,
            *(
                lax.dynamic_slice_in_dim(bc_conv[0], at * own, own, 2)
                for at in (sub_index, 1 - sub_index)
            ),
            *(
                lax.dynamic_slice_in_dim(to_end, at * own, own, 2)
                for at in (sub_index, 1 - sub_index)
            ),
        )

    def pair_layout(values):
        return jnp.repeat(values.reshape(set_groups, pairs, 2), HEAD_DIM, axis=-1)[:, :, None, :]

    decay_first = pair_layout(half_totals[:, 0])
    decay_second = pair_layout(half_totals[:, 1])
    chip_decay = decay_first * decay_second

    def chip_ends(x_pair, start, count):
        own_end, other_end = end_states(x_pair, start, count)
        first = jnp.where(sub_index == 0, own_end, other_end)
        second = jnp.where(sub_index == 0, other_end, own_end)
        return first, decay_second[start : start + count] * first + second

    pieces = 2 if (set_groups * pairs) % 2 == 0 else 1
    rounds = ctx_size + pieces - 2
    early = set_groups // 2 if (pieces == 2 and set_groups % 2 == 0 and rounds > 0) else set_groups
    first_end, chip_end = chip_ends((x_own, x_other), 0, early)
    ctx_index = lax.axis_index("ctx")
    scan_inputs = (x_own, c_cols, b_rows, cum_rows, cum_cols, step_rows, skip_row)

    def scan_group(group, inputs, target):
        count = len(inputs)
        extra = {} if target is None else {"input_output_aliases": {count: 0}}
        tile = pl.BlockSpec((block_len, group_width), lambda g, c: (c, group))
        in_specs = [
            tile,
            pl.BlockSpec((1, block_len, state), lambda g, c: (group, c, 0)),
            pl.BlockSpec((1, state, block_len), lambda g, c: (group, 0, c)),
            pl.BlockSpec((1, per_group, block_len), lambda g, c: (group, 0, c)),
            pl.BlockSpec((1, block_len, per_group), lambda g, c: (group, c, 0)),
            pl.BlockSpec((1, per_group, block_len), lambda g, c: (group, 0, c)),
            pl.BlockSpec((1, group_width), lambda g, c: (0, group)),
        ]
        operands = tuple(inputs)
        kernel = scan_kernel
        if target is not None:
            in_specs = in_specs + [pl.BlockSpec(memory_space=pl.ANY)]
            operands = operands + (target,)
            kernel = lambda *refs: scan_kernel(*refs[:count], *refs[count + 1 :])
        return pl.pallas_call(
            kernel,
            grid=(1, blocks),
            in_specs=in_specs,
            out_specs=tile,
            out_shape=jax.ShapeDtypeStruct((own, channels), F32),
            scratch_shapes=[pltpu.VMEM((pairs, state, 128), F32)],
            **extra,
        )(*operands)

    piece_shape = (pieces, set_groups * pairs // pieces, half, 128)
    full_shape = (set_groups, pairs, half, 128)
    decay_pieces = jnp.broadcast_to(chip_decay, full_shape).reshape(piece_shape)
    if early == set_groups:
        end_pieces = chip_end.reshape(piece_shape)
    else:
        end_pieces = chip_end.reshape((1,) + piece_shape[1:])
    received = jnp.zeros(piece_shape, F32)
    y_local = None
    placed = [min(group, max(rounds, 1) - 1) for group in range(set_groups)]
    for step_index in range(max(rounds, 1)):
        send_at = jnp.clip(step_index - ctx_index, 0, pieces - 1)
        outgoing = lax.dynamic_index_in_dim(
            end_pieces, send_at, 0, keepdims=False
        ) + lax.dynamic_index_in_dim(decay_pieces, send_at, 0, keepdims=False) * (
            lax.dynamic_index_in_dim(received, send_at, 0, keepdims=False)
        )
        held = scan_inputs
        x_pair = (x_own, x_other)
        if any(p == step_index for p in placed):
            outgoing, held, x_pair = lax.optimization_barrier((outgoing, scan_inputs, x_pair))
        if rounds > 0:
            arrived = passed_along(outgoing, "ctx", 1)
        for group in range(set_groups):
            if placed[group] == step_index:
                y_local = scan_group(group, held, y_local)
        late = None
        if step_index == 0 and early < set_groups:
            late = chip_ends(x_pair, early, set_groups - early)
        if rounds == 0:
            break
        if any(p == step_index for p in placed):
            arrived, y_local, late = lax.optimization_barrier((arrived, y_local, late))
        if late is not None:
            first_end = jnp.concatenate([first_end, late[0]], 0)
            chip_end = jnp.concatenate([chip_end, late[1]], 0)
            end_pieces = chip_end.reshape(piece_shape)
        recv_at = step_index - ctx_index + 1
        valid = (recv_at >= 0) & (recv_at < pieces) & (ctx_index > 0)
        updated = lax.dynamic_update_index_in_dim(
            received, arrived, jnp.clip(recv_at, 0, pieces - 1), 0
        )
        received = jnp.where(valid, updated, received)
    carried = received.reshape(full_shape)
    into_second = decay_first * carried + first_end
    keep = jnp.where(sub_index == 0, carried, into_second)
    got = swapped(jnp.where(sub_index == 0, into_second, carried), "sub")
    low = jnp.where(sub_index == 0, keep, got)
    high = jnp.where(sub_index == 0, got, keep)
    incoming = jnp.stack([low, high], 2).reshape(set_groups, pairs, state, 128)

    out_len = min(256, own)
    return pl.pallas_call(
        out_kernel,
        grid=(set_groups, own // out_len),
        in_specs=[
            pl.BlockSpec((out_len, group_width), lambda g, c: (c, g)),
            pl.BlockSpec((1, out_len, state), lambda g, c: (g, c, 0)),
            pl.BlockSpec((1, out_len, per_group), lambda g, c: (g, c, 0)),
            pl.BlockSpec((1, pairs, state, 128), lambda g, c: (g, 0, 0, 0)),
            pl.BlockSpec((out_len, group_width), lambda g, c: (c, g)),
            pl.BlockSpec((1, group_width), lambda g, c: (0, g)),
        ],
        out_specs=pl.BlockSpec((out_len, group_width), lambda g, c: (c, g)),
        out_shape=jax.ShapeDtypeStruct((own, channels), jnp.bfloat16),
        scratch_shapes=[pltpu.VMEM((out_len, group_width), F32)],
    )(y_local, c_cols, cum_device.transpose(0, 2, 1), incoming, z_gate, norm_w[None, :])


def solution(mesh):
    in_specs = (
        P(("groups", "ctx"), "head"),
        P(None, "head", "sub", ("groups", "ctx")),
        P(("groups", "ctx", "sub"), "head"),
        P("head", ("groups", "ctx")),
        P(None, "head"),
        P("head"),
        P(None, None, "head", None),
        P(None, "head", None),
        P("head"),
        P("head"),
        P("head"),
        P("head"),
    )
    out_specs = P(("groups", "ctx", "sub"), "head")
    return jax.shard_map(
        per_device, mesh=mesh, in_specs=in_specs, out_specs=out_specs, check_vma=False
    )
```

```python
import jax
import jax.numpy as jnp
from jax import lax
from jax.experimental import pallas as pl
from jax.experimental.pallas import tpu as pltpu
from jax.sharding import PartitionSpec as P

HEADS = 128
HEAD_DIM = 64
GROUPS = 8
CONV_K = 4


HIGHEST = lax.Precision.HIGHEST
F32 = jnp.float32


def passed_along(x, axis, by):
    length = lax.axis_size(axis)
    pairs = [(i, i + by) for i in range(length) if 0 <= i + by < length]
    return lax.ppermute(x, axis, pairs)


def swapped(x, axis):
    return lax.ppermute(x, axis, [(0, 1), (1, 0)])


def conv_rows(padded, weights, bias_row):
    sequence_length = padded.shape[0] - (CONV_K - 1)
    total = jnp.zeros((sequence_length, padded.shape[1]), jnp.float32) + bias_row[None, :]
    for tap_index in range(CONV_K):
        total = total + weights[tap_index][None, :] * padded[
            tap_index : tap_index + sequence_length
        ].astype(jnp.float32)
    return jax.nn.silu(total)


def conv_cols(padded, weights, bias_block):
    sequence_length = padded.shape[-1] - (CONV_K - 1)
    total = jnp.zeros(padded.shape[:-1] + (sequence_length,), jnp.float32) + bias_block[..., None]
    for tap_index in range(CONV_K):
        total = total + weights[tap_index][..., None] * padded[
            ..., tap_index : tap_index + sequence_length
        ].astype(jnp.float32)
    return jax.nn.silu(total)


def dot(a, b):
    return jnp.dot(a, b, precision=HIGHEST, preferred_element_type=F32)


def split(a):
    high = a.astype(jnp.bfloat16)
    return high, (a - high.astype(F32)).astype(jnp.bfloat16)


def dot3(a_parts, b_parts):
    a_high, a_low = a_parts
    b_high, b_low = b_parts
    flat = lambda u, v: jnp.dot(u, v, preferred_element_type=F32)
    return flat(a_high, b_high) + (flat(a_high, b_low) + flat(a_low, b_high))


def pair_columns(cumc, pair, rows):
    left = lax.broadcasted_iota(jnp.int32, (1, 128), 1) < HEAD_DIM
    return jnp.where(
        left,
        jnp.broadcast_to(cumc[:, 2 * pair : 2 * pair + 1], (rows, 128)),
        jnp.broadcast_to(cumc[:, 2 * pair + 1 : 2 * pair + 2], (rows, 128)),
    )


def scan_kernel(xa_ref, xb_ref, flag_ref, ct_ref, b_ref, cumr_ref, cumc_ref, stp_ref, dsk_ref, y_ref, e_ref):
    chunk = pl.program_id(1)
    block_len = xa_ref.shape[0]
    first = flag_ref[0:1, 0:1] > 0.5
    pairs = e_ref.shape[0]
    heads = 2 * pairs

    @pl.when(chunk == 0)
    def _():
        e_ref[...] = jnp.zeros_like(e_ref)

    ct = split(ct_ref[0])
    bm = b_ref[0]
    scores = dot3(ct, split(bm))
    rows = lax.broadcasted_iota(jnp.int32, (block_len, block_len), 0)
    cols = lax.broadcasted_iota(jnp.int32, (block_len, block_len), 1)
    causal = rows >= cols
    cumr = cumr_ref[0]
    cumc = cumc_ref[0]
    stp = stp_ref[0]
    left = lax.broadcasted_iota(jnp.int32, (1, 128), 1) < HEAD_DIM
    for pair in range(pairs):
        lanes = slice(pair * 128, (pair + 1) * 128)
        xp = jnp.where(first, xa_ref[:, lanes], xb_ref[:, lanes])
        xs = split(xp)
        s_old = e_ref[pair]
        ys = []
        us = []
        for side in range(2):
            head = 2 * pair + side
            dq = jnp.broadcast_to(cumc[:, head : head + 1], (block_len, block_len))
            ck = cumr[head : head + 1, :]
            sk = stp[head : head + 1, :]
            dec = jnp.exp(jnp.where(causal, dq - ck, -jnp.inf))
            ys.append(dot3(split(scores * dec * sk), xs))
            wk = jnp.exp(dq[block_len - 1 : block_len, :] - ck) * sk
            us.append(dot3(split(bm * wk), xs))
        cq = pair_columns(cumc, pair, block_len)
        inflow = dot3(ct, split(s_old)) * jnp.exp(cq)
        y = jnp.where(left, ys[0], ys[1]) + inflow
        y_ref[:, lanes] = y + xp * dsk_ref[:, lanes]
        e_ref[pair] = jnp.exp(cq[block_len - 1 : block_len, :]) * s_old + jnp.where(
            left, us[0], us[1]
        )


def end_kernel(xc_ref, b_ref, wk_ref, e_ref):
    pairs = e_ref.shape[1]
    bm = b_ref[0]
    wk = wk_ref[0]
    left = lax.broadcasted_iota(jnp.int32, (1, 128), 1) < HEAD_DIM
    for pair in range(pairs):
        xs = split(xc_ref[:, pair * 128 : (pair + 1) * 128])
        us = [
            dot3(split(bm * wk[2 * pair + side : 2 * pair + side + 1, :]), xs) for side in range(2)
        ]
        e_ref[0, pair] = jnp.where(left, us[0], us[1])


def end_pair_kernel(xa_ref, xb_ref, ba_ref, bb_ref, wa_ref, wb_ref, ea_ref, eb_ref):
    end_kernel(xa_ref, ba_ref, wa_ref, ea_ref)
    end_kernel(xb_ref, bb_ref, wb_ref, eb_ref)


def out_kernel(y_ref, ct_ref, cumc_ref, v_ref, z_ref, nw_ref, o_ref, g_ref):
    pairs = v_ref.shape[1]
    heads = 2 * pairs
    ct = split(ct_ref[0])
    cumc = cumc_ref[0]
    total = jnp.zeros((y_ref.shape[0], 128), F32)
    for pair in range(pairs):
        lanes = slice(pair * 128, (pair + 1) * 128)
        cq = pair_columns(cumc, pair, y_ref.shape[0])
        y = y_ref[:, lanes] + dot3(ct, split(v_ref[0, pair])) * jnp.exp(cq)
        z = z_ref[:, lanes].astype(F32)
        gated = y * (z / (1.0 + jnp.exp(-z)))
        g_ref[:, lanes] = gated
        total = total + gated * gated
    mean_square = jnp.sum(total, axis=-1, keepdims=True) / g_ref.shape[1]
    o_ref[...] = (g_ref[...] * lax.rsqrt(mean_square + 1e-05) * nw_ref[...]).astype(o_ref.dtype)


def per_device(
    x_raw,
    bc_raw,
    z_gate,
    dt_raw,
    conv_x_w,
    conv_x_b,
    conv_bc_w,
    conv_bc_b,
    dt_bias,
    a_log,
    d_skip,
    norm_w,
):
    tokens = x_raw.shape[0]
    heads_dev = dt_raw.shape[0]
    per_group = HEADS // GROUPS
    set_groups = heads_dev // per_group
    pairs = per_group // 2
    group_width = per_group * HEAD_DIM
    nsub = lax.axis_size("sub")
    ctx_size = lax.axis_size("ctx")
    sub_index = lax.axis_index("sub")
    own = tokens // nsub
    half = bc_raw.shape[2]
    state = half * nsub
    channels = heads_dev * HEAD_DIM
    rim_len = CONV_K - 1

    bc_tail = bc_raw[..., tokens - rim_len :]
    rims = passed_along(
        jnp.concatenate(
            [x_raw[tokens - rim_len :], bc_tail.reshape(-1, rim_len).transpose(1, 0)], 1
        ),
        "ctx",
        1,
    )
    x_rim = rims[:, :channels]
    bc_rim = rims[:, channels:].transpose(1, 0).reshape(bc_tail.shape)
    x_first = conv_rows(jnp.concatenate([x_rim, x_raw[:own]], 0), conv_x_w, conv_x_b)
    x_second = conv_rows(x_raw[own - rim_len :], conv_x_w, conv_x_b)
    first_flag = jnp.full((8, 128), sub_index == 0, F32)
    bc_weights = lax.dynamic_slice_in_dim(conv_bc_w, sub_index * half, half, 3)
    bc_bias = lax.dynamic_slice_in_dim(conv_bc_b, sub_index * half, half, 2)
    bc_conv = conv_cols(jnp.concatenate([bc_rim, bc_raw], 3), bc_weights, bc_bias)
    bc_mine = lax.dynamic_slice_in_dim(bc_conv, sub_index * own, own, 3)
    bc_theirs = swapped(lax.dynamic_slice_in_dim(bc_conv, (1 - sub_index) * own, own, 3), "sub")
    bc_own = jnp.stack(
        [
            jnp.where(sub_index == 0, bc_mine, bc_theirs),
            jnp.where(sub_index == 0, bc_theirs, bc_mine),
        ],
        2,
    ).reshape(2, set_groups, state, own)
    b_rows = bc_own[0]
    c_cols = bc_own[1].transpose(0, 2, 1)

    step_sizes = jax.nn.softplus(dt_raw + dt_bias[:, None])
    log_decay = -jnp.exp(a_log)[:, None] * step_sizes
    half_totals = jnp.exp(log_decay.reshape(heads_dev, nsub, own).sum(-1))
    step_own = lax.dynamic_slice_in_dim(step_sizes, sub_index * own, own, 1)
    decay_own = lax.dynamic_slice_in_dim(log_decay, sub_index * own, own, 1)
    block_len = min(128, own)
    blocks = own // block_len
    upper = (
        lax.broadcasted_iota(jnp.int32, (block_len, block_len), 0)
        <= lax.broadcasted_iota(jnp.int32, (block_len, block_len), 1)
    ).astype(F32)
    cum_local = jnp.einsum(
        "hct,tu->hcu", decay_own.reshape(heads_dev, blocks, block_len), upper, precision=HIGHEST
    )
    block_totals = cum_local[..., -1]
    offsets = jnp.cumsum(block_totals, axis=-1) - block_totals
    cum_device = (cum_local + offsets[..., None]).reshape(set_groups, per_group, own)
    cum_rows = cum_local.reshape(set_groups, per_group, own)
    cum_cols = cum_rows.transpose(0, 2, 1)
    step_rows = step_own.reshape(set_groups, per_group, own)
    skip_row = jnp.repeat(d_skip, HEAD_DIM)[None, :]

    cum_all = jnp.einsum(
        "hjct,tu->hjcu",
        log_decay.reshape(heads_dev, nsub, blocks, block_len),
        upper,
        precision=HIGHEST,
    )
    all_totals = cum_all[..., -1]
    cum_all = (cum_all + (jnp.cumsum(all_totals, axis=-1) - all_totals)[..., None]).reshape(
        heads_dev, nsub, own
    )
    to_end = jnp.exp(cum_all[..., own - 1 :] - cum_all) * step_sizes.reshape(heads_dev, nsub, own)
    to_end = to_end.reshape(set_groups, per_group, tokens)

    def end_states(x_pair, start, count):
        x_spec = pl.BlockSpec((own, group_width), lambda g: (0, g + start))
        b_spec = pl.BlockSpec((1, half, own), lambda g: (g + start, 0, 0))
        w_spec = pl.BlockSpec((1, per_group, own), lambda g: (g + start, 0, 0))
        e_spec = pl.BlockSpec((1, pairs, half, 128), lambda g: (g, 0, 0, 0))
        return pl.pallas_call(
            end_pair_kernel,
            grid=(count,),
            in_specs=[x_spec, x_spec, b_spec, b_spec, w_spec, w_spec],
            out_specs=[e_spec, e_spec],
            out_shape=[jax.ShapeDtypeStruct((count, pairs, half, 128), F32)] * 2,
        )(
            *x_pair,
            *(
                lax.dynamic_slice_in_dim(bc_conv[0], at * own, own, 2)
                for at in (0, 1)
            ),
            *(
                lax.dynamic_slice_in_dim(to_end, at * own, own, 2)
                for at in (0, 1)
            ),
        )

    def pair_layout(values):
        return jnp.repeat(values.reshape(set_groups, pairs, 2), HEAD_DIM, axis=-1)[:, :, None, :]

    decay_first = pair_layout(half_totals[:, 0])
    decay_second = pair_layout(half_totals[:, 1])
    chip_decay = decay_first * decay_second

    def chip_ends(x_pair, start, count):
        first, second = end_states(x_pair, start, count)
        return first, decay_second[start : start + count] * first + second

    pieces = 2 if (set_groups * pairs) % 2 == 0 else 1
    rounds = ctx_size + pieces - 2
    early = set_groups // 2 if (pieces == 2 and set_groups % 2 == 0 and rounds > 0) else set_groups
    first_end, chip_end = chip_ends((x_first, x_second), 0, early)
    ctx_index = lax.axis_index("ctx")
    scan_inputs = (x_first, x_second, first_flag, c_cols, b_rows, cum_rows, cum_cols, step_rows, skip_row)

    def scan_group(group, inputs, target):
        count = len(inputs)
        extra = {} if target is None else {"input_output_aliases": {count: 0}}
        tile = pl.BlockSpec((block_len, group_width), lambda g, c: (c, group))
        in_specs = [
            tile,
            tile,
            pl.BlockSpec((8, 128), lambda g, c: (0, 0)),
            pl.BlockSpec((1, block_len, state), lambda g, c: (group, c, 0)),
            pl.BlockSpec((1, state, block_len), lambda g, c: (group, 0, c)),
            pl.BlockSpec((1, per_group, block_len), lambda g, c: (group, 0, c)),
            pl.BlockSpec((1, block_len, per_group), lambda g, c: (group, c, 0)),
            pl.BlockSpec((1, per_group, block_len), lambda g, c: (group, 0, c)),
            pl.BlockSpec((1, group_width), lambda g, c: (0, group)),
        ]
        operands = tuple(inputs)
        kernel = scan_kernel
        if target is not None:
            in_specs = in_specs + [pl.BlockSpec(memory_space=pl.ANY)]
            operands = operands + (target,)
            kernel = lambda *refs: scan_kernel(*refs[:count], *refs[count + 1 :])
        return pl.pallas_call(
            kernel,
            grid=(1, blocks),
            in_specs=in_specs,
            out_specs=tile,
            out_shape=jax.ShapeDtypeStruct((own, channels), F32),
            scratch_shapes=[pltpu.VMEM((pairs, state, 128), F32)],
            **extra,
        )(*operands)

    piece_shape = (pieces, set_groups * pairs // pieces, half, 128)
    full_shape = (set_groups, pairs, half, 128)
    decay_pieces = jnp.broadcast_to(chip_decay, full_shape).reshape(piece_shape)
    if early == set_groups:
        end_pieces = chip_end.reshape(piece_shape)
    else:
        end_pieces = chip_end.reshape((1,) + piece_shape[1:])
    received = jnp.zeros(piece_shape, F32)
    y_local = None
    placed = [min(group, max(rounds, 1) - 1) for group in range(set_groups)]
    for step_index in range(max(rounds, 1)):
        send_at = jnp.clip(step_index - ctx_index, 0, pieces - 1)
        outgoing = lax.dynamic_index_in_dim(
            end_pieces, send_at, 0, keepdims=False
        ) + lax.dynamic_index_in_dim(decay_pieces, send_at, 0, keepdims=False) * (
            lax.dynamic_index_in_dim(received, send_at, 0, keepdims=False)
        )
        held = scan_inputs
        x_pair = (x_first, x_second)
        if any(p == step_index for p in placed):
            outgoing, held, x_pair = lax.optimization_barrier((outgoing, scan_inputs, x_pair))
        if rounds > 0:
            arrived = passed_along(outgoing, "ctx", 1)
        for group in range(set_groups):
            if placed[group] == step_index:
                y_local = scan_group(group, held, y_local)
        late = None
        if step_index == 0 and early < set_groups:
            late = chip_ends(x_pair, early, set_groups - early)
        if rounds == 0:
            break
        if any(p == step_index for p in placed):
            arrived, y_local, late = lax.optimization_barrier((arrived, y_local, late))
        if late is not None:
            first_end = jnp.concatenate([first_end, late[0]], 0)
            chip_end = jnp.concatenate([chip_end, late[1]], 0)
            end_pieces = chip_end.reshape(piece_shape)
        recv_at = step_index - ctx_index + 1
        valid = (recv_at >= 0) & (recv_at < pieces) & (ctx_index > 0)
        updated = lax.dynamic_update_index_in_dim(
            received, arrived, jnp.clip(recv_at, 0, pieces - 1), 0
        )
        received = jnp.where(valid, updated, received)
    carried = received.reshape(full_shape)
    into_second = decay_first * carried + first_end
    keep = jnp.where(sub_index == 0, carried, into_second)
    got = swapped(jnp.where(sub_index == 0, into_second, carried), "sub")
    low = jnp.where(sub_index == 0, keep, got)
    high = jnp.where(sub_index == 0, got, keep)
    incoming = jnp.stack([low, high], 2).reshape(set_groups, pairs, state, 128)

    out_len = min(256, own)
    return pl.pallas_call(
        out_kernel,
        grid=(set_groups, own // out_len),
        in_specs=[
            pl.BlockSpec((out_len, group_width), lambda g, c: (c, g)),
            pl.BlockSpec((1, out_len, state), lambda g, c: (g, c, 0)),
            pl.BlockSpec((1, out_len, per_group), lambda g, c: (g, c, 0)),
            pl.BlockSpec((1, pairs, state, 128), lambda g, c: (g, 0, 0, 0)),
            pl.BlockSpec((out_len, group_width), lambda g, c: (c, g)),
            pl.BlockSpec((1, group_width), lambda g, c: (0, g)),
        ],
        out_specs=pl.BlockSpec((out_len, group_width), lambda g, c: (c, g)),
        out_shape=jax.ShapeDtypeStruct((own, channels), jnp.bfloat16),
        scratch_shapes=[pltpu.VMEM((out_len, group_width), F32)],
    )(y_local, c_cols, cum_device.transpose(0, 2, 1), incoming, z_gate, norm_w[None, :])


def solution(mesh):
    in_specs = (
        P(("groups", "ctx"), "head"),
        P(None, "head", "sub", ("groups", "ctx")),
        P(("groups", "ctx", "sub"), "head"),
        P("head", ("groups", "ctx")),
        P(None, "head"),
        P("head"),
        P(None, None, "head", None),
        P(None, "head", None),
        P("head"),
        P("head"),
        P("head"),
        P("head"),
    )
    out_specs = P(("groups", "ctx", "sub"), "head")
    return jax.shard_map(
        per_device, mesh=mesh, in_specs=in_specs, out_specs=out_specs, check_vma=False
    )
```

```python
import jax
import jax.numpy as jnp
from jax import lax
from jax.experimental import pallas as pl
from jax.experimental.pallas import tpu as pltpu
from jax.sharding import PartitionSpec as P

HEADS = 128
HEAD_DIM = 64
GROUPS = 8
CONV_K = 4


HIGHEST = lax.Precision.HIGHEST
F32 = jnp.float32


def passed_along(x, axis, by):
    length = lax.axis_size(axis)
    pairs = [(i, i + by) for i in range(length) if 0 <= i + by < length]
    return lax.ppermute(x, axis, pairs)


def swapped(x, axis):
    return lax.ppermute(x, axis, [(0, 1), (1, 0)])


def conv_rows(padded, weights, bias_row):
    sequence_length = padded.shape[0] - (CONV_K - 1)
    total = jnp.zeros((sequence_length, padded.shape[1]), jnp.float32) + bias_row[None, :]
    for tap_index in range(CONV_K):
        total = total + weights[tap_index][None, :] * padded[
            tap_index : tap_index + sequence_length
        ].astype(jnp.float32)
    return jax.nn.silu(total)


def conv_cols(padded, weights, bias_block):
    sequence_length = padded.shape[-1] - (CONV_K - 1)
    total = jnp.zeros(padded.shape[:-1] + (sequence_length,), jnp.float32) + bias_block[..., None]
    for tap_index in range(CONV_K):
        total = total + weights[tap_index][..., None] * padded[
            ..., tap_index : tap_index + sequence_length
        ].astype(jnp.float32)
    return jax.nn.silu(total)


def dot(a, b):
    return jnp.dot(a, b, precision=HIGHEST, preferred_element_type=F32)


def split(a):
    high = a.astype(jnp.bfloat16)
    return high, (a - high.astype(F32)).astype(jnp.bfloat16)


def dot3(a_parts, b_parts):
    a_high, a_low = a_parts
    b_high, b_low = b_parts
    flat = lambda u, v: jnp.dot(u, v, preferred_element_type=F32)
    return flat(a_high, b_high) + (flat(a_high, b_low) + flat(a_low, b_high))


def pair_columns(cumc, pair, rows):
    left = lax.broadcasted_iota(jnp.int32, (1, 128), 1) < HEAD_DIM
    return jnp.where(
        left,
        jnp.broadcast_to(cumc[:, 2 * pair : 2 * pair + 1], (rows, 128)),
        jnp.broadcast_to(cumc[:, 2 * pair + 1 : 2 * pair + 2], (rows, 128)),
    )


def scan_kernel(xc_ref, ct_ref, b_ref, cumr_ref, cumc_ref, stp_ref, dsk_ref, y_ref, e_ref):
    chunk = pl.program_id(1)
    block_len = xc_ref.shape[0]
    pairs = e_ref.shape[0]
    heads = 2 * pairs

    @pl.when(chunk == 0)
    def _():
        e_ref[...] = jnp.zeros_like(e_ref)

    ct = split(ct_ref[0])
    bm = b_ref[0]
    scores = dot3(ct, split(bm))
    rows = lax.broadcasted_iota(jnp.int32, (block_len, block_len), 0)
    cols = lax.broadcasted_iota(jnp.int32, (block_len, block_len), 1)
    causal = rows >= cols
    cumr = cumr_ref[0]
    cumc = cumc_ref[0]
    stp = stp_ref[0]
    left = lax.broadcasted_iota(jnp.int32, (1, 128), 1) < HEAD_DIM
    for pair in range(pairs):
        lanes = slice(pair * 128, (pair + 1) * 128)
        xp = xc_ref[:, lanes]
        xs = split(xp)
        s_old = e_ref[pair]
        ys = []
        us = []
        for side in range(2):
            head = 2 * pair + side
            dq = jnp.broadcast_to(cumc[:, head : head + 1], (block_len, block_len))
            ck = cumr[head : head + 1, :]
            sk = stp[head : head + 1, :]
            dec = jnp.exp(jnp.where(causal, dq - ck, -jnp.inf))
            ys.append(dot3(split(scores * dec * sk), xs))
            wk = jnp.exp(dq[block_len - 1 : block_len, :] - ck) * sk
            us.append(dot3(split(bm * wk), xs))
        cq = pair_columns(cumc, pair, block_len)
        inflow = dot3(ct, split(s_old)) * jnp.exp(cq)
        y = jnp.where(left, ys[0], ys[1]) + inflow
        y_ref[:, lanes] = y + xp * dsk_ref[:, lanes]
        e_ref[pair] = jnp.exp(cq[block_len - 1 : block_len, :]) * s_old + jnp.where(
            left, us[0], us[1]
        )


def end_kernel(xc_ref, b_ref, wk_ref, e_ref):
    pairs = e_ref.shape[1]
    bm = b_ref[0]
    wk = wk_ref[0]
    left = lax.broadcasted_iota(jnp.int32, (1, 128), 1) < HEAD_DIM
    for pair in range(pairs):
        xs = split(xc_ref[:, pair * 128 : (pair + 1) * 128])
        us = [
            dot3(split(bm * wk[2 * pair + side : 2 * pair + side + 1, :]), xs) for side in range(2)
        ]
        e_ref[0, pair] = jnp.where(left, us[0], us[1])


def end_pair_kernel(xa_ref, xb_ref, ba_ref, bb_ref, wa_ref, wb_ref, ea_ref, eb_ref):
    end_kernel(xa_ref, ba_ref, wa_ref, ea_ref)
    end_kernel(xb_ref, bb_ref, wb_ref, eb_ref)


def out_kernel(y_ref, ct_ref, cumc_ref, v_ref, z_ref, nw_ref, o_ref, g_ref):
    pairs = v_ref.shape[1]
    heads = 2 * pairs
    ct = split(ct_ref[0])
    cumc = cumc_ref[0]
    total = jnp.zeros((y_ref.shape[0], 128), F32)
    for pair in range(pairs):
        lanes = slice(pair * 128, (pair + 1) * 128)
        cq = pair_columns(cumc, pair, y_ref.shape[0])
        y = y_ref[:, lanes] + dot3(ct, split(v_ref[0, pair])) * jnp.exp(cq)
        z = z_ref[:, lanes].astype(F32)
        gated = y * (z / (1.0 + jnp.exp(-z)))
        g_ref[:, lanes] = gated
        total = total + gated * gated
    mean_square = jnp.sum(total, axis=-1, keepdims=True) / g_ref.shape[1]
    o_ref[...] = (g_ref[...] * lax.rsqrt(mean_square + 1e-05) * nw_ref[...]).astype(o_ref.dtype)


def per_device(
    x_raw,
    bc_raw,
    z_gate,
    dt_raw,
    conv_x_w,
    conv_x_b,
    conv_bc_w,
    conv_bc_b,
    dt_bias,
    a_log,
    d_skip,
    norm_w,
):
    tokens = x_raw.shape[0]
    heads_dev = dt_raw.shape[0]
    per_group = HEADS // GROUPS
    set_groups = heads_dev // per_group
    pairs = per_group // 2
    group_width = per_group * HEAD_DIM
    nsub = lax.axis_size("sub")
    ctx_size = lax.axis_size("ctx")
    sub_index = lax.axis_index("sub")
    own = tokens // nsub
    half = bc_raw.shape[2]
    state = half * nsub
    channels = heads_dev * HEAD_DIM
    rim_len = CONV_K - 1

    bc_tail = bc_raw[..., tokens - rim_len :]
    rims = passed_along(
        jnp.concatenate(
            [x_raw[tokens - rim_len :], bc_tail.reshape(-1, rim_len).transpose(1, 0)], 1
        ),
        "ctx",
        1,
    )
    x_rim = rims[:, :channels]
    bc_rim = rims[:, channels:].transpose(1, 0).reshape(bc_tail.shape)
    x_pad = jnp.concatenate([x_rim, x_raw], 0)
    x_own = conv_rows(
        lax.dynamic_slice_in_dim(x_pad, sub_index * own, own + rim_len, 0), conv_x_w, conv_x_b
    )
    x_other = conv_rows(
        lax.dynamic_slice_in_dim(x_pad, (1 - sub_index) * own, own + rim_len, 0),
        conv_x_w,
        conv_x_b,
    )
    bc_weights = lax.dynamic_slice_in_dim(conv_bc_w, sub_index * half, half, 3)
    bc_bias = lax.dynamic_slice_in_dim(conv_bc_b, sub_index * half, half, 2)
    bc_conv = conv_cols(jnp.concatenate([bc_rim, bc_raw], 3), bc_weights, bc_bias)
    bc_mine = lax.dynamic_slice_in_dim(bc_conv, sub_index * own, own, 3)
    bc_theirs = swapped(lax.dynamic_slice_in_dim(bc_conv, (1 - sub_index) * own, own, 3), "sub")
    bc_own = jnp.stack(
        [
            jnp.where(sub_index == 0, bc_mine, bc_theirs),
            jnp.where(sub_index == 0, bc_theirs, bc_mine),
        ],
        2,
    ).reshape(2, set_groups, state, own)
    b_rows = bc_own[0]
    c_cols = bc_own[1].transpose(0, 2, 1)

    step_sizes = jax.nn.softplus(dt_raw + dt_bias[:, None])
    log_decay = -jnp.exp(a_log)[:, None] * step_sizes
    half_totals = jnp.exp(log_decay.reshape(heads_dev, nsub, own).sum(-1))
    step_own = lax.dynamic_slice_in_dim(step_sizes, sub_index * own, own, 1)
    decay_own = lax.dynamic_slice_in_dim(log_decay, sub_index * own, own, 1)
    block_len = min(128, own)
    blocks = own // block_len
    upper = (
        lax.broadcasted_iota(jnp.int32, (block_len, block_len), 0)
        <= lax.broadcasted_iota(jnp.int32, (block_len, block_len), 1)
    ).astype(F32)
    cum_local = jnp.einsum(
        "hct,tu->hcu", decay_own.reshape(heads_dev, blocks, block_len), upper, precision=HIGHEST
    )
    block_totals = cum_local[..., -1]
    offsets = jnp.cumsum(block_totals, axis=-1) - block_totals
    cum_device = (cum_local + offsets[..., None]).reshape(set_groups, per_group, own)
    cum_rows = cum_local.reshape(set_groups, per_group, own)
    cum_cols = cum_rows.transpose(0, 2, 1)
    step_rows = step_own.reshape(set_groups, per_group, own)
    skip_row = jnp.repeat(d_skip, HEAD_DIM)[None, :]

    cum_all = jnp.einsum(
        "hjct,tu->hjcu",
        log_decay.reshape(heads_dev, nsub, blocks, block_len),
        upper,
        precision=HIGHEST,
    )
    all_totals = cum_all[..., -1]
    cum_all = (cum_all + (jnp.cumsum(all_totals, axis=-1) - all_totals)[..., None]).reshape(
        heads_dev, nsub, own
    )
    to_end = jnp.exp(cum_all[..., own - 1 :] - cum_all) * step_sizes.reshape(heads_dev, nsub, own)
    to_end = to_end.reshape(set_groups, per_group, tokens)

    def end_states(x_pair, start, count):
        x_spec = pl.BlockSpec((own, group_width), lambda g: (0, g + start))
        b_spec = pl.BlockSpec((1, half, own), lambda g: (g + start, 0, 0))
        w_spec = pl.BlockSpec((1, per_group, own), lambda g: (g + start, 0, 0))
        e_spec = pl.BlockSpec((1, pairs, half, 128), lambda g: (g, 0, 0, 0))
        return pl.pallas_call(
            end_pair_kernel,
            grid=(count,),
            in_specs=[x_spec, x_spec, b_spec, b_spec, w_spec, w_spec],
            out_specs=[e_spec, e_spec],
            out_shape=[jax.ShapeDtypeStruct((count, pairs, half, 128), F32)] * 2,
        )(
            *x_pair,
            *(
                lax.dynamic_slice_in_dim(bc_conv[0], at * own, own, 2)
                for at in (sub_index, 1 - sub_index)
            ),
            *(
                lax.dynamic_slice_in_dim(to_end, at * own, own, 2)
                for at in (sub_index, 1 - sub_index)
            ),
        )

    def pair_layout(values):
        return jnp.repeat(values.reshape(set_groups, pairs, 2), HEAD_DIM, axis=-1)[:, :, None, :]

    decay_first = pair_layout(half_totals[:, 0])
    decay_second = pair_layout(half_totals[:, 1])
    chip_decay = decay_first * decay_second

    def chip_ends(x_pair, start, count):
        own_end, other_end = end_states(x_pair, start, count)
        first = jnp.where(sub_index == 0, own_end, other_end)
        second = jnp.where(sub_index == 0, other_end, own_end)
        return first, decay_second[start : start + count] * first + second

    pieces = 2 if (set_groups * pairs) % 2 == 0 else 1
    rounds = ctx_size + pieces - 2
    early = set_groups // 2 if (pieces == 2 and set_groups % 2 == 0 and rounds > 0) else set_groups
    first_end, chip_end = chip_ends((x_own, x_other), 0, early)
    ctx_index = lax.axis_index("ctx")
    scan_inputs = (x_own, c_cols, b_rows, cum_rows, cum_cols, step_rows, skip_row)

    def scan_group(group, inputs, target):
        count = len(inputs)
        extra = {} if target is None else {"input_output_aliases": {count: 0}}
        tile = pl.BlockSpec((block_len, group_width), lambda g, c: (c, group))
        in_specs = [
            tile,
            pl.BlockSpec((1, block_len, state), lambda g, c: (group, c, 0)),
            pl.BlockSpec((1, state, block_len), lambda g, c: (group, 0, c)),
            pl.BlockSpec((1, per_group, block_len), lambda g, c: (group, 0, c)),
            pl.BlockSpec((1, block_len, per_group), lambda g, c: (group, c, 0)),
            pl.BlockSpec((1, per_group, block_len), lambda g, c: (group, 0, c)),
            pl.BlockSpec((1, group_width), lambda g, c: (0, group)),
        ]
        operands = tuple(inputs)
        kernel = scan_kernel
        if target is not None:
            in_specs = in_specs + [pl.BlockSpec(memory_space=pl.ANY)]
            operands = operands + (target,)
            kernel = lambda *refs: scan_kernel(*refs[:count], *refs[count + 1 :])
        return pl.pallas_call(
            kernel,
            grid=(1, blocks),
            in_specs=in_specs,
            out_specs=tile,
            out_shape=jax.ShapeDtypeStruct((own, channels), F32),
            scratch_shapes=[pltpu.VMEM((pairs, state, 128), F32)],
            **extra,
        )(*operands)

    piece_shape = (pieces, set_groups * pairs // pieces, half, 128)
    full_shape = (set_groups, pairs, half, 128)
    decay_pieces = jnp.broadcast_to(chip_decay, full_shape).reshape(piece_shape)
    if early == set_groups:
        end_pieces = chip_end.reshape(piece_shape)
    else:
        end_pieces = chip_end.reshape((1,) + piece_shape[1:])
    received = jnp.zeros(piece_shape, F32)
    y_local = None
    placed = [min(group, max(rounds, 1) - 1) for group in range(set_groups)]
    for step_index in range(max(rounds, 1)):
        send_at = jnp.clip(step_index - ctx_index, 0, pieces - 1)
        outgoing = lax.dynamic_index_in_dim(
            end_pieces, send_at, 0, keepdims=False
        ) + lax.dynamic_index_in_dim(decay_pieces, send_at, 0, keepdims=False) * (
            lax.dynamic_index_in_dim(received, send_at, 0, keepdims=False)
        )
        held = scan_inputs
        x_pair = (x_own, x_other)
        if any(p == step_index for p in placed):
            outgoing, held, x_pair = lax.optimization_barrier((outgoing, scan_inputs, x_pair))
        if rounds > 0:
            arrived = passed_along(outgoing, "ctx", 1)
        for group in range(set_groups):
            if placed[group] == step_index:
                y_local = scan_group(group, held, y_local)
        late = None
        if step_index == 0 and early < set_groups:
            late = chip_ends(x_pair, early, set_groups - early)
        if rounds == 0:
            break
        if any(p == step_index for p in placed):
            arrived, y_local, late = lax.optimization_barrier((arrived, y_local, late))
        if late is not None:
            first_end = jnp.concatenate([first_end, late[0]], 0)
            chip_end = jnp.concatenate([chip_end, late[1]], 0)
            end_pieces = chip_end.reshape(piece_shape)
        recv_at = step_index - ctx_index + 1
        valid = (recv_at >= 0) & (recv_at < pieces) & (ctx_index > 0)
        updated = lax.dynamic_update_index_in_dim(
            received, arrived, jnp.clip(recv_at, 0, pieces - 1), 0
        )
        received = jnp.where(valid, updated, received)
    carried = received.reshape(full_shape)
    into_second = decay_first * carried + first_end
    keep = jnp.where(sub_index == 0, carried, into_second)
    got = swapped(jnp.where(sub_index == 0, into_second, carried), "sub")
    low = jnp.where(sub_index == 0, keep, got)
    high = jnp.where(sub_index == 0, got, keep)
    incoming = jnp.stack([low, high], 2).reshape(set_groups, pairs, state, 128)

    out_len = min(512, own)
    return pl.pallas_call(
        out_kernel,
        grid=(set_groups, own // out_len),
        in_specs=[
            pl.BlockSpec((out_len, group_width), lambda g, c: (c, g)),
            pl.BlockSpec((1, out_len, state), lambda g, c: (g, c, 0)),
            pl.BlockSpec((1, out_len, per_group), lambda g, c: (g, c, 0)),
            pl.BlockSpec((1, pairs, state, 128), lambda g, c: (g, 0, 0, 0)),
            pl.BlockSpec((out_len, group_width), lambda g, c: (c, g)),
            pl.BlockSpec((1, group_width), lambda g, c: (0, g)),
        ],
        out_specs=pl.BlockSpec((out_len, group_width), lambda g, c: (c, g)),
        out_shape=jax.ShapeDtypeStruct((own, channels), jnp.bfloat16),
        scratch_shapes=[pltpu.VMEM((out_len, group_width), F32)],
    )(y_local, c_cols, cum_device.transpose(0, 2, 1), incoming, z_gate, norm_w[None, :])


def solution(mesh):
    in_specs = (
        P(("groups", "ctx"), "head"),
        P(None, "head", "sub", ("groups", "ctx")),
        P(("groups", "ctx", "sub"), "head"),
        P("head", ("groups", "ctx")),
        P(None, "head"),
        P("head"),
        P(None, None, "head", None),
        P(None, "head", None),
        P("head"),
        P("head"),
        P("head"),
        P("head"),
    )
    out_specs = P(("groups", "ctx", "sub"), "head")
    return jax.shard_map(
        per_device, mesh=mesh, in_specs=in_specs, out_specs=out_specs, check_vma=False
    )
```

```python
import jax
import jax.numpy as jnp
from jax import lax
from jax.experimental import pallas as pl
from jax.experimental.pallas import tpu as pltpu
from jax.sharding import PartitionSpec as P

HEADS = 128
HEAD_DIM = 64
GROUPS = 8
CONV_K = 4
SUB_LEN = 128


HIGHEST = lax.Precision.HIGHEST
F32 = jnp.float32


def passed_along(x, axis, by):
    length = lax.axis_size(axis)
    pairs = [(i, i + by) for i in range(length) if 0 <= i + by < length]
    return lax.ppermute(x, axis, pairs)


def swapped(x, axis):
    return lax.ppermute(x, axis, [(0, 1), (1, 0)])


def conv_rows(padded, weights, bias_row):
    sequence_length = padded.shape[0] - (CONV_K - 1)
    total = jnp.zeros((sequence_length, padded.shape[1]), jnp.float32) + bias_row[None, :]
    for tap_index in range(CONV_K):
        total = total + weights[tap_index][None, :] * padded[
            tap_index : tap_index + sequence_length
        ].astype(jnp.float32)
    return jax.nn.silu(total)


def conv_cols(padded, weights, bias_block):
    sequence_length = padded.shape[-1] - (CONV_K - 1)
    total = jnp.zeros(padded.shape[:-1] + (sequence_length,), jnp.float32) + bias_block[..., None]
    for tap_index in range(CONV_K):
        total = total + weights[tap_index][..., None] * padded[
            ..., tap_index : tap_index + sequence_length
        ].astype(jnp.float32)
    return jax.nn.silu(total)


def dot(a, b):
    return jnp.dot(a, b, precision=HIGHEST, preferred_element_type=F32)


def split(a):
    high = a.astype(jnp.bfloat16)
    return high, (a - high.astype(F32)).astype(jnp.bfloat16)


def dot3(a_parts, b_parts):
    a_high, a_low = a_parts
    b_high, b_low = b_parts
    flat = lambda u, v: jnp.dot(u, v, preferred_element_type=F32)
    return flat(a_high, b_high) + (flat(a_high, b_low) + flat(a_low, b_high))


def pair_columns(cumc, pair, rows):
    left = lax.broadcasted_iota(jnp.int32, (1, 128), 1) < HEAD_DIM
    return jnp.where(
        left,
        jnp.broadcast_to(cumc[:, 2 * pair : 2 * pair + 1], (rows, 128)),
        jnp.broadcast_to(cumc[:, 2 * pair + 1 : 2 * pair + 2], (rows, 128)),
    )


def scan_kernel(xc_ref, ct_ref, b_ref, cumr_ref, cumc_ref, stp_ref, dsk_ref, y_ref, e_ref):
    chunk = pl.program_id(1)
    pairs = e_ref.shape[0]
    block_len = SUB_LEN

    @pl.when(chunk == 0)
    def _():
        e_ref[...] = jnp.zeros_like(e_ref)

    rows = lax.broadcasted_iota(jnp.int32, (block_len, block_len), 0)
    cols = lax.broadcasted_iota(jnp.int32, (block_len, block_len), 1)
    causal = rows >= cols
    left = lax.broadcasted_iota(jnp.int32, (1, 128), 1) < HEAD_DIM
    for start in range(0, xc_ref.shape[0], block_len):
        span = slice(start, start + block_len)
        ct = split(ct_ref[0, span, :])
        bm = b_ref[0, :, span]
        scores = dot3(ct, split(bm))
        cumr = cumr_ref[0, :, span]
        cumc = cumc_ref[0, span, :]
        stp = stp_ref[0, :, span]
        for pair in range(pairs):
            lanes = slice(pair * 128, (pair + 1) * 128)
            xp = xc_ref[span, lanes]
            xs = split(xp)
            s_old = e_ref[pair]
            ys = []
            us = []
            for side in range(2):
                head = 2 * pair + side
                dq = jnp.broadcast_to(cumc[:, head : head + 1], (block_len, block_len))
                ck = cumr[head : head + 1, :]
                sk = stp[head : head + 1, :]
                dec = jnp.exp(jnp.where(causal, dq - ck, -jnp.inf))
                ys.append(dot3(split(scores * dec * sk), xs))
                wk = jnp.exp(dq[block_len - 1 : block_len, :] - ck) * sk
                us.append(dot3(split(bm * wk), xs))
            cq = pair_columns(cumc, pair, block_len)
            inflow = dot3(ct, split(s_old)) * jnp.exp(cq)
            y = jnp.where(left, ys[0], ys[1]) + inflow
            y_ref[span, lanes] = y + xp * dsk_ref[:, lanes]
            e_ref[pair] = jnp.exp(cq[block_len - 1 : block_len, :]) * s_old + jnp.where(
                left, us[0], us[1]
            )


def end_kernel(xc_ref, b_ref, wk_ref, e_ref):
    pairs = e_ref.shape[1]
    bm = b_ref[0]
    wk = wk_ref[0]
    left = lax.broadcasted_iota(jnp.int32, (1, 128), 1) < HEAD_DIM
    for pair in range(pairs):
        xs = split(xc_ref[:, pair * 128 : (pair + 1) * 128])
        us = [
            dot3(split(bm * wk[2 * pair + side : 2 * pair + side + 1, :]), xs) for side in range(2)
        ]
        e_ref[0, pair] = jnp.where(left, us[0], us[1])


def end_pair_kernel(xa_ref, xb_ref, ba_ref, bb_ref, wa_ref, wb_ref, ea_ref, eb_ref):
    end_kernel(xa_ref, ba_ref, wa_ref, ea_ref)
    end_kernel(xb_ref, bb_ref, wb_ref, eb_ref)


def out_kernel(y_ref, ct_ref, cumc_ref, v_ref, z_ref, nw_ref, o_ref, g_ref):
    pairs = v_ref.shape[1]
    heads = 2 * pairs
    ct = split(ct_ref[0])
    cumc = cumc_ref[0]
    total = jnp.zeros((y_ref.shape[0], 128), F32)
    for pair in range(pairs):
        lanes = slice(pair * 128, (pair + 1) * 128)
        cq = pair_columns(cumc, pair, y_ref.shape[0])
        y = y_ref[:, lanes] + dot3(ct, split(v_ref[0, pair])) * jnp.exp(cq)
        z = z_ref[:, lanes].astype(F32)
        gated = y * (z / (1.0 + jnp.exp(-z)))
        g_ref[:, lanes] = gated
        total = total + gated * gated
    mean_square = jnp.sum(total, axis=-1, keepdims=True) / g_ref.shape[1]
    o_ref[...] = (g_ref[...] * lax.rsqrt(mean_square + 1e-05) * nw_ref[...]).astype(o_ref.dtype)


def per_device(
    x_raw,
    bc_raw,
    z_gate,
    dt_raw,
    conv_x_w,
    conv_x_b,
    conv_bc_w,
    conv_bc_b,
    dt_bias,
    a_log,
    d_skip,
    norm_w,
):
    tokens = x_raw.shape[0]
    heads_dev = dt_raw.shape[0]
    per_group = HEADS // GROUPS
    set_groups = heads_dev // per_group
    pairs = per_group // 2
    group_width = per_group * HEAD_DIM
    nsub = lax.axis_size("sub")
    ctx_size = lax.axis_size("ctx")
    sub_index = lax.axis_index("sub")
    own = tokens // nsub
    half = bc_raw.shape[2]
    state = half * nsub
    channels = heads_dev * HEAD_DIM
    rim_len = CONV_K - 1

    bc_tail = bc_raw[..., tokens - rim_len :]
    rims = passed_along(
        jnp.concatenate(
            [x_raw[tokens - rim_len :], bc_tail.reshape(-1, rim_len).transpose(1, 0)], 1
        ),
        "ctx",
        1,
    )
    x_rim = rims[:, :channels]
    bc_rim = rims[:, channels:].transpose(1, 0).reshape(bc_tail.shape)
    x_pad = jnp.concatenate([x_rim, x_raw], 0)
    x_own = conv_rows(
        lax.dynamic_slice_in_dim(x_pad, sub_index * own, own + rim_len, 0), conv_x_w, conv_x_b
    )
    x_other = conv_rows(
        lax.dynamic_slice_in_dim(x_pad, (1 - sub_index) * own, own + rim_len, 0),
        conv_x_w,
        conv_x_b,
    )
    bc_weights = lax.dynamic_slice_in_dim(conv_bc_w, sub_index * half, half, 3)
    bc_bias = lax.dynamic_slice_in_dim(conv_bc_b, sub_index * half, half, 2)
    bc_conv = conv_cols(jnp.concatenate([bc_rim, bc_raw], 3), bc_weights, bc_bias)
    bc_mine = lax.dynamic_slice_in_dim(bc_conv, sub_index * own, own, 3)
    bc_theirs = swapped(lax.dynamic_slice_in_dim(bc_conv, (1 - sub_index) * own, own, 3), "sub")
    bc_own = jnp.stack(
        [
            jnp.where(sub_index == 0, bc_mine, bc_theirs),
            jnp.where(sub_index == 0, bc_theirs, bc_mine),
        ],
        2,
    ).reshape(2, set_groups, state, own)
    b_rows = bc_own[0]
    c_cols = bc_own[1].transpose(0, 2, 1)

    step_sizes = jax.nn.softplus(dt_raw + dt_bias[:, None])
    log_decay = -jnp.exp(a_log)[:, None] * step_sizes
    half_totals = jnp.exp(log_decay.reshape(heads_dev, nsub, own).sum(-1))
    step_own = lax.dynamic_slice_in_dim(step_sizes, sub_index * own, own, 1)
    decay_own = lax.dynamic_slice_in_dim(log_decay, sub_index * own, own, 1)
    block_len = min(128, own)
    blocks = own // block_len
    upper = (
        lax.broadcasted_iota(jnp.int32, (block_len, block_len), 0)
        <= lax.broadcasted_iota(jnp.int32, (block_len, block_len), 1)
    ).astype(F32)
    cum_local = jnp.einsum(
        "hct,tu->hcu", decay_own.reshape(heads_dev, blocks, block_len), upper, precision=HIGHEST
    )
    block_totals = cum_local[..., -1]
    offsets = jnp.cumsum(block_totals, axis=-1) - block_totals
    cum_device = (cum_local + offsets[..., None]).reshape(set_groups, per_group, own)
    cum_rows = cum_local.reshape(set_groups, per_group, own)
    cum_cols = cum_rows.transpose(0, 2, 1)
    step_rows = step_own.reshape(set_groups, per_group, own)
    skip_row = jnp.repeat(d_skip, HEAD_DIM)[None, :]

    cum_all = jnp.einsum(
        "hjct,tu->hjcu",
        log_decay.reshape(heads_dev, nsub, blocks, block_len),
        upper,
        precision=HIGHEST,
    )
    all_totals = cum_all[..., -1]
    cum_all = (cum_all + (jnp.cumsum(all_totals, axis=-1) - all_totals)[..., None]).reshape(
        heads_dev, nsub, own
    )
    to_end = jnp.exp(cum_all[..., own - 1 :] - cum_all) * step_sizes.reshape(heads_dev, nsub, own)
    to_end = to_end.reshape(set_groups, per_group, tokens)

    def end_states(x_pair, start, count):
        x_spec = pl.BlockSpec((own, group_width), lambda g: (0, g + start))
        b_spec = pl.BlockSpec((1, half, own), lambda g: (g + start, 0, 0))
        w_spec = pl.BlockSpec((1, per_group, own), lambda g: (g + start, 0, 0))
        e_spec = pl.BlockSpec((1, pairs, half, 128), lambda g: (g, 0, 0, 0))
        return pl.pallas_call(
            end_pair_kernel,
            grid=(count,),
            in_specs=[x_spec, x_spec, b_spec, b_spec, w_spec, w_spec],
            out_specs=[e_spec, e_spec],
            out_shape=[jax.ShapeDtypeStruct((count, pairs, half, 128), F32)] * 2,
        )(
            *x_pair,
            *(
                lax.dynamic_slice_in_dim(bc_conv[0], at * own, own, 2)
                for at in (sub_index, 1 - sub_index)
            ),
            *(
                lax.dynamic_slice_in_dim(to_end, at * own, own, 2)
                for at in (sub_index, 1 - sub_index)
            ),
        )

    def pair_layout(values):
        return jnp.repeat(values.reshape(set_groups, pairs, 2), HEAD_DIM, axis=-1)[:, :, None, :]

    decay_first = pair_layout(half_totals[:, 0])
    decay_second = pair_layout(half_totals[:, 1])
    chip_decay = decay_first * decay_second

    def chip_ends(x_pair, start, count):
        own_end, other_end = end_states(x_pair, start, count)
        first = jnp.where(sub_index == 0, own_end, other_end)
        second = jnp.where(sub_index == 0, other_end, own_end)
        return first, decay_second[start : start + count] * first + second

    pieces = 2 if (set_groups * pairs) % 2 == 0 else 1
    rounds = ctx_size + pieces - 2
    early = set_groups // 2 if (pieces == 2 and set_groups % 2 == 0 and rounds > 0) else set_groups
    first_end, chip_end = chip_ends((x_own, x_other), 0, early)
    ctx_index = lax.axis_index("ctx")
    scan_inputs = (x_own, c_cols, b_rows, cum_rows, cum_cols, step_rows, skip_row)

    step_len = min(2 * block_len, own)

    def scan_group(group, inputs, target):
        count = len(inputs)
        extra = {} if target is None else {"input_output_aliases": {count: 0}}
        tile = pl.BlockSpec((step_len, group_width), lambda g, c: (c, group))
        in_specs = [
            tile,
            pl.BlockSpec((1, step_len, state), lambda g, c: (group, c, 0)),
            pl.BlockSpec((1, state, step_len), lambda g, c: (group, 0, c)),
            pl.BlockSpec((1, per_group, step_len), lambda g, c: (group, 0, c)),
            pl.BlockSpec((1, step_len, per_group), lambda g, c: (group, c, 0)),
            pl.BlockSpec((1, per_group, step_len), lambda g, c: (group, 0, c)),
            pl.BlockSpec((1, group_width), lambda g, c: (0, group)),
        ]
        operands = tuple(inputs)
        kernel = scan_kernel
        if target is not None:
            in_specs = in_specs + [pl.BlockSpec(memory_space=pl.ANY)]
            operands = operands + (target,)
            kernel = lambda *refs: scan_kernel(*refs[:count], *refs[count + 1 :])
        return pl.pallas_call(
            kernel,
            grid=(1, own // step_len),
            in_specs=in_specs,
            out_specs=tile,
            out_shape=jax.ShapeDtypeStruct((own, channels), F32),
            scratch_shapes=[pltpu.VMEM((pairs, state, 128), F32)],
            **extra,
        )(*operands)

    piece_shape = (pieces, set_groups * pairs // pieces, half, 128)
    full_shape = (set_groups, pairs, half, 128)
    decay_pieces = jnp.broadcast_to(chip_decay, full_shape).reshape(piece_shape)
    if early == set_groups:
        end_pieces = chip_end.reshape(piece_shape)
    else:
        end_pieces = chip_end.reshape((1,) + piece_shape[1:])
    received = jnp.zeros(piece_shape, F32)
    y_local = None
    placed = [min(group, max(rounds, 1) - 1) for group in range(set_groups)]
    for step_index in range(max(rounds, 1)):
        send_at = jnp.clip(step_index - ctx_index, 0, pieces - 1)
        outgoing = lax.dynamic_index_in_dim(
            end_pieces, send_at, 0, keepdims=False
        ) + lax.dynamic_index_in_dim(decay_pieces, send_at, 0, keepdims=False) * (
            lax.dynamic_index_in_dim(received, send_at, 0, keepdims=False)
        )
        held = scan_inputs
        x_pair = (x_own, x_other)
        if any(p == step_index for p in placed):
            outgoing, held, x_pair = lax.optimization_barrier((outgoing, scan_inputs, x_pair))
        if rounds > 0:
            arrived = passed_along(outgoing, "ctx", 1)
        for group in range(set_groups):
            if placed[group] == step_index:
                y_local = scan_group(group, held, y_local)
        late = None
        if step_index == 0 and early < set_groups:
            late = chip_ends(x_pair, early, set_groups - early)
        if rounds == 0:
            break
        if any(p == step_index for p in placed):
            arrived, y_local, late = lax.optimization_barrier((arrived, y_local, late))
        if late is not None:
            first_end = jnp.concatenate([first_end, late[0]], 0)
            chip_end = jnp.concatenate([chip_end, late[1]], 0)
            end_pieces = chip_end.reshape(piece_shape)
        recv_at = step_index - ctx_index + 1
        valid = (recv_at >= 0) & (recv_at < pieces) & (ctx_index > 0)
        updated = lax.dynamic_update_index_in_dim(
            received, arrived, jnp.clip(recv_at, 0, pieces - 1), 0
        )
        received = jnp.where(valid, updated, received)
    carried = received.reshape(full_shape)
    into_second = decay_first * carried + first_end
    keep = jnp.where(sub_index == 0, carried, into_second)
    got = swapped(jnp.where(sub_index == 0, into_second, carried), "sub")
    low = jnp.where(sub_index == 0, keep, got)
    high = jnp.where(sub_index == 0, got, keep)
    incoming = jnp.stack([low, high], 2).reshape(set_groups, pairs, state, 128)

    out_len = min(512, own)
    return pl.pallas_call(
        out_kernel,
        grid=(set_groups, own // out_len),
        in_specs=[
            pl.BlockSpec((out_len, group_width), lambda g, c: (c, g)),
            pl.BlockSpec((1, out_len, state), lambda g, c: (g, c, 0)),
            pl.BlockSpec((1, out_len, per_group), lambda g, c: (g, c, 0)),
            pl.BlockSpec((1, pairs, state, 128), lambda g, c: (g, 0, 0, 0)),
            pl.BlockSpec((out_len, group_width), lambda g, c: (c, g)),
            pl.BlockSpec((1, group_width), lambda g, c: (0, g)),
        ],
        out_specs=pl.BlockSpec((out_len, group_width), lambda g, c: (c, g)),
        out_shape=jax.ShapeDtypeStruct((own, channels), jnp.bfloat16),
        scratch_shapes=[pltpu.VMEM((out_len, group_width), F32)],
    )(y_local, c_cols, cum_device.transpose(0, 2, 1), incoming, z_gate, norm_w[None, :])


def solution(mesh):
    in_specs = (
        P(("groups", "ctx"), "head"),
        P(None, "head", "sub", ("groups", "ctx")),
        P(("groups", "ctx", "sub"), "head"),
        P("head", ("groups", "ctx")),
        P(None, "head"),
        P("head"),
        P(None, None, "head", None),
        P(None, "head", None),
        P("head"),
        P("head"),
        P("head"),
        P("head"),
    )
    out_specs = P(("groups", "ctx", "sub"), "head")
    return jax.shard_map(
        per_device, mesh=mesh, in_specs=in_specs, out_specs=out_specs, check_vma=False
    )
```

```python
import jax
import jax.numpy as jnp
from jax import lax
from jax.experimental import pallas as pl
from jax.experimental.pallas import tpu as pltpu
from jax.sharding import PartitionSpec as P

HEADS = 128
HEAD_DIM = 64
GROUPS = 8
CONV_K = 4


HIGHEST = lax.Precision.HIGHEST
F32 = jnp.float32


def passed_along(x, axis, by):
    length = lax.axis_size(axis)
    pairs = [(i, i + by) for i in range(length) if 0 <= i + by < length]
    return lax.ppermute(x, axis, pairs)


def swapped(x, axis):
    return lax.ppermute(x, axis, [(0, 1), (1, 0)])


def conv_rows(padded, weights, bias_row):
    sequence_length = padded.shape[0] - (CONV_K - 1)
    total = jnp.zeros((sequence_length, padded.shape[1]), jnp.float32) + bias_row[None, :]
    for tap_index in range(CONV_K):
        total = total + weights[tap_index][None, :] * padded[
            tap_index : tap_index + sequence_length
        ].astype(jnp.float32)
    return jax.nn.silu(total)


def conv_cols(padded, weights, bias_block):
    sequence_length = padded.shape[-1] - (CONV_K - 1)
    total = jnp.zeros(padded.shape[:-1] + (sequence_length,), jnp.float32) + bias_block[..., None]
    for tap_index in range(CONV_K):
        total = total + weights[tap_index][..., None] * padded[
            ..., tap_index : tap_index + sequence_length
        ].astype(jnp.float32)
    return jax.nn.silu(total)


def dot(a, b):
    return jnp.dot(a, b, precision=HIGHEST, preferred_element_type=F32)


def split(a):
    high = a.astype(jnp.bfloat16)
    return high, (a - high.astype(F32)).astype(jnp.bfloat16)


def dot3(a_parts, b_parts):
    a_high, a_low = a_parts
    b_high, b_low = b_parts
    flat = lambda u, v: jnp.dot(u, v, preferred_element_type=F32)
    return flat(a_high, b_high) + (flat(a_high, b_low) + flat(a_low, b_high))


def pair_columns(cumc, pair, rows):
    left = lax.broadcasted_iota(jnp.int32, (1, 128), 1) < HEAD_DIM
    return jnp.where(
        left,
        jnp.broadcast_to(cumc[:, 2 * pair : 2 * pair + 1], (rows, 128)),
        jnp.broadcast_to(cumc[:, 2 * pair + 1 : 2 * pair + 2], (rows, 128)),
    )


def scan_kernel(xc_ref, ct_ref, b_ref, cumr_ref, cumc_ref, stp_ref, dsk_ref, y_ref, e_ref):
    chunk = pl.program_id(1)
    block_len = xc_ref.shape[0]
    pairs = e_ref.shape[0]
    heads = 2 * pairs

    @pl.when(chunk == 0)
    def _():
        e_ref[...] = jnp.zeros_like(e_ref)

    ct = split(ct_ref[0])
    bm = b_ref[0]
    scores = dot3(ct, split(bm))
    rows = lax.broadcasted_iota(jnp.int32, (block_len, block_len), 0)
    cols = lax.broadcasted_iota(jnp.int32, (block_len, block_len), 1)
    causal = rows >= cols
    cumr = cumr_ref[0]
    cumc = cumc_ref[0]
    stp = stp_ref[0]
    left = lax.broadcasted_iota(jnp.int32, (1, 128), 1) < HEAD_DIM
    for pair in range(pairs):
        lanes = slice(pair * 128, (pair + 1) * 128)
        xp = xc_ref[:, lanes]
        xs = split(xp)
        s_old = e_ref[pair]
        ys = []
        us = []
        for side in range(2):
            head = 2 * pair + side
            dq = jnp.broadcast_to(cumc[:, head : head + 1], (block_len, block_len))
            ck = cumr[head : head + 1, :]
            sk = stp[head : head + 1, :]
            dec = jnp.exp(jnp.where(causal, dq - ck, -jnp.inf))
            ys.append(dot3(split(scores * dec * sk), xs))
            wk = jnp.exp(dq[block_len - 1 : block_len, :] - ck) * sk
            us.append(dot3(split(bm * wk), xs))
        cq = pair_columns(cumc, pair, block_len)
        inflow = dot3(ct, split(s_old)) * jnp.exp(cq)
        y = jnp.where(left, ys[0], ys[1]) + inflow
        y_ref[:, lanes] = y + xp * dsk_ref[:, lanes]
        e_ref[pair] = jnp.exp(cq[block_len - 1 : block_len, :]) * s_old + jnp.where(
            left, us[0], us[1]
        )


def end_kernel(xc_ref, b_ref, wk_ref, e_ref):
    pairs = e_ref.shape[1]
    bm = b_ref[0]
    wk = wk_ref[0]
    left = lax.broadcasted_iota(jnp.int32, (1, 128), 1) < HEAD_DIM
    for pair in range(pairs):
        xs = split(xc_ref[:, pair * 128 : (pair + 1) * 128])
        us = [
            dot3(split(bm * wk[2 * pair + side : 2 * pair + side + 1, :]), xs) for side in range(2)
        ]
        e_ref[0, pair] = jnp.where(left, us[0], us[1])


def end_pair_kernel(xa_ref, xb_ref, ba_ref, bb_ref, wa_ref, wb_ref, ea_ref, eb_ref):
    end_kernel(xa_ref, ba_ref, wa_ref, ea_ref)
    end_kernel(xb_ref, bb_ref, wb_ref, eb_ref)


def out_kernel(y_ref, ct_ref, cumc_ref, v_ref, z_ref, nw_ref, o_ref, g_ref):
    pairs = v_ref.shape[1]
    heads = 2 * pairs
    ct = split(ct_ref[0])
    cumc = cumc_ref[0]
    total = jnp.zeros((y_ref.shape[0], 128), F32)
    for pair in range(pairs):
        lanes = slice(pair * 128, (pair + 1) * 128)
        cq = pair_columns(cumc, pair, y_ref.shape[0])
        y = y_ref[:, lanes] + dot3(ct, split(v_ref[0, pair])) * jnp.exp(cq)
        z = z_ref[:, lanes].astype(F32)
        gated = y * (z / (1.0 + jnp.exp(-z)))
        g_ref[:, lanes] = gated
        total = total + gated * gated
    mean_square = jnp.sum(total, axis=-1, keepdims=True) / g_ref.shape[1]
    o_ref[...] = (g_ref[...] * lax.rsqrt(mean_square + 1e-05) * nw_ref[...]).astype(o_ref.dtype)


def per_device(
    x_raw,
    bc_raw,
    z_gate,
    dt_raw,
    conv_x_w,
    conv_x_b,
    conv_bc_w,
    conv_bc_b,
    dt_bias,
    a_log,
    d_skip,
    norm_w,
):
    tokens = x_raw.shape[0]
    heads_dev = dt_raw.shape[0]
    per_group = HEADS // GROUPS
    set_groups = heads_dev // per_group
    pairs = per_group // 2
    group_width = per_group * HEAD_DIM
    nsub = lax.axis_size("sub")
    ctx_size = lax.axis_size("ctx")
    sub_index = lax.axis_index("sub")
    own = tokens // nsub
    half = bc_raw.shape[2]
    state = half * nsub
    channels = heads_dev * HEAD_DIM
    rim_len = CONV_K - 1

    bc_tail = bc_raw[..., tokens - rim_len :]
    rims = passed_along(
        jnp.concatenate(
            [x_raw[tokens - rim_len :], bc_tail.reshape(-1, rim_len).transpose(1, 0)], 1
        ),
        "ctx",
        1,
    )
    x_rim = rims[:, :channels]
    bc_rim = rims[:, channels:].transpose(1, 0).reshape(bc_tail.shape)
    x_pad = jnp.concatenate([x_rim, x_raw], 0)
    x_own = conv_rows(
        lax.dynamic_slice_in_dim(x_pad, sub_index * own, own + rim_len, 0), conv_x_w, conv_x_b
    )
    x_other = conv_rows(
        lax.dynamic_slice_in_dim(x_pad, (1 - sub_index) * own, own + rim_len, 0),
        conv_x_w,
        conv_x_b,
    )
    bc_weights = lax.dynamic_slice_in_dim(conv_bc_w, sub_index * half, half, 3)
    bc_bias = lax.dynamic_slice_in_dim(conv_bc_b, sub_index * half, half, 2)
    bc_conv = conv_cols(jnp.concatenate([bc_rim, bc_raw], 3), bc_weights, bc_bias)
    bc_mine = lax.dynamic_slice_in_dim(bc_conv, sub_index * own, own, 3)
    bc_theirs = swapped(lax.dynamic_slice_in_dim(bc_conv, (1 - sub_index) * own, own, 3), "sub")
    bc_own = jnp.stack(
        [
            jnp.where(sub_index == 0, bc_mine, bc_theirs),
            jnp.where(sub_index == 0, bc_theirs, bc_mine),
        ],
        2,
    ).reshape(2, set_groups, state, own)
    b_rows = bc_own[0]
    c_cols = bc_own[1].transpose(0, 2, 1)

    step_sizes = jax.nn.softplus(dt_raw + dt_bias[:, None])
    log_decay = -jnp.exp(a_log)[:, None] * step_sizes
    half_totals = jnp.exp(log_decay.reshape(heads_dev, nsub, own).sum(-1))
    step_own = lax.dynamic_slice_in_dim(step_sizes, sub_index * own, own, 1)
    decay_own = lax.dynamic_slice_in_dim(log_decay, sub_index * own, own, 1)
    block_len = min(128, own)
    blocks = own // block_len
    upper = (
        lax.broadcasted_iota(jnp.int32, (block_len, block_len), 0)
        <= lax.broadcasted_iota(jnp.int32, (block_len, block_len), 1)
    ).astype(F32)
    cum_local = jnp.einsum(
        "hct,tu->hcu", decay_own.reshape(heads_dev, blocks, block_len), upper, precision=HIGHEST
    )
    block_totals = cum_local[..., -1]
    offsets = jnp.cumsum(block_totals, axis=-1) - block_totals
    cum_device = (cum_local + offsets[..., None]).reshape(set_groups, per_group, own)
    cum_rows = cum_local.reshape(set_groups, per_group, own)
    cum_cols = cum_rows.transpose(0, 2, 1)
    step_rows = step_own.reshape(set_groups, per_group, own)
    skip_row = jnp.repeat(d_skip, HEAD_DIM)[None, :]

    cum_all = jnp.einsum(
        "hjct,tu->hjcu",
        log_decay.reshape(heads_dev, nsub, blocks, block_len),
        upper,
        precision=HIGHEST,
    )
    all_totals = cum_all[..., -1]
    cum_all = (cum_all + (jnp.cumsum(all_totals, axis=-1) - all_totals)[..., None]).reshape(
        heads_dev, nsub, own
    )
    to_end = jnp.exp(cum_all[..., own - 1 :] - cum_all) * step_sizes.reshape(heads_dev, nsub, own)
    to_end = to_end.reshape(set_groups, per_group, tokens)

    def end_states(x_pair, start, count):
        x_spec = pl.BlockSpec((own, group_width), lambda g: (0, g + start))
        b_spec = pl.BlockSpec((1, half, own), lambda g: (g + start, 0, 0))
        w_spec = pl.BlockSpec((1, per_group, own), lambda g: (g + start, 0, 0))
        e_spec = pl.BlockSpec((1, pairs, half, 128), lambda g: (g, 0, 0, 0))
        return pl.pallas_call(
            end_pair_kernel,
            grid=(count,),
            in_specs=[x_spec, x_spec, b_spec, b_spec, w_spec, w_spec],
            out_specs=[e_spec, e_spec],
            out_shape=[jax.ShapeDtypeStruct((count, pairs, half, 128), F32)] * 2,
        )(
            *x_pair,
            *(
                lax.dynamic_slice_in_dim(bc_conv[0], at * own, own, 2)
                for at in (sub_index, 1 - sub_index)
            ),
            *(
                lax.dynamic_slice_in_dim(to_end, at * own, own, 2)
                for at in (sub_index, 1 - sub_index)
            ),
        )

    def pair_layout(values):
        return jnp.repeat(values.reshape(set_groups, pairs, 2), HEAD_DIM, axis=-1)[:, :, None, :]

    decay_first = pair_layout(half_totals[:, 0])
    decay_second = pair_layout(half_totals[:, 1])
    chip_decay = decay_first * decay_second

    def chip_ends(x_pair, start, count):
        own_end, other_end = end_states(x_pair, start, count)
        first = jnp.where(sub_index == 0, own_end, other_end)
        second = jnp.where(sub_index == 0, other_end, own_end)
        return first, decay_second[start : start + count] * first + second

    pieces = 2 if (set_groups * pairs) % 2 == 0 else 1
    rounds = ctx_size + pieces - 2
    early = set_groups // 2 if (pieces == 2 and set_groups % 2 == 0 and rounds > 0) else set_groups
    first_end, chip_end = chip_ends((x_own, x_other), 0, early)
    ctx_index = lax.axis_index("ctx")
    scan_inputs = (x_own, c_cols, b_rows, cum_rows, cum_cols, step_rows, skip_row)

    def scan_group(group, inputs, target):
        count = len(inputs)
        extra = {} if target is None else {"input_output_aliases": {count: 0}}
        tile = pl.BlockSpec((block_len, group_width), lambda g, c: (c, group))
        in_specs = [
            tile,
            pl.BlockSpec((1, block_len, state), lambda g, c: (group, c, 0)),
            pl.BlockSpec((1, state, block_len), lambda g, c: (group, 0, c)),
            pl.BlockSpec((1, per_group, block_len), lambda g, c: (group, 0, c)),
            pl.BlockSpec((1, block_len, per_group), lambda g, c: (group, c, 0)),
            pl.BlockSpec((1, per_group, block_len), lambda g, c: (group, 0, c)),
            pl.BlockSpec((1, group_width), lambda g, c: (0, group)),
        ]
        operands = tuple(inputs)
        kernel = scan_kernel
        if target is not None:
            in_specs = in_specs + [pl.BlockSpec(memory_space=pl.ANY)]
            operands = operands + (target,)
            kernel = lambda *refs: scan_kernel(*refs[:count], *refs[count + 1 :])
        return pl.pallas_call(
            kernel,
            grid=(1, blocks),
            in_specs=in_specs,
            out_specs=tile,
            out_shape=jax.ShapeDtypeStruct((own, channels), F32),
            scratch_shapes=[pltpu.VMEM((pairs, state, 128), F32)],
            **extra,
        )(*operands)

    piece_shape = (pieces, set_groups * pairs // pieces, half, 128)
    full_shape = (set_groups, pairs, half, 128)
    decay_pieces = jnp.broadcast_to(chip_decay, full_shape).reshape(piece_shape)
    if early == set_groups:
        end_pieces = chip_end.reshape(piece_shape)
    else:
        end_pieces = chip_end.reshape((1,) + piece_shape[1:])
    received = jnp.zeros(piece_shape, F32)
    y_local = None
    placed = [min(max(group, 1), max(rounds, 1) - 1) for group in range(set_groups)]
    for step_index in range(max(rounds, 1)):
        send_at = jnp.clip(step_index - ctx_index, 0, pieces - 1)
        outgoing = lax.dynamic_index_in_dim(
            end_pieces, send_at, 0, keepdims=False
        ) + lax.dynamic_index_in_dim(decay_pieces, send_at, 0, keepdims=False) * (
            lax.dynamic_index_in_dim(received, send_at, 0, keepdims=False)
        )
        held = scan_inputs
        x_pair = (x_own, x_other)
        if any(p == step_index for p in placed) or (step_index == 0 and early < set_groups):
            outgoing, held, x_pair = lax.optimization_barrier((outgoing, scan_inputs, x_pair))
        if rounds > 0:
            arrived = passed_along(outgoing, "ctx", 1)
        for group in range(set_groups):
            if placed[group] == step_index:
                y_local = scan_group(group, held, y_local)
        late = None
        if step_index == 0 and early < set_groups:
            late = chip_ends(x_pair, early, set_groups - early)
        if rounds == 0:
            break
        if any(p == step_index for p in placed) or (step_index == 0 and early < set_groups):
            arrived, y_local, late = lax.optimization_barrier((arrived, y_local, late))
        if late is not None:
            first_end = jnp.concatenate([first_end, late[0]], 0)
            chip_end = jnp.concatenate([chip_end, late[1]], 0)
            end_pieces = chip_end.reshape(piece_shape)
        recv_at = step_index - ctx_index + 1
        valid = (recv_at >= 0) & (recv_at < pieces) & (ctx_index > 0)
        updated = lax.dynamic_update_index_in_dim(
            received, arrived, jnp.clip(recv_at, 0, pieces - 1), 0
        )
        received = jnp.where(valid, updated, received)
    carried = received.reshape(full_shape)
    into_second = decay_first * carried + first_end
    keep = jnp.where(sub_index == 0, carried, into_second)
    got = swapped(jnp.where(sub_index == 0, into_second, carried), "sub")
    low = jnp.where(sub_index == 0, keep, got)
    high = jnp.where(sub_index == 0, got, keep)
    incoming = jnp.stack([low, high], 2).reshape(set_groups, pairs, state, 128)

    out_len = min(512, own)
    return pl.pallas_call(
        out_kernel,
        grid=(set_groups, own // out_len),
        in_specs=[
            pl.BlockSpec((out_len, group_width), lambda g, c: (c, g)),
            pl.BlockSpec((1, out_len, state), lambda g, c: (g, c, 0)),
            pl.BlockSpec((1, out_len, per_group), lambda g, c: (g, c, 0)),
            pl.BlockSpec((1, pairs, state, 128), lambda g, c: (g, 0, 0, 0)),
            pl.BlockSpec((out_len, group_width), lambda g, c: (c, g)),
            pl.BlockSpec((1, group_width), lambda g, c: (0, g)),
        ],
        out_specs=pl.BlockSpec((out_len, group_width), lambda g, c: (c, g)),
        out_shape=jax.ShapeDtypeStruct((own, channels), jnp.bfloat16),
        scratch_shapes=[pltpu.VMEM((out_len, group_width), F32)],
    )(y_local, c_cols, cum_device.transpose(0, 2, 1), incoming, z_gate, norm_w[None, :])


def solution(mesh):
    in_specs = (
        P(("groups", "ctx"), "head"),
        P(None, "head", "sub", ("groups", "ctx")),
        P(("groups", "ctx", "sub"), "head"),
        P("head", ("groups", "ctx")),
        P(None, "head"),
        P("head"),
        P(None, None, "head", None),
        P(None, "head", None),
        P("head"),
        P("head"),
        P("head"),
        P("head"),
    )
    out_specs = P(("groups", "ctx", "sub"), "head")
    return jax.shard_map(
        per_device, mesh=mesh, in_specs=in_specs, out_specs=out_specs, check_vma=False
    )
```
